128 devices in a mesh: gy: 64 (over z, y, x), pa: 2 (over core).
Axes of the slice: x: 4, y: 4, z: 4, core: 2. Of those that a mesh axis runs over, the one named last changes fastest.
Arguments:
- mass_per_volume: float32 [512, 128, 128], P('gy', 'pa'), may hold values from 0.5 to 1.5
- mass_flux_vector: float32 [3, 512, 128, 128], P(None, 'gy', 'pa'), may hold values from -1.5 to 1.5
- total_heat_content: float32 [512, 128, 128], P('gy', 'pa'), may hold values from 1.6 to 4.4
Outputs:
- time_rate: float32 [5, 512, 128, 128], P(None, 'gy', 'pa')
- smoothed: float32 [5, 512, 128, 128], P(None, 'gy', 'pa')
The draws below stay inside these ranges and needn't reach their ends.
All inputs are finite; a program needn't handle non-finite values.
Results may differ from the reference program's by a relative error of at most 0.0003.
Values sent between devices are 32-bit elements; how exact they have to be, the bound alone decides.
No kernel may reach another device: no remote copies, remote signals or barrier semaphores. Data moves between devices by JAX's collectives and lax.ppermute only.
A program may use at most 256 MiB of HBM per device.

```python
import jax
import jax.numpy as jnp
import numpy as np
from jax import lax

NX = 128
NY = 512
NZ = 128


def row_signs():
    return (1.0 - 2.0 * (jnp.arange(NY) % 2).astype(jnp.float32))[:, None, None]


def draw_mass_per_volume(key, part):
    shape_all = (NY, NZ, NX)
    rough = jnp.clip(0.1 * jax.random.normal(key, shape_all, jnp.float32), -0.2, 0.2)
    return 1.0 + 0.3 * row_signs() + rough


def draw_total_heat_content(key, part):
    shape_all = (NY, NZ, NX)
    rough = jnp.clip(0.25 * jax.random.normal(key, shape_all, jnp.float32), -0.5, 0.5)
    return 3.0 + 0.9 * row_signs() + rough


def draw_mass_flux_vector(key, part):
    shape_all = (3, NY, NZ, NX)
    return jnp.clip(0.4 * jax.random.normal(key, shape_all, jnp.float32), -1.5, 1.5)


def setup_inputs(seed: int = 0) -> dict:
    seeds = jax.random.split(jax.random.key(seed), 4)
    mass_per_volume = draw_mass_per_volume(jax.random.fold_in(seeds[3], 71), 0)
    mass_flux_vector = draw_mass_flux_vector(jax.random.fold_in(seeds[3], 71), 0)
    total_heat_content = draw_total_heat_content(jax.random.fold_in(seeds[3], 71), 0)
    return dict(mass_per_volume=mass_per_volume, mass_flux_vector=mass_flux_vector, total_heat_content=total_heat_content)


GAMMA_GAS = 1.4
PRANDTL = 0.72
VISCOSITY = 0.25
ALPHA_FILTER = 0.499
ALPHA_SLOPE = 0.498
STRETCH = 1.2
STREAM_STEP = 1.0
SPAN_STEP = 0.5

def slope_weights():
    near_weight = (2.0 + ALPHA_SLOPE) / 3.0
    far_weight = (4.0 * ALPHA_SLOPE - 1.0) / 12.0
    return (near_weight, far_weight)

def system_rows(system_kind, points):
    lower = np.zeros(points)
    middle = np.ones(points)
    upper = np.zeros(points)
    weights = np.zeros((7, points))
    if system_kind == 'slope':
        near_weight, far_weight = slope_weights()
        lower[:] = ALPHA_SLOPE
        upper[:] = ALPHA_SLOPE
        weights[1] = -far_weight
        weights[2] = -near_weight
        weights[4] = near_weight
        weights[5] = far_weight
        for edge_row in (1, points - 2):
            lower[edge_row] = 0.25
            upper[edge_row] = 0.25
            weights[:, edge_row] = 0.0
            weights[2, edge_row] = -0.75
            weights[4, edge_row] = 0.75
        lower[0] = 0.0
        upper[0] = 2.0
        weights[:, 0] = 0.0
        weights[3, 0] = -2.5
        weights[4, 0] = 2.0
        weights[5, 0] = 0.5
        lower[points - 1] = 2.0
        upper[points - 1] = 0.0
        weights[:, points - 1] = 0.0
        weights[3, points - 1] = 2.5
        weights[2, points - 1] = -2.0
        weights[1, points - 1] = -0.5
    else:
        strength = ALPHA_FILTER
        lower[:] = strength
        upper[:] = strength
        weights[3] = 11.0 / 16.0 + 5.0 * strength / 8.0
        weights[2] = 15.0 / 64.0 + 17.0 * strength / 32.0
        weights[4] = weights[2]
        weights[1] = -3.0 / 32.0 + 3.0 * strength / 16.0
        weights[5] = weights[1]
        weights[0] = 1.0 / 64.0 - strength / 32.0
        weights[6] = weights[0]
        for edge_row in (2, points - 3):
            weights[:, edge_row] = 0.0
            weights[3, edge_row] = 5.0 / 8.0 + 3.0 * strength / 4.0
            weights[2, edge_row] = 0.25 + strength / 2.0
            weights[4, edge_row] = 0.25 + strength / 2.0
            weights[1, edge_row] = -1.0 / 16.0 + strength / 8.0
            weights[5, edge_row] = -1.0 / 16.0 + strength / 8.0
        for edge_row in (1, points - 2):
            weights[:, edge_row] = 0.0
            weights[3, edge_row] = 0.5 + strength
            weights[2, edge_row] = 0.25 + strength / 2.0
            weights[4, edge_row] = 0.25 + strength / 2.0
        for edge_row in (0, points - 1):
            lower[edge_row] = 0.0
            upper[edge_row] = 0.0
            weights[:, edge_row] = 0.0
            weights[3, edge_row] = 1.0
    return (lower, middle, upper, weights)

def inverse_metric(points):
    places = 2.0 * np.arange(points) / (points - 1) - 1.0
    growth = np.exp(STRETCH * places)
    cosh_values = 0.5 * (growth + 1.0 / growth)
    edge_growth = np.exp(STRETCH)
    tanh_value = (edge_growth - 1.0 / edge_growth) / (edge_growth + 1.0 / edge_growth)
    return tanh_value * cosh_values ** 2 / (0.64 * STRETCH)

def stencil_sum(padded, weights, rim_rows):
    rows_here = padded.shape[1] - 2 * rim_rows
    summed = jnp.zeros((padded.shape[0], rows_here, padded.shape[2]), jnp.float32)
    for offset in range(-rim_rows, rim_rows + 1):
        summed = summed + weights[:, 3 + offset, :, None] * padded[:, rim_rows + offset:rim_rows + offset + rows_here]
    return summed

def wall_apply(field_lines, system_kind):
    points = field_lines.shape[0]
    lower, middle, upper, weights = system_rows(system_kind, points)
    padded = jnp.pad(field_lines[None], ((0, 0), (3, 3), (0, 0)))
    right_side = stencil_sum(padded, jnp.asarray(weights[None], jnp.float32), 3)[0]
    return lax.linalg.tridiagonal_solve(jnp.asarray(lower, jnp.float32), jnp.asarray(middle, jnp.float32), jnp.asarray(upper, jnp.float32), right_side)

def periodic_slope(fields, axis_at, spacing):
    points = fields.shape[axis_at]
    near_weight, far_weight = slope_weights()
    wave_numbers = np.arange(points // 2 + 1)
    angles = 2.0 * np.pi * wave_numbers / points
    modified = (2.0 * near_weight * np.sin(angles) + 2.0 * far_weight * np.sin(2.0 * angles)) / (1.0 + 2.0 * ALPHA_SLOPE * np.cos(angles)) / spacing
    modified[points // 2] = 0.0
    modified[0] = 0.0
    broadcast_shape = [1] * fields.ndim
    broadcast_shape[axis_at] = points // 2 + 1
    factor = jnp.asarray(modified.reshape(broadcast_shape), jnp.float32)
    spectrum = jnp.fft.rfft(fields, axis=axis_at)
    return jnp.fft.irfft(spectrum * (1j * factor), n=points, axis=axis_at).astype(jnp.float32)

def recover_basic_quantities(mass_per_volume, mass_flux_vector, total_heat_content):
    fluid_speed_vector = mass_flux_vector / mass_per_volume[None]
    kinetic = 0.5 * jnp.sum(fluid_speed_vector * mass_flux_vector, axis=0)
    thermo_push = (GAMMA_GAS - 1.0) * (total_heat_content - kinetic)
    thermo_warmth = thermo_push / mass_per_volume
    return (fluid_speed_vector, thermo_push, thermo_warmth)

def flux_along(direction, mass_flux_vector, total_heat_content, fluid_speed_vector, thermo_push, gradients):
    divergence = gradients[0][0] + gradients[1][1] + gradients[2][2]
    conduct = VISCOSITY * GAMMA_GAS / ((GAMMA_GAS - 1.0) * PRANDTL)
    rows_out = [mass_flux_vector[direction]]
    energy_flux = (total_heat_content + thermo_push) * fluid_speed_vector[direction]
    for component in range(3):
        stress = VISCOSITY * (gradients[direction][component] + gradients[component][direction])
        if component == direction:
            stress = stress - 2.0 / 3.0 * VISCOSITY * divergence
            rows_out.append(mass_flux_vector[component] * fluid_speed_vector[direction] + thermo_push - stress)
        else:
            rows_out.append(mass_flux_vector[component] * fluid_speed_vector[direction] - stress)
        energy_flux = energy_flux - fluid_speed_vector[component] * stress
    energy_flux = energy_flux - conduct * gradients[direction][3]
    rows_out.append(energy_flux)
    return jnp.stack(rows_out)

def reference(mass_per_volume, mass_flux_vector, total_heat_content):
    points, span_cells, stream_cells = mass_per_volume.shape
    line_count = span_cells * stream_cells
    fluid_speed_vector, thermo_push, thermo_warmth = recover_basic_quantities(mass_per_volume, mass_flux_vector, total_heat_content)
    basic_quantities = jnp.concatenate([fluid_speed_vector, thermo_warmth[None]], axis=0)
    state_all = jnp.concatenate([mass_per_volume[None], mass_flux_vector, total_heat_content[None]], axis=0)
    metric = jnp.asarray(inverse_metric(points), jnp.float32)[:, None, None]
    smoothed = jnp.stack([wall_apply(state_all[member].reshape(points, line_count), 'smooth').reshape(points, span_cells, stream_cells) for member in range(5)])
    wall_grad = jnp.stack([wall_apply(basic_quantities[member].reshape(points, line_count), 'slope').reshape(points, span_cells, stream_cells) * metric for member in range(4)])
    gradients = [periodic_slope(basic_quantities, 3, STREAM_STEP), wall_grad, periodic_slope(basic_quantities, 2, SPAN_STEP)]
    stream_term = periodic_slope(flux_along(0, mass_flux_vector, total_heat_content, fluid_speed_vector, thermo_push, gradients), 3, STREAM_STEP)
    flux_wall = flux_along(1, mass_flux_vector, total_heat_content, fluid_speed_vector, thermo_push, gradients)
    wall_term = jnp.stack([wall_apply(flux_wall[member].reshape(points, line_count), 'slope').reshape(points, span_cells, stream_cells) * metric for member in range(5)])
    span_term = periodic_slope(flux_along(2, mass_flux_vector, total_heat_content, fluid_speed_vector, thermo_push, gradients), 2, SPAN_STEP)
    time_rate = -(stream_term + wall_term + span_term)
    row_numbers = jnp.arange(points)
    at_wall = (row_numbers == 0) | (row_numbers == points - 1)
    held_rows = jnp.where(at_wall[None, :, None, None], 0.0, time_rate[1:4])
    time_rate = jnp.concatenate([time_rate[:1], held_rows, time_rate[4:]], axis=0)
    return (time_rate, smoothed)
```

```python
import functools

import jax
import jax.numpy as jnp
import numpy as np
from jax import lax
from jax.sharding import PartitionSpec as P

GAMMA_GAS = 1.4
PRANDTL = 0.72
VISCOSITY = 0.25
ALPHA_FILTER = 0.499
ALPHA_SLOPE = 0.498
STRETCH = 1.2
STREAM_STEP = 1.0
SPAN_STEP = 0.5
HIGHEST = lax.Precision.HIGHEST


def slope_weights():
    near_weight = (2.0 + ALPHA_SLOPE) / 3.0
    far_weight = (4.0 * ALPHA_SLOPE - 1.0) / 12.0
    return (near_weight, far_weight)


def system_rows(system_kind, points):
    lower = np.zeros(points)
    middle = np.ones(points)
    upper = np.zeros(points)
    weights = np.zeros((7, points))
    if system_kind == "slope":
        near_weight, far_weight = slope_weights()
        lower[:] = ALPHA_SLOPE
        upper[:] = ALPHA_SLOPE
        weights[1] = -far_weight
        weights[2] = -near_weight
        weights[4] = near_weight
        weights[5] = far_weight
        for edge_row in (1, points - 2):
            lower[edge_row] = 0.25
            upper[edge_row] = 0.25
            weights[:, edge_row] = 0.0
            weights[2, edge_row] = -0.75
            weights[4, edge_row] = 0.75
        lower[0] = 0.0
        upper[0] = 2.0
        weights[:, 0] = 0.0
        weights[3, 0] = -2.5
        weights[4, 0] = 2.0
        weights[5, 0] = 0.5
        lower[points - 1] = 2.0
        upper[points - 1] = 0.0
        weights[:, points - 1] = 0.0
        weights[3, points - 1] = 2.5
        weights[2, points - 1] = -2.0
        weights[1, points - 1] = -0.5
    else:
        strength = ALPHA_FILTER
        lower[:] = strength
        upper[:] = strength
        weights[3] = 11.0 / 16.0 + 5.0 * strength / 8.0
        weights[2] = 15.0 / 64.0 + 17.0 * strength / 32.0
        weights[4] = weights[2]
        weights[1] = -3.0 / 32.0 + 3.0 * strength / 16.0
        weights[5] = weights[1]
        weights[0] = 1.0 / 64.0 - strength / 32.0
        weights[6] = weights[0]
        for edge_row in (2, points - 3):
            weights[:, edge_row] = 0.0
            weights[3, edge_row] = 5.0 / 8.0 + 3.0 * strength / 4.0
            weights[2, edge_row] = 0.25 + strength / 2.0
            weights[4, edge_row] = 0.25 + strength / 2.0
            weights[1, edge_row] = -1.0 / 16.0 + strength / 8.0
            weights[5, edge_row] = -1.0 / 16.0 + strength / 8.0
        for edge_row in (1, points - 2):
            weights[:, edge_row] = 0.0
            weights[3, edge_row] = 0.5 + strength
            weights[2, edge_row] = 0.25 + strength / 2.0
            weights[4, edge_row] = 0.25 + strength / 2.0
        for edge_row in (0, points - 1):
            lower[edge_row] = 0.0
            upper[edge_row] = 0.0
            weights[:, edge_row] = 0.0
            weights[3, edge_row] = 1.0
    return (lower, middle, upper, weights)


def inverse_metric(points):
    places = 2.0 * np.arange(points) / (points - 1) - 1.0
    growth = np.exp(STRETCH * places)
    cosh_values = 0.5 * (growth + 1.0 / growth)
    edge_growth = np.exp(STRETCH)
    tanh_value = (edge_growth - 1.0 / edge_growth) / (edge_growth + 1.0 / edge_growth)
    return tanh_value * cosh_values**2 / (0.64 * STRETCH)


def periodic_matrix(points, spacing):
    near_weight, far_weight = slope_weights()
    wave_numbers = np.arange(1, points // 2)
    angles = 2.0 * np.pi * wave_numbers / points
    modified = (2.0 * near_weight * np.sin(angles) + 2.0 * far_weight * np.sin(2.0 * angles)) / (
        1.0 + 2.0 * ALPHA_SLOPE * np.cos(angles)
    )
    phases = np.arange(points)[:, None] * wave_numbers[None, :] % points
    circulant = -2.0 / (points * spacing) * (np.sin(2.0 * np.pi * phases / points) @ modified)
    shifts = (np.arange(points)[:, None] - np.arange(points)[None, :]) % points
    return circulant[shifts].T


@functools.lru_cache(maxsize=None)
def wall_tables(kind, points, rows, pad):
    lower, middle, upper, weights = system_rows(kind, points)
    system = np.diag(middle) + np.diag(lower[1:], -1) + np.diag(upper[:-1], 1)
    inv = np.linalg.inv(system)
    stencil = np.zeros((points, points + 6))
    for row in range(points):
        for offset in range(-3, 4):
            if weights[3 + offset, row] != 0.0:
                assert abs(offset) <= pad and 0 <= row + offset < points
                stencil[row, row + offset + 3] = weights[3 + offset, row]
    scale = inverse_metric(points) if kind == "slope" else np.ones(points)
    blocks = points // rows
    combine = np.zeros((blocks, rows + 2, rows + 2 * pad))
    rise_gain = np.zeros((blocks, rows))
    fall_gain = np.zeros((blocks, rows))
    rise_step = np.zeros(blocks)
    fall_step = np.zeros(blocks)
    for block in range(blocks):
        lo, hi = block * rows, block * rows + rows
        own = slice(lo, hi)
        rise_part = np.zeros(rows)
        fall_part = np.zeros(rows)
        alpha = np.zeros(rows)
        beta = np.zeros(rows)
        if block > 0:
            ref = hi if block < blocks - 1 else lo
            alpha = inv[own, lo - 1] / inv[ref, lo - 1]
            rise_step[block] = inv[ref, lo - 1] / inv[lo, lo - 1]
            fall_part = inv[lo - 1, own]
        if block < blocks - 1:
            ref = lo - 1 if block > 0 else hi - 1
            beta = inv[own, hi] / inv[ref, hi]
            fall_step[block] = inv[ref, hi] / inv[hi - 1, hi]
            rise_part = inv[hi, own]
        local = inv[own, own] - np.outer(alpha, rise_part) - np.outer(beta, fall_part)
        rows_stencil = stencil[own, lo - pad + 3 : hi + pad + 3]
        outside = stencil[own].copy()
        outside[:, lo - pad + 3 : hi + pad + 3] = 0.0
        assert not outside.any()
        combine[block, :rows] = scale[own, None] * (local @ rows_stencil)
        combine[block, rows] = rise_part @ rows_stencil
        combine[block, rows + 1] = fall_part @ rows_stencil
        rise_gain[block] = scale[own] * alpha
        fall_gain[block] = scale[own] * beta
    rounds = []
    shift = 1
    while shift < blocks:
        rise = np.zeros(blocks)
        fall = np.zeros(blocks)
        for block in range(blocks):
            if block - shift >= 0:
                rise[block] = np.prod(rise_step[block - shift + 1 : block + 1])
            if block + shift <= blocks - 1:
                fall[block] = np.prod(fall_step[block : block + shift])
        rounds.append((shift, rise, fall))
        shift *= 2
    return combine, rise_gain, fall_gain, rounds


def wall_apply(padded, kinds, rows, pad, position):
    count = lax.axis_size("gy")
    points = rows * count
    parts = [wall_tables(kind, points, rows, pad) for kind in kinds]
    pick = lambda table: lax.dynamic_index_in_dim(
        jnp.asarray(np.stack(table, axis=1), jnp.float32), position, 0, keepdims=False
    )
    combine = pick([part[0] for part in parts])
    rise_gain = pick([part[1] for part in parts])
    fall_gain = pick([part[2] for part in parts])
    summed = None
    for tap in range(rows + 2 * pad):
        term = combine[:, :, tap, None, None] * padded[:, None, tap]
        summed = term if summed is None else summed + term
    rise = summed[:, rows]
    fall = summed[:, rows + 1]
    for level, (shift, _, _) in enumerate(parts[0][3]):
        rise_coef = pick([part[3][level][1] for part in parts])
        fall_coef = pick([part[3][level][2] for part in parts])
        up_pairs = [(i, i + shift) for i in range(count - shift)]
        down_pairs = [(i + shift, i) for i in range(count - shift)]
        from_below = lax.ppermute(rise, "gy", up_pairs)
        from_above = lax.ppermute(fall, "gy", down_pairs)
        rise = rise + rise_coef[:, None, None] * from_below
        fall = fall + fall_coef[:, None, None] * from_above
    return (
        summed[:, :rows]
        + rise_gain[:, :, None, None] * rise[:, None]
        + fall_gain[:, :, None, None] * fall[:, None]
    )


def halo(block, width):
    count = lax.axis_size("gy")
    up_pairs = [(i, i + 1) for i in range(count - 1)]
    down_pairs = [(i + 1, i) for i in range(count - 1)]
    below = lax.ppermute(block[:, block.shape[1] - width :], "gy", up_pairs)
    above = lax.ppermute(block[:, :width], "gy", down_pairs)
    return jnp.concatenate([below, block, above], axis=1)


def stream_slope(fields, stream_matrix):
    flat_rows = fields.reshape(-1, stream_matrix.shape[0])
    return jnp.dot(
        flat_rows, stream_matrix, precision=HIGHEST, preferred_element_type=jnp.float32
    ).reshape(fields.shape)


def span_slope(fields, own_block, other_block):
    other = lax.ppermute(fields, "pa", [(0, 1), (1, 0)])
    return jnp.einsum("fyzx,zw->fywx", fields, own_block, precision=HIGHEST) + jnp.einsum(
        "fyzx,zw->fywx", other, other_block, precision=HIGHEST
    )


def flux_along(direction, momentum, energy, speed, push, gradients):
    divergence = gradients[0][0] + gradients[1][1] + gradients[2][2]
    conduct = VISCOSITY * GAMMA_GAS / ((GAMMA_GAS - 1.0) * PRANDTL)
    rows_out = [momentum[direction]]
    energy_flux = (energy + push) * speed[direction]
    for component in range(3):
        stress = VISCOSITY * (gradients[direction][component] + gradients[component][direction])
        if component == direction:
            stress = stress - 2.0 / 3.0 * VISCOSITY * divergence
            rows_out.append(momentum[component] * speed[direction] + push - stress)
        else:
            rows_out.append(momentum[component] * speed[direction] - stress)
        energy_flux = energy_flux - speed[component] * stress
    energy_flux = energy_flux - conduct * gradients[direction][3]
    rows_out.append(energy_flux)
    return jnp.stack(rows_out)


def per_device(mass_per_volume, mass_flux_vector, total_heat_content):
    rows, span_own, stream_cells = mass_per_volume.shape
    count = lax.axis_size("gy")
    points = rows * count
    position = lax.axis_index("gy")
    span_total = span_own * lax.axis_size("pa")
    stream_matrix = jnp.asarray(periodic_matrix(stream_cells, STREAM_STEP), jnp.float32)
    span_full = periodic_matrix(span_total, SPAN_STEP)
    own_block = jnp.asarray(span_full[:span_own, :span_own], jnp.float32)
    other_block = jnp.asarray(span_full[span_own : 2 * span_own, :span_own], jnp.float32)

    state = jnp.concatenate(
        [mass_per_volume[None], mass_flux_vector, total_heat_content[None]], axis=0
    )
    padded = halo(state, 3)
    global_rows = position * rows - 3 + jnp.arange(rows + 6)
    inside = ((global_rows >= 0) & (global_rows < points))[:, None, None]
    density = jnp.where(inside, padded[0], 1.0)
    speed_pad = padded[1:4] / density[None]
    kinetic = 0.5 * jnp.sum(speed_pad * padded[1:4], axis=0)
    push_pad = (GAMMA_GAS - 1.0) * (padded[4] - kinetic)
    warmth_pad = push_pad / density
    basic_pad = jnp.concatenate([speed_pad, warmth_pad[None]], axis=0)

    wall_grad = wall_apply(basic_pad, ["slope"] * 4, rows, 3, position)
    smoothed = wall_apply(padded, ["smooth"] * 5, rows, 3, position)

    basic = basic_pad[:, 3 : 3 + rows]
    speed = basic[:3]
    push = push_pad[3 : 3 + rows]
    grad_stream = stream_slope(basic, stream_matrix)
    grad_span = span_slope(basic, own_block, other_block)
    gradients = [grad_stream, wall_grad, grad_span]
    momentum = mass_flux_vector
    energy = total_heat_content

    flux_wall = flux_along(1, momentum, energy, speed, push, gradients)
    wall_term = wall_apply(halo(flux_wall, 2), ["slope"] * 5, rows, 2, position)
    stream_term = stream_slope(
        flux_along(0, momentum, energy, speed, push, gradients), stream_matrix
    )
    span_term = span_slope(
        flux_along(2, momentum, energy, speed, push, gradients), own_block, other_block
    )
    time_rate = -(stream_term + wall_term + span_term)
    own_rows = position * rows + jnp.arange(rows)
    at_wall = ((own_rows == 0) | (own_rows == points - 1))[None, :, None, None]
    held = jnp.where(at_wall, 0.0, time_rate[1:4])
    time_rate = jnp.concatenate([time_rate[:1], held, time_rate[4:]], axis=0)
    return (time_rate, smoothed)


def solution(mesh):
    placed = (P("gy", "pa", None), P(None, "gy", "pa", None), P("gy", "pa", None))
    return jax.shard_map(
        per_device,
        mesh=mesh,
        in_specs=placed,
        out_specs=(P(None, "gy", "pa", None), P(None, "gy", "pa", None)),
        check_vma=False,
    )
```

```python
import functools

import jax
import jax.numpy as jnp
import numpy as np
from jax import lax
from jax.sharding import PartitionSpec as P

GAMMA_GAS = 1.4
PRANDTL = 0.72
VISCOSITY = 0.25
ALPHA_FILTER = 0.499
ALPHA_SLOPE = 0.498
STRETCH = 1.2
STREAM_STEP = 1.0
SPAN_STEP = 0.5
HIGHEST = lax.Precision.HIGHEST


def slope_weights():
    near_weight = (2.0 + ALPHA_SLOPE) / 3.0
    far_weight = (4.0 * ALPHA_SLOPE - 1.0) / 12.0
    return (near_weight, far_weight)


def system_rows(system_kind, points):
    lower = np.zeros(points)
    middle = np.ones(points)
    upper = np.zeros(points)
    weights = np.zeros((7, points))
    if system_kind == "slope":
        near_weight, far_weight = slope_weights()
        lower[:] = ALPHA_SLOPE
        upper[:] = ALPHA_SLOPE
        weights[1] = -far_weight
        weights[2] = -near_weight
        weights[4] = near_weight
        weights[5] = far_weight
        for edge_row in (1, points - 2):
            lower[edge_row] = 0.25
            upper[edge_row] = 0.25
            weights[:, edge_row] = 0.0
            weights[2, edge_row] = -0.75
            weights[4, edge_row] = 0.75
        lower[0] = 0.0
        upper[0] = 2.0
        weights[:, 0] = 0.0
        weights[3, 0] = -2.5
        weights[4, 0] = 2.0
        weights[5, 0] = 0.5
        lower[points - 1] = 2.0
        upper[points - 1] = 0.0
        weights[:, points - 1] = 0.0
        weights[3, points - 1] = 2.5
        weights[2, points - 1] = -2.0
        weights[1, points - 1] = -0.5
    else:
        strength = ALPHA_FILTER
        lower[:] = strength
        upper[:] = strength
        weights[3] = 11.0 / 16.0 + 5.0 * strength / 8.0
        weights[2] = 15.0 / 64.0 + 17.0 * strength / 32.0
        weights[4] = weights[2]
        weights[1] = -3.0 / 32.0 + 3.0 * strength / 16.0
        weights[5] = weights[1]
        weights[0] = 1.0 / 64.0 - strength / 32.0
        weights[6] = weights[0]
        for edge_row in (2, points - 3):
            weights[:, edge_row] = 0.0
            weights[3, edge_row] = 5.0 / 8.0 + 3.0 * strength / 4.0
            weights[2, edge_row] = 0.25 + strength / 2.0
            weights[4, edge_row] = 0.25 + strength / 2.0
            weights[1, edge_row] = -1.0 / 16.0 + strength / 8.0
            weights[5, edge_row] = -1.0 / 16.0 + strength / 8.0
        for edge_row in (1, points - 2):
            weights[:, edge_row] = 0.0
            weights[3, edge_row] = 0.5 + strength
            weights[2, edge_row] = 0.25 + strength / 2.0
            weights[4, edge_row] = 0.25 + strength / 2.0
        for edge_row in (0, points - 1):
            lower[edge_row] = 0.0
            upper[edge_row] = 0.0
            weights[:, edge_row] = 0.0
            weights[3, edge_row] = 1.0
    return (lower, middle, upper, weights)


def inverse_metric(points):
    places = 2.0 * np.arange(points) / (points - 1) - 1.0
    growth = np.exp(STRETCH * places)
    cosh_values = 0.5 * (growth + 1.0 / growth)
    edge_growth = np.exp(STRETCH)
    tanh_value = (edge_growth - 1.0 / edge_growth) / (edge_growth + 1.0 / edge_growth)
    return tanh_value * cosh_values**2 / (0.64 * STRETCH)


def periodic_matrix(points, spacing):
    near_weight, far_weight = slope_weights()
    wave_numbers = np.arange(1, points // 2)
    angles = 2.0 * np.pi * wave_numbers / points
    modified = (2.0 * near_weight * np.sin(angles) + 2.0 * far_weight * np.sin(2.0 * angles)) / (
        1.0 + 2.0 * ALPHA_SLOPE * np.cos(angles)
    )
    phases = np.arange(points)[:, None] * wave_numbers[None, :] % points
    circulant = -2.0 / (points * spacing) * (np.sin(2.0 * np.pi * phases / points) @ modified)
    shifts = (np.arange(points)[:, None] - np.arange(points)[None, :]) % points
    return circulant[shifts].T


@functools.lru_cache(maxsize=None)
def wall_tables(kind, points, rows, pad):
    lower, middle, upper, weights = system_rows(kind, points)
    system = np.diag(middle) + np.diag(lower[1:], -1) + np.diag(upper[:-1], 1)
    inv = np.linalg.inv(system)
    stencil = np.zeros((points, points + 6))
    for row in range(points):
        for offset in range(-3, 4):
            if weights[3 + offset, row] != 0.0:
                assert abs(offset) <= pad and 0 <= row + offset < points
                stencil[row, row + offset + 3] = weights[3 + offset, row]
    scale = inverse_metric(points) if kind == "slope" else np.ones(points)
    blocks = points // rows
    combine = np.zeros((blocks, rows + 2, rows + 2 * pad))
    rise_gain = np.zeros((blocks, rows))
    fall_gain = np.zeros((blocks, rows))
    rise_step = np.zeros(blocks)
    fall_step = np.zeros(blocks)
    for block in range(blocks):
        lo, hi = block * rows, block * rows + rows
        own = slice(lo, hi)
        rise_part = np.zeros(rows)
        fall_part = np.zeros(rows)
        alpha = np.zeros(rows)
        beta = np.zeros(rows)
        if block > 0:
            ref = hi if block < blocks - 1 else lo
            alpha = inv[own, lo - 1] / inv[ref, lo - 1]
            rise_step[block] = inv[ref, lo - 1] / inv[lo, lo - 1]
            fall_part = inv[lo - 1, own]
        if block < blocks - 1:
            ref = lo - 1 if block > 0 else hi - 1
            beta = inv[own, hi] / inv[ref, hi]
            fall_step[block] = inv[ref, hi] / inv[hi - 1, hi]
            rise_part = inv[hi, own]
        local = inv[own, own] - np.outer(alpha, rise_part) - np.outer(beta, fall_part)
        rows_stencil = stencil[own, lo - pad + 3 : hi + pad + 3]
        outside = stencil[own].copy()
        outside[:, lo - pad + 3 : hi + pad + 3] = 0.0
        assert not outside.any()
        combine[block, :rows] = scale[own, None] * (local @ rows_stencil)
        combine[block, rows] = rise_part @ rows_stencil
        combine[block, rows + 1] = fall_part @ rows_stencil
        rise_gain[block] = scale[own] * alpha
        fall_gain[block] = scale[own] * beta
    rounds = []
    shift = 1
    while shift < blocks:
        rise = np.zeros(blocks)
        fall = np.zeros(blocks)
        for block in range(blocks):
            if block - shift >= 0:
                rise[block] = np.prod(rise_step[block - shift + 1 : block + 1])
            if block + shift <= blocks - 1:
                fall[block] = np.prod(fall_step[block : block + shift])
        rounds.append((shift, rise, fall))
        shift *= 2
    return combine, rise_gain, fall_gain, rounds


def wall_apply(groups, rows, pad, position):
    count = lax.axis_size("gy")
    points = rows * count
    tables = [wall_tables(kind, points, rows, pad) for _, kind in groups]
    pick = lambda table: lax.dynamic_index_in_dim(
        jnp.asarray(table, jnp.float32), position, 0, keepdims=False
    )

    def taps(padded, combine):
        summed = None
        for tap in range(rows + 2 * pad):
            term = combine[:, tap, None, None] * padded[:, None, tap]
            summed = term if summed is None else summed + term
        return summed

    partials = [
        taps(padded, pick(table[0])[rows:]) for (padded, _), table in zip(groups, tables)
    ]
    sizes = [padded.shape[0] for padded, _ in groups]
    rise = jnp.concatenate([part[:, 0] for part in partials], axis=0)
    fall = jnp.concatenate([part[:, 1] for part in partials], axis=0)
    for level, (shift, _, _) in enumerate(tables[0][3]):
        rise_coef = pick(
            np.concatenate([np.repeat(t[3][level][1][:, None], n, 1) for t, n in zip(tables, sizes)], 1)
        )
        fall_coef = pick(
            np.concatenate([np.repeat(t[3][level][2][:, None], n, 1) for t, n in zip(tables, sizes)], 1)
        )
        up_pairs = [(i, i + shift) for i in range(count - shift)]
        down_pairs = [(i + shift, i) for i in range(count - shift)]
        from_below = lax.ppermute(rise, "gy", up_pairs)
        from_above = lax.ppermute(fall, "gy", down_pairs)
        rise = rise + rise_coef[:, None, None] * from_below
        fall = fall + fall_coef[:, None, None] * from_above
    results = []
    first = 0
    for (padded, _), table, size in zip(groups, tables, sizes):
        local = taps(padded, pick(table[0])[:rows])
        rise_gain = pick(table[1])
        fall_gain = pick(table[2])
        results.append(
            local
            + rise_gain[None, :, None, None] * rise[first : first + size, None]
            + fall_gain[None, :, None, None] * fall[first : first + size, None]
        )
        first += size
    return results


def halo(block, width):
    count = lax.axis_size("gy")
    up_pairs = [(i, i + 1) for i in range(count - 1)]
    down_pairs = [(i + 1, i) for i in range(count - 1)]
    below = lax.ppermute(block[:, block.shape[1] - width :], "gy", up_pairs)
    above = lax.ppermute(block[:, :width], "gy", down_pairs)
    return jnp.concatenate([below, block, above], axis=1)


def stream_slope(fields, stream_matrix):
    flat_rows = fields.reshape(-1, stream_matrix.shape[0])
    return jnp.dot(
        flat_rows, stream_matrix, precision=HIGHEST, preferred_element_type=jnp.float32
    ).reshape(fields.shape)


def span_slope(fields, own_block, other_block):
    other = lax.ppermute(fields, "pa", [(0, 1), (1, 0)])
    return jnp.einsum("fyzx,zw->fywx", fields, own_block, precision=HIGHEST) + jnp.einsum(
        "fyzx,zw->fywx", other, other_block, precision=HIGHEST
    )


def flux_along(direction, momentum, energy, speed, push, gradients):
    divergence = gradients[0][0] + gradients[1][1] + gradients[2][2]
    conduct = VISCOSITY * GAMMA_GAS / ((GAMMA_GAS - 1.0) * PRANDTL)
    rows_out = [momentum[direction]]
    energy_flux = (energy + push) * speed[direction]
    for component in range(3):
        stress = VISCOSITY * (gradients[direction][component] + gradients[component][direction])
        if component == direction:
            stress = stress - 2.0 / 3.0 * VISCOSITY * divergence
            rows_out.append(momentum[component] * speed[direction] + push - stress)
        else:
            rows_out.append(momentum[component] * speed[direction] - stress)
        energy_flux = energy_flux - speed[component] * stress
    energy_flux = energy_flux - conduct * gradients[direction][3]
    rows_out.append(energy_flux)
    return jnp.stack(rows_out)


def per_device(mass_per_volume, mass_flux_vector, total_heat_content):
    rows, span_own, stream_cells = mass_per_volume.shape
    count = lax.axis_size("gy")
    points = rows * count
    position = lax.axis_index("gy")
    span_total = span_own * lax.axis_size("pa")
    stream_matrix = jnp.asarray(periodic_matrix(stream_cells, STREAM_STEP), jnp.float32)
    span_full = periodic_matrix(span_total, SPAN_STEP)
    own_block = jnp.asarray(span_full[:span_own, :span_own], jnp.float32)
    other_block = jnp.asarray(span_full[span_own : 2 * span_own, :span_own], jnp.float32)

    state = jnp.concatenate(
        [mass_per_volume[None], mass_flux_vector, total_heat_content[None]], axis=0
    )
    padded = halo(state, 3)
    global_rows = position * rows - 3 + jnp.arange(rows + 6)
    inside = ((global_rows >= 0) & (global_rows < points))[:, None, None]
    density = jnp.where(inside, padded[0], 1.0)
    speed_pad = padded[1:4] / density[None]
    kinetic = 0.5 * jnp.sum(speed_pad * padded[1:4], axis=0)
    push_pad = (GAMMA_GAS - 1.0) * (padded[4] - kinetic)
    warmth_pad = push_pad / density
    basic_pad = jnp.concatenate([speed_pad, warmth_pad[None]], axis=0)

    wall_grad, smoothed = wall_apply(
        [(basic_pad, "slope"), (padded, "smooth")], rows, 3, position
    )

    basic = basic_pad[:, 3 : 3 + rows]
    speed = basic[:3]
    push = push_pad[3 : 3 + rows]
    grad_stream = stream_slope(basic, stream_matrix)
    grad_span = span_slope(basic, own_block, other_block)
    gradients = [grad_stream, wall_grad, grad_span]
    momentum = mass_flux_vector
    energy = total_heat_content

    flux_wall = flux_along(1, momentum, energy, speed, push, gradients)
    (wall_term,) = wall_apply([(halo(flux_wall, 2), "slope")], rows, 2, position)
    stream_term = stream_slope(
        flux_along(0, momentum, energy, speed, push, gradients), stream_matrix
    )
    span_term = span_slope(
        flux_along(2, momentum, energy, speed, push, gradients), own_block, other_block
    )
    time_rate = -(stream_term + wall_term + span_term)
    own_rows = position * rows + jnp.arange(rows)
    at_wall = ((own_rows == 0) | (own_rows == points - 1))[None, :, None, None]
    held = jnp.where(at_wall, 0.0, time_rate[1:4])
    time_rate = jnp.concatenate([time_rate[:1], held, time_rate[4:]], axis=0)
    return (time_rate, smoothed)


def solution(mesh):
    placed = (P("gy", "pa", None), P(None, "gy", "pa", None), P("gy", "pa", None))
    return jax.shard_map(
        per_device,
        mesh=mesh,
        in_specs=placed,
        out_specs=(P(None, "gy", "pa", None), P(None, "gy", "pa", None)),
        check_vma=False,
    )
```

```python
import functools

import jax
import jax.numpy as jnp
import numpy as np
from jax import lax
from jax.sharding import PartitionSpec as P

GAMMA_GAS = 1.4
PRANDTL = 0.72
VISCOSITY = 0.25
ALPHA_FILTER = 0.499
ALPHA_SLOPE = 0.498
STRETCH = 1.2
STREAM_STEP = 1.0
SPAN_STEP = 0.5
HIGHEST = lax.Precision.HIGHEST


def slope_weights():
    near_weight = (2.0 + ALPHA_SLOPE) / 3.0
    far_weight = (4.0 * ALPHA_SLOPE - 1.0) / 12.0
    return (near_weight, far_weight)


def system_rows(system_kind, points):
    lower = np.zeros(points)
    middle = np.ones(points)
    upper = np.zeros(points)
    weights = np.zeros((7, points))
    if system_kind == "slope":
        near_weight, far_weight = slope_weights()
        lower[:] = ALPHA_SLOPE
        upper[:] = ALPHA_SLOPE
        weights[1] = -far_weight
        weights[2] = -near_weight
        weights[4] = near_weight
        weights[5] = far_weight
        for edge_row in (1, points - 2):
            lower[edge_row] = 0.25
            upper[edge_row] = 0.25
            weights[:, edge_row] = 0.0
            weights[2, edge_row] = -0.75
            weights[4, edge_row] = 0.75
        lower[0] = 0.0
        upper[0] = 2.0
        weights[:, 0] = 0.0
        weights[3, 0] = -2.5
        weights[4, 0] = 2.0
        weights[5, 0] = 0.5
        lower[points - 1] = 2.0
        upper[points - 1] = 0.0
        weights[:, points - 1] = 0.0
        weights[3, points - 1] = 2.5
        weights[2, points - 1] = -2.0
        weights[1, points - 1] = -0.5
    else:
        strength = ALPHA_FILTER
        lower[:] = strength
        upper[:] = strength
        weights[3] = 11.0 / 16.0 + 5.0 * strength / 8.0
        weights[2] = 15.0 / 64.0 + 17.0 * strength / 32.0
        weights[4] = weights[2]
        weights[1] = -3.0 / 32.0 + 3.0 * strength / 16.0
        weights[5] = weights[1]
        weights[0] = 1.0 / 64.0 - strength / 32.0
        weights[6] = weights[0]
        for edge_row in (2, points - 3):
            weights[:, edge_row] = 0.0
            weights[3, edge_row] = 5.0 / 8.0 + 3.0 * strength / 4.0
            weights[2, edge_row] = 0.25 + strength / 2.0
            weights[4, edge_row] = 0.25 + strength / 2.0
            weights[1, edge_row] = -1.0 / 16.0 + strength / 8.0
            weights[5, edge_row] = -1.0 / 16.0 + strength / 8.0
        for edge_row in (1, points - 2):
            weights[:, edge_row] = 0.0
            weights[3, edge_row] = 0.5 + strength
            weights[2, edge_row] = 0.25 + strength / 2.0
            weights[4, edge_row] = 0.25 + strength / 2.0
        for edge_row in (0, points - 1):
            lower[edge_row] = 0.0
            upper[edge_row] = 0.0
            weights[:, edge_row] = 0.0
            weights[3, edge_row] = 1.0
    return (lower, middle, upper, weights)


def inverse_metric(points):
    places = 2.0 * np.arange(points) / (points - 1) - 1.0
    growth = np.exp(STRETCH * places)
    cosh_values = 0.5 * (growth + 1.0 / growth)
    edge_growth = np.exp(STRETCH)
    tanh_value = (edge_growth - 1.0 / edge_growth) / (edge_growth + 1.0 / edge_growth)
    return tanh_value * cosh_values**2 / (0.64 * STRETCH)


def periodic_matrix(points, spacing):
    near_weight, far_weight = slope_weights()
    wave_numbers = np.arange(1, points // 2)
    angles = 2.0 * np.pi * wave_numbers / points
    modified = (2.0 * near_weight * np.sin(angles) + 2.0 * far_weight * np.sin(2.0 * angles)) / (
        1.0 + 2.0 * ALPHA_SLOPE * np.cos(angles)
    )
    phases = np.arange(points)[:, None] * wave_numbers[None, :] % points
    circulant = -2.0 / (points * spacing) * (np.sin(2.0 * np.pi * phases / points) @ modified)
    shifts = (np.arange(points)[:, None] - np.arange(points)[None, :]) % points
    return circulant[shifts].T


@functools.lru_cache(maxsize=None)
def wall_tables(kind, points, rows, pad):
    lower, middle, upper, weights = system_rows(kind, points)
    system = np.diag(middle) + np.diag(lower[1:], -1) + np.diag(upper[:-1], 1)
    inv = np.linalg.inv(system)
    stencil = np.zeros((points, points + 6))
    for row in range(points):
        for offset in range(-3, 4):
            if weights[3 + offset, row] != 0.0:
                assert abs(offset) <= pad and 0 <= row + offset < points
                stencil[row, row + offset + 3] = weights[3 + offset, row]
    scale = inverse_metric(points) if kind == "slope" else np.ones(points)
    blocks = points // rows
    combine = np.zeros((blocks, rows + 2, rows + 2 * pad))
    rise_gain = np.zeros((blocks, rows))
    fall_gain = np.zeros((blocks, rows))
    rise_step = np.zeros(blocks)
    fall_step = np.zeros(blocks)
    for block in range(blocks):
        lo, hi = block * rows, block * rows + rows
        own = slice(lo, hi)
        rise_part = np.zeros(rows)
        fall_part = np.zeros(rows)
        alpha = np.zeros(rows)
        beta = np.zeros(rows)
        if block > 0:
            ref = hi if block < blocks - 1 else lo
            alpha = inv[own, lo - 1] / inv[ref, lo - 1]
            rise_step[block] = inv[ref, lo - 1] / inv[lo, lo - 1]
            fall_part = inv[lo - 1, own]
        if block < blocks - 1:
            ref = lo - 1 if block > 0 else hi - 1
            beta = inv[own, hi] / inv[ref, hi]
            fall_step[block] = inv[ref, hi] / inv[hi - 1, hi]
            rise_part = inv[hi, own]
        local = inv[own, own] - np.outer(alpha, rise_part) - np.outer(beta, fall_part)
        rows_stencil = stencil[own, lo - pad + 3 : hi + pad + 3]
        outside = stencil[own].copy()
        outside[:, lo - pad + 3 : hi + pad + 3] = 0.0
        assert not outside.any()
        combine[block, :rows] = scale[own, None] * (local @ rows_stencil)
        combine[block, rows] = rise_part @ rows_stencil
        combine[block, rows + 1] = fall_part @ rows_stencil
        rise_gain[block] = scale[own] * alpha
        fall_gain[block] = scale[own] * beta
    return combine, rise_gain, fall_gain, rise_step, fall_step


def scan_rounds(blocks):
    rounds = []
    stride = 1
    while stride < blocks:
        radix = min(4, -(-blocks // stride))
        rounds.append((stride, list(range(1, radix))))
        stride *= radix
    return rounds


def scan_coefs(rise_step, fall_step, shift):
    blocks = rise_step.shape[0]
    rise = np.zeros(blocks)
    fall = np.zeros(blocks)
    for block in range(blocks):
        if block - shift >= 0:
            rise[block] = np.prod(rise_step[block - shift + 1 : block + 1])
        if block + shift <= blocks - 1:
            fall[block] = np.prod(fall_step[block : block + shift])
    return rise, fall


class TableBank:
    def __init__(self):
        self.parts = []
        self.width = 0

    def add(self, table):
        table = np.asarray(table, np.float64)
        handle = (self.width, table.shape[1:])
        self.parts.append(table.reshape(table.shape[0], -1))
        self.width += self.parts[-1].shape[1]
        return handle

    def lookup(self, position):
        whole = jnp.asarray(np.concatenate(self.parts, axis=1), jnp.float32)
        self.row = lax.dynamic_index_in_dim(whole, position, 0, keepdims=False)

    def get(self, handle):
        start, shape = handle
        return self.row[start : start + int(np.prod(shape))].reshape(shape)


def plan_wall(bank, kinds_sizes, points, rows, pad):
    tables = [wall_tables(kind, points, rows, pad) for kind, _ in kinds_sizes]
    groups = [
        (bank.add(table[0]), bank.add(table[1]), bank.add(table[2])) for table in tables
    ]
    blocks = points // rows
    rounds = []
    for stride, multiples in scan_rounds(blocks):
        entries = []
        for multiple in multiples:
            shift = stride * multiple
            coefs = [scan_coefs(table[3], table[4], shift) for table in tables]
            rise = np.concatenate(
                [np.repeat(c[0][:, None], n, 1) for c, (_, n) in zip(coefs, kinds_sizes)], 1
            )
            fall = np.concatenate(
                [np.repeat(c[1][:, None], n, 1) for c, (_, n) in zip(coefs, kinds_sizes)], 1
            )
            entries.append((shift, bank.add(rise), bank.add(fall)))
        rounds.append(entries)
    return groups, rounds


def wall_apply(bank, plan, padded_groups, rows, pad):
    count = lax.axis_size("gy")
    groups, rounds = plan

    def taps(padded, combine):
        summed = None
        for tap in range(rows + 2 * pad):
            term = combine[:, tap, None, None] * padded[:, None, tap]
            summed = term if summed is None else summed + term
        return summed

    partials = [
        taps(padded, bank.get(handles[0])[rows:])
        for padded, handles in zip(padded_groups, groups)
    ]
    sizes = [padded.shape[0] for padded in padded_groups]
    rise = jnp.concatenate([part[:, 0] for part in partials], axis=0)
    fall = jnp.concatenate([part[:, 1] for part in partials], axis=0)
    for entries in rounds:
        rise_next, fall_next = rise, fall
        for shift, rise_handle, fall_handle in entries:
            up_pairs = [(i, i + shift) for i in range(count - shift)]
            down_pairs = [(i + shift, i) for i in range(count - shift)]
            from_below = lax.ppermute(rise, "gy", up_pairs)
            from_above = lax.ppermute(fall, "gy", down_pairs)
            rise_next = rise_next + bank.get(rise_handle)[:, None, None] * from_below
            fall_next = fall_next + bank.get(fall_handle)[:, None, None] * from_above
        rise, fall = rise_next, fall_next
    results = []
    first = 0
    for padded, handles, size in zip(padded_groups, groups, sizes):
        local = taps(padded, bank.get(handles[0])[:rows])
        rise_gain = bank.get(handles[1])
        fall_gain = bank.get(handles[2])
        results.append(
            local
            + rise_gain[None, :, None, None] * rise[first : first + size, None]
            + fall_gain[None, :, None, None] * fall[first : first + size, None]
        )
        first += size
    return results


def halo(block, width):
    count = lax.axis_size("gy")
    up_pairs = [(i, i + 1) for i in range(count - 1)]
    down_pairs = [(i + 1, i) for i in range(count - 1)]
    below = lax.ppermute(block[:, block.shape[1] - width :], "gy", up_pairs)
    above = lax.ppermute(block[:, :width], "gy", down_pairs)
    return jnp.concatenate([below, block, above], axis=1)


def stream_slope(fields, stream_matrix):
    flat_rows = fields.reshape(-1, stream_matrix.shape[0])
    return jnp.dot(
        flat_rows, stream_matrix, precision=HIGHEST, preferred_element_type=jnp.float32
    ).reshape(fields.shape)


def span_slope(fields, own_block, other_block):
    other = lax.ppermute(fields, "pa", [(0, 1), (1, 0)])
    return jnp.einsum("fyzx,zw->fywx", fields, own_block, precision=HIGHEST) + jnp.einsum(
        "fyzx,zw->fywx", other, other_block, precision=HIGHEST
    )


def flux_along(direction, momentum, energy, speed, push, gradients):
    divergence = gradients[0][0] + gradients[1][1] + gradients[2][2]
    conduct = VISCOSITY * GAMMA_GAS / ((GAMMA_GAS - 1.0) * PRANDTL)
    rows_out = [momentum[direction]]
    energy_flux = (energy + push) * speed[direction]
    for component in range(3):
        stress = VISCOSITY * (gradients[direction][component] + gradients[component][direction])
        if component == direction:
            stress = stress - 2.0 / 3.0 * VISCOSITY * divergence
            rows_out.append(momentum[component] * speed[direction] + push - stress)
        else:
            rows_out.append(momentum[component] * speed[direction] - stress)
        energy_flux = energy_flux - speed[component] * stress
    energy_flux = energy_flux - conduct * gradients[direction][3]
    rows_out.append(energy_flux)
    return jnp.stack(rows_out)


def per_device(mass_per_volume, mass_flux_vector, total_heat_content):
    rows, span_own, stream_cells = mass_per_volume.shape
    count = lax.axis_size("gy")
    points = rows * count
    position = lax.axis_index("gy")
    span_total = span_own * lax.axis_size("pa")
    stream_matrix = jnp.asarray(periodic_matrix(stream_cells, STREAM_STEP), jnp.float32)
    span_full = periodic_matrix(span_total, SPAN_STEP)
    own_block = jnp.asarray(span_full[:span_own, :span_own], jnp.float32)
    other_block = jnp.asarray(span_full[span_own : 2 * span_own, :span_own], jnp.float32)

    bank = TableBank()
    first_plan = plan_wall(bank, [("slope", 4), ("smooth", 5)], points, rows, 3)
    second_plan = plan_wall(bank, [("slope", 5)], points, rows, 2)
    bank.lookup(position)

    state = jnp.concatenate(
        [mass_per_volume[None], mass_flux_vector, total_heat_content[None]], axis=0
    )
    padded = halo(state, 3)
    global_rows = position * rows - 3 + jnp.arange(rows + 6)
    inside = ((global_rows >= 0) & (global_rows < points))[:, None, None]
    density = jnp.where(inside, padded[0], 1.0)
    speed_pad = padded[1:4] / density[None]
    kinetic = 0.5 * jnp.sum(speed_pad * padded[1:4], axis=0)
    push_pad = (GAMMA_GAS - 1.0) * (padded[4] - kinetic)
    warmth_pad = push_pad / density
    basic_pad = jnp.concatenate([speed_pad, warmth_pad[None]], axis=0)

    wall_grad, smoothed = wall_apply(bank, first_plan, [basic_pad, padded], rows, 3)

    basic = basic_pad[:, 3 : 3 + rows]
    speed = basic[:3]
    push = push_pad[3 : 3 + rows]
    grad_stream = stream_slope(basic, stream_matrix)
    grad_span = span_slope(basic, own_block, other_block)
    gradients = [grad_stream, wall_grad, grad_span]
    momentum = mass_flux_vector
    energy = total_heat_content

    flux_wall = flux_along(1, momentum, energy, speed, push, gradients)
    (wall_term,) = wall_apply(bank, second_plan, [halo(flux_wall, 2)], rows, 2)
    stream_term = stream_slope(
        flux_along(0, momentum, energy, speed, push, gradients), stream_matrix
    )
    span_term = span_slope(
        flux_along(2, momentum, energy, speed, push, gradients), own_block, other_block
    )
    time_rate = -(stream_term + wall_term + span_term)
    own_rows = position * rows + jnp.arange(rows)
    at_wall = ((own_rows == 0) | (own_rows == points - 1))[None, :, None, None]
    held = jnp.where(at_wall, 0.0, time_rate[1:4])
    time_rate = jnp.concatenate([time_rate[:1], held, time_rate[4:]], axis=0)
    return (time_rate, smoothed)


def solution(mesh):
    placed = (P("gy", "pa", None), P(None, "gy", "pa", None), P("gy", "pa", None))
    return jax.shard_map(
        per_device,
        mesh=mesh,
        in_specs=placed,
        out_specs=(P(None, "gy", "pa", None), P(None, "gy", "pa", None)),
        check_vma=False,
    )
```

```python
import functools

import jax
import jax.numpy as jnp
import numpy as np
from jax import lax
from jax.sharding import PartitionSpec as P

GAMMA_GAS = 1.4
PRANDTL = 0.72
VISCOSITY = 0.25
ALPHA_FILTER = 0.499
ALPHA_SLOPE = 0.498
STRETCH = 1.2
STREAM_STEP = 1.0
SPAN_STEP = 0.5
HIGHEST = lax.Precision.HIGHEST
LEVEL_AXES = ("gx", "gm", "gz")
WALL_AXES = ("gz", "gm", "gx")


def slope_weights():
    near_weight = (2.0 + ALPHA_SLOPE) / 3.0
    far_weight = (4.0 * ALPHA_SLOPE - 1.0) / 12.0
    return (near_weight, far_weight)


def system_rows(system_kind, points):
    lower = np.zeros(points)
    middle = np.ones(points)
    upper = np.zeros(points)
    weights = np.zeros((7, points))
    if system_kind == "slope":
        near_weight, far_weight = slope_weights()
        lower[:] = ALPHA_SLOPE
        upper[:] = ALPHA_SLOPE
        weights[1] = -far_weight
        weights[2] = -near_weight
        weights[4] = near_weight
        weights[5] = far_weight
        for edge_row in (1, points - 2):
            lower[edge_row] = 0.25
            upper[edge_row] = 0.25
            weights[:, edge_row] = 0.0
            weights[2, edge_row] = -0.75
            weights[4, edge_row] = 0.75
        lower[0] = 0.0
        upper[0] = 2.0
        weights[:, 0] = 0.0
        weights[3, 0] = -2.5
        weights[4, 0] = 2.0
        weights[5, 0] = 0.5
        lower[points - 1] = 2.0
        upper[points - 1] = 0.0
        weights[:, points - 1] = 0.0
        weights[3, points - 1] = 2.5
        weights[2, points - 1] = -2.0
        weights[1, points - 1] = -0.5
    else:
        strength = ALPHA_FILTER
        lower[:] = strength
        upper[:] = strength
        weights[3] = 11.0 / 16.0 + 5.0 * strength / 8.0
        weights[2] = 15.0 / 64.0 + 17.0 * strength / 32.0
        weights[4] = weights[2]
        weights[1] = -3.0 / 32.0 + 3.0 * strength / 16.0
        weights[5] = weights[1]
        weights[0] = 1.0 / 64.0 - strength / 32.0
        weights[6] = weights[0]
        for edge_row in (2, points - 3):
            weights[:, edge_row] = 0.0
            weights[3, edge_row] = 5.0 / 8.0 + 3.0 * strength / 4.0
            weights[2, edge_row] = 0.25 + strength / 2.0
            weights[4, edge_row] = 0.25 + strength / 2.0
            weights[1, edge_row] = -1.0 / 16.0 + strength / 8.0
            weights[5, edge_row] = -1.0 / 16.0 + strength / 8.0
        for edge_row in (1, points - 2):
            weights[:, edge_row] = 0.0
            weights[3, edge_row] = 0.5 + strength
            weights[2, edge_row] = 0.25 + strength / 2.0
            weights[4, edge_row] = 0.25 + strength / 2.0
        for edge_row in (0, points - 1):
            lower[edge_row] = 0.0
            upper[edge_row] = 0.0
            weights[:, edge_row] = 0.0
            weights[3, edge_row] = 1.0
    return (lower, middle, upper, weights)


def inverse_metric(points):
    places = 2.0 * np.arange(points) / (points - 1) - 1.0
    growth = np.exp(STRETCH * places)
    cosh_values = 0.5 * (growth + 1.0 / growth)
    edge_growth = np.exp(STRETCH)
    tanh_value = (edge_growth - 1.0 / edge_growth) / (edge_growth + 1.0 / edge_growth)
    return tanh_value * cosh_values**2 / (0.64 * STRETCH)


def periodic_matrix(points, spacing):
    near_weight, far_weight = slope_weights()
    wave_numbers = np.arange(1, points // 2)
    angles = 2.0 * np.pi * wave_numbers / points
    modified = (2.0 * near_weight * np.sin(angles) + 2.0 * far_weight * np.sin(2.0 * angles)) / (
        1.0 + 2.0 * ALPHA_SLOPE * np.cos(angles)
    )
    phases = np.arange(points)[:, None] * wave_numbers[None, :] % points
    circulant = -2.0 / (points * spacing) * (np.sin(2.0 * np.pi * phases / points) @ modified)
    shifts = (np.arange(points)[:, None] - np.arange(points)[None, :]) % points
    return circulant[shifts].T


@functools.lru_cache(maxsize=None)
def wall_tables(kind, points, rows, pad):
    lower, middle, upper, weights = system_rows(kind, points)
    system = np.diag(middle) + np.diag(lower[1:], -1) + np.diag(upper[:-1], 1)
    inv = np.linalg.inv(system)
    stencil = np.zeros((points, points + 6))
    for row in range(points):
        for offset in range(-3, 4):
            if weights[3 + offset, row] != 0.0:
                assert abs(offset) <= pad and 0 <= row + offset < points
                stencil[row, row + offset + 3] = weights[3 + offset, row]
    scale = inverse_metric(points) if kind == "slope" else np.ones(points)
    blocks = points // rows
    combine = np.zeros((blocks, rows + 2, rows + 2 * pad))
    rise_gain = np.zeros((blocks, rows))
    fall_gain = np.zeros((blocks, rows))
    rise_step = np.zeros(blocks)
    fall_step = np.zeros(blocks)
    for block in range(blocks):
        lo, hi = block * rows, block * rows + rows
        own = slice(lo, hi)
        rise_part = np.zeros(rows)
        fall_part = np.zeros(rows)
        alpha = np.zeros(rows)
        beta = np.zeros(rows)
        if block > 0:
            ref = hi if block < blocks - 1 else lo
            alpha = inv[own, lo - 1] / inv[ref, lo - 1]
            rise_step[block] = inv[ref, lo - 1] / inv[lo, lo - 1]
            fall_part = inv[lo - 1, own]
        if block < blocks - 1:
            ref = lo - 1 if block > 0 else hi - 1
            beta = inv[own, hi] / inv[ref, hi]
            fall_step[block] = inv[ref, hi] / inv[hi - 1, hi]
            rise_part = inv[hi, own]
        local = inv[own, own] - np.outer(alpha, rise_part) - np.outer(beta, fall_part)
        rows_stencil = stencil[own, lo - pad + 3 : hi + pad + 3]
        outside = stencil[own].copy()
        outside[:, lo - pad + 3 : hi + pad + 3] = 0.0
        assert not outside.any()
        combine[block, :rows] = scale[own, None] * (local @ rows_stencil)
        combine[block, rows] = rise_part @ rows_stencil
        combine[block, rows + 1] = fall_part @ rows_stencil
        rise_gain[block] = scale[own] * alpha
        fall_gain[block] = scale[own] * beta
    return combine, rise_gain, fall_gain, rise_step, fall_step


def level_tables(rise_step, fall_step, sizes):
    blocks = rise_step.shape[0]

    def rise_weight(source, target):
        return np.prod(rise_step[source + 1 : target + 1]) if source <= target else 0.0

    def fall_weight(source, target):
        return np.prod(fall_step[target:source]) if source >= target else 0.0

    levels = []
    stride = 1
    for level, size in enumerate(sizes):
        span = stride * size
        rise_own = np.zeros((blocks, size))
        rise_total = np.zeros((blocks, size))
        fall_own = np.zeros((blocks, size))
        fall_total = np.zeros((blocks, size))
        for block in range(blocks):
            base = block // span * span
            mine = block // stride % size
            last, first = base + span - 1, base
            for member in range(size):
                group_first = base + member * stride
                group_last = group_first + stride - 1
                if level == 0 or member < mine:
                    rise_own[block, member] = rise_weight(group_last, block)
                if level == 0 or member > mine:
                    fall_own[block, member] = fall_weight(group_first, block)
                rise_total[block, member] = rise_weight(group_last, last)
                fall_total[block, member] = fall_weight(group_first, first)
        levels.append((rise_own, rise_total, fall_own, fall_total))
        stride = span
    return levels


class TableBank:
    def __init__(self):
        self.parts = []
        self.width = 0

    def add(self, table):
        table = np.asarray(table, np.float64)
        handle = (self.width, table.shape[1:])
        self.parts.append(table.reshape(table.shape[0], -1))
        self.width += self.parts[-1].shape[1]
        return handle

    def lookup(self, position):
        whole = jnp.asarray(np.concatenate(self.parts, axis=1), jnp.float32)
        self.row = lax.dynamic_index_in_dim(whole, position, 0, keepdims=False)

    def get(self, handle):
        start, shape = handle
        return self.row[start : start + int(np.prod(shape))].reshape(shape)


def plan_wall(bank, kinds_sizes, points, rows, pad, sizes):
    tables = [wall_tables(kind, points, rows, pad) for kind, _ in kinds_sizes]
    groups = [
        (bank.add(table[0]), bank.add(table[1]), bank.add(table[2])) for table in tables
    ]
    per_kind = [level_tables(table[3], table[4], sizes) for table in tables]
    levels = []
    for level in range(len(sizes)):
        handles = []
        for part in range(4):
            joined = np.concatenate(
                [
                    np.repeat(kind_levels[level][part][:, :, None], n, 2)
                    for kind_levels, (_, n) in zip(per_kind, kinds_sizes)
                ],
                2,
            )
            handles.append(bank.add(joined))
        levels.append(handles)
    return groups, levels


def wall_apply(bank, plan, padded_groups, rows, pad):
    groups, levels = plan

    def taps(padded, combine):
        summed = None
        for tap in range(rows + 2 * pad):
            term = combine[:, tap, None, None] * padded[:, None, tap]
            summed = term if summed is None else summed + term
        return summed

    partials = [
        taps(padded, bank.get(handles[0])[rows:])
        for padded, handles in zip(padded_groups, groups)
    ]
    sizes = [padded.shape[0] for padded in padded_groups]
    rise_total = jnp.concatenate([part[:, 0] for part in partials], axis=0)
    fall_total = jnp.concatenate([part[:, 1] for part in partials], axis=0)
    rise = fall = None
    for axis, handles in zip(LEVEL_AXES, levels):
        gathered = lax.all_gather(jnp.stack([rise_total, fall_total]), axis)
        weights = [bank.get(handle)[:, :, None, None] for handle in handles]
        rise_part = jnp.sum(weights[0] * gathered[:, 0], axis=0)
        fall_part = jnp.sum(weights[2] * gathered[:, 1], axis=0)
        rise = rise_part if rise is None else rise + rise_part
        fall = fall_part if fall is None else fall + fall_part
        rise_total = jnp.sum(weights[1] * gathered[:, 0], axis=0)
        fall_total = jnp.sum(weights[3] * gathered[:, 1], axis=0)
    results = []
    first = 0
    for padded, handles, size in zip(padded_groups, groups, sizes):
        local = taps(padded, bank.get(handles[0])[:rows])
        rise_gain = bank.get(handles[1])
        fall_gain = bank.get(handles[2])
        results.append(
            local
            + rise_gain[None, :, None, None] * rise[first : first + size, None]
            + fall_gain[None, :, None, None] * fall[first : first + size, None]
        )
        first += size
    return results


def halo(block, width, count):
    up_pairs = [(i, i + 1) for i in range(count - 1)]
    down_pairs = [(i + 1, i) for i in range(count - 1)]
    below = lax.ppermute(block[:, block.shape[1] - width :], WALL_AXES, up_pairs)
    above = lax.ppermute(block[:, :width], WALL_AXES, down_pairs)
    return jnp.concatenate([below, block, above], axis=1)


def stream_slope(fields, stream_matrix):
    flat_rows = fields.reshape(-1, stream_matrix.shape[0])
    return jnp.dot(
        flat_rows, stream_matrix, precision=HIGHEST, preferred_element_type=jnp.float32
    ).reshape(fields.shape)


def span_slope(fields, own_block, other_block):
    other = lax.ppermute(fields, "pa", [(0, 1), (1, 0)])
    return jnp.einsum("fyzx,zw->fywx", fields, own_block, precision=HIGHEST) + jnp.einsum(
        "fyzx,zw->fywx", other, other_block, precision=HIGHEST
    )


def flux_along(direction, momentum, energy, speed, push, gradients):
    divergence = gradients[0][0] + gradients[1][1] + gradients[2][2]
    conduct = VISCOSITY * GAMMA_GAS / ((GAMMA_GAS - 1.0) * PRANDTL)
    rows_out = [momentum[direction]]
    energy_flux = (energy + push) * speed[direction]
    for component in range(3):
        stress = VISCOSITY * (gradients[direction][component] + gradients[component][direction])
        if component == direction:
            stress = stress - 2.0 / 3.0 * VISCOSITY * divergence
            rows_out.append(momentum[component] * speed[direction] + push - stress)
        else:
            rows_out.append(momentum[component] * speed[direction] - stress)
        energy_flux = energy_flux - speed[component] * stress
    energy_flux = energy_flux - conduct * gradients[direction][3]
    rows_out.append(energy_flux)
    return jnp.stack(rows_out)


def per_device(level_sizes, mass_per_volume, mass_flux_vector, total_heat_content):
    rows, span_own, stream_cells = mass_per_volume.shape
    count = int(np.prod(level_sizes))
    points = rows * count
    position = lax.axis_index(WALL_AXES)
    span_total = span_own * lax.axis_size("pa")
    stream_matrix = jnp.asarray(periodic_matrix(stream_cells, STREAM_STEP), jnp.float32)
    span_full = periodic_matrix(span_total, SPAN_STEP)
    own_block = jnp.asarray(span_full[:span_own, :span_own], jnp.float32)
    other_block = jnp.asarray(span_full[span_own : 2 * span_own, :span_own], jnp.float32)

    bank = TableBank()
    first_plan = plan_wall(
        bank, [("slope", 4), ("smooth", 5)], points, rows, 3, level_sizes
    )
    second_plan = plan_wall(bank, [("slope", 5)], points, rows, 2, level_sizes)
    bank.lookup(position)

    state = jnp.concatenate(
        [mass_per_volume[None], mass_flux_vector, total_heat_content[None]], axis=0
    )
    padded = halo(state, 3, count)
    global_rows = position * rows - 3 + jnp.arange(rows + 6)
    inside = ((global_rows >= 0) & (global_rows < points))[:, None, None]
    density = jnp.where(inside, padded[0], 1.0)
    speed_pad = padded[1:4] / density[None]
    kinetic = 0.5 * jnp.sum(speed_pad * padded[1:4], axis=0)
    push_pad = (GAMMA_GAS - 1.0) * (padded[4] - kinetic)
    warmth_pad = push_pad / density
    basic_pad = jnp.concatenate([speed_pad, warmth_pad[None]], axis=0)

    wall_grad, smoothed = wall_apply(bank, first_plan, [basic_pad, padded], rows, 3)

    basic = basic_pad[:, 3 : 3 + rows]
    speed = basic[:3]
    push = push_pad[3 : 3 + rows]
    grad_stream = stream_slope(basic, stream_matrix)
    grad_span = span_slope(basic, own_block, other_block)
    gradients = [grad_stream, wall_grad, grad_span]
    momentum = mass_flux_vector
    energy = total_heat_content

    flux_wall = flux_along(1, momentum, energy, speed, push, gradients)
    (wall_term,) = wall_apply(bank, second_plan, [halo(flux_wall, 2, count)], rows, 2)
    stream_term = stream_slope(
        flux_along(0, momentum, energy, speed, push, gradients), stream_matrix
    )
    span_term = span_slope(
        flux_along(2, momentum, energy, speed, push, gradients), own_block, other_block
    )
    time_rate = -(stream_term + wall_term + span_term)
    own_rows = position * rows + jnp.arange(rows)
    at_wall = ((own_rows == 0) | (own_rows == points - 1))[None, :, None, None]
    held = jnp.where(at_wall, 0.0, time_rate[1:4])
    time_rate = jnp.concatenate([time_rate[:1], held, time_rate[4:]], axis=0)
    return (time_rate, smoothed)


def solution(mesh):
    rows_devices = mesh.shape["gy"]
    fast = int(np.gcd(rows_devices, 4))
    middle = int(np.gcd(rows_devices // fast, 4))
    slow = rows_devices // fast // middle
    split = jax.sharding.Mesh(
        mesh.devices.reshape(slow, middle, fast, mesh.shape["pa"]), WALL_AXES + ("pa",)
    )
    placed = (
        P(WALL_AXES, "pa", None),
        P(None, WALL_AXES, "pa", None),
        P(WALL_AXES, "pa", None),
    )
    return jax.shard_map(
        functools.partial(per_device, (fast, middle, slow)),
        mesh=split,
        in_specs=placed,
        out_specs=(P(None, WALL_AXES, "pa", None), P(None, WALL_AXES, "pa", None)),
        check_vma=False,
    )
```

```python
import functools

import jax
import jax.numpy as jnp
import numpy as np
from jax import lax
from jax.sharding import PartitionSpec as P

GAMMA_GAS = 1.4
PRANDTL = 0.72
VISCOSITY = 0.25
ALPHA_FILTER = 0.499
ALPHA_SLOPE = 0.498
STRETCH = 1.2
STREAM_STEP = 1.0
SPAN_STEP = 0.5
HIGHEST = lax.Precision.HIGHEST


def slope_weights():
    near_weight = (2.0 + ALPHA_SLOPE) / 3.0
    far_weight = (4.0 * ALPHA_SLOPE - 1.0) / 12.0
    return (near_weight, far_weight)


def system_rows(system_kind, points):
    lower = np.zeros(points)
    middle = np.ones(points)
    upper = np.zeros(points)
    weights = np.zeros((7, points))
    if system_kind == "slope":
        near_weight, far_weight = slope_weights()
        lower[:] = ALPHA_SLOPE
        upper[:] = ALPHA_SLOPE
        weights[1] = -far_weight
        weights[2] = -near_weight
        weights[4] = near_weight
        weights[5] = far_weight
        for edge_row in (1, points - 2):
            lower[edge_row] = 0.25
            upper[edge_row] = 0.25
            weights[:, edge_row] = 0.0
            weights[2, edge_row] = -0.75
            weights[4, edge_row] = 0.75
        lower[0] = 0.0
        upper[0] = 2.0
        weights[:, 0] = 0.0
        weights[3, 0] = -2.5
        weights[4, 0] = 2.0
        weights[5, 0] = 0.5
        lower[points - 1] = 2.0
        upper[points - 1] = 0.0
        weights[:, points - 1] = 0.0
        weights[3, points - 1] = 2.5
        weights[2, points - 1] = -2.0
        weights[1, points - 1] = -0.5
    else:
        strength = ALPHA_FILTER
        lower[:] = strength
        upper[:] = strength
        weights[3] = 11.0 / 16.0 + 5.0 * strength / 8.0
        weights[2] = 15.0 / 64.0 + 17.0 * strength / 32.0
        weights[4] = weights[2]
        weights[1] = -3.0 / 32.0 + 3.0 * strength / 16.0
        weights[5] = weights[1]
        weights[0] = 1.0 / 64.0 - strength / 32.0
        weights[6] = weights[0]
        for edge_row in (2, points - 3):
            weights[:, edge_row] = 0.0
            weights[3, edge_row] = 5.0 / 8.0 + 3.0 * strength / 4.0
            weights[2, edge_row] = 0.25 + strength / 2.0
            weights[4, edge_row] = 0.25 + strength / 2.0
            weights[1, edge_row] = -1.0 / 16.0 + strength / 8.0
            weights[5, edge_row] = -1.0 / 16.0 + strength / 8.0
        for edge_row in (1, points - 2):
            weights[:, edge_row] = 0.0
            weights[3, edge_row] = 0.5 + strength
            weights[2, edge_row] = 0.25 + strength / 2.0
            weights[4, edge_row] = 0.25 + strength / 2.0
        for edge_row in (0, points - 1):
            lower[edge_row] = 0.0
            upper[edge_row] = 0.0
            weights[:, edge_row] = 0.0
            weights[3, edge_row] = 1.0
    return (lower, middle, upper, weights)


def inverse_metric(points):
    places = 2.0 * np.arange(points) / (points - 1) - 1.0
    growth = np.exp(STRETCH * places)
    cosh_values = 0.5 * (growth + 1.0 / growth)
    edge_growth = np.exp(STRETCH)
    tanh_value = (edge_growth - 1.0 / edge_growth) / (edge_growth + 1.0 / edge_growth)
    return tanh_value * cosh_values**2 / (0.64 * STRETCH)


def periodic_matrix(points, spacing):
    near_weight, far_weight = slope_weights()
    wave_numbers = np.arange(1, points // 2)
    angles = 2.0 * np.pi * wave_numbers / points
    modified = (2.0 * near_weight * np.sin(angles) + 2.0 * far_weight * np.sin(2.0 * angles)) / (
        1.0 + 2.0 * ALPHA_SLOPE * np.cos(angles)
    )
    phases = np.arange(points)[:, None] * wave_numbers[None, :] % points
    circulant = -2.0 / (points * spacing) * (np.sin(2.0 * np.pi * phases / points) @ modified)
    shifts = (np.arange(points)[:, None] - np.arange(points)[None, :]) % points
    return circulant[shifts].T


@functools.lru_cache(maxsize=None)
def wall_tables(kind, points, rows, pad):
    lower, middle, upper, weights = system_rows(kind, points)
    system = np.diag(middle) + np.diag(lower[1:], -1) + np.diag(upper[:-1], 1)
    inv = np.linalg.inv(system)
    stencil = np.zeros((points, points + 6))
    for row in range(points):
        for offset in range(-3, 4):
            if weights[3 + offset, row] != 0.0:
                assert abs(offset) <= pad and 0 <= row + offset < points
                stencil[row, row + offset + 3] = weights[3 + offset, row]
    scale = inverse_metric(points) if kind == "slope" else np.ones(points)
    blocks = points // rows
    combine = np.zeros((blocks, rows + 2, rows + 2 * pad))
    rise_gain = np.zeros((blocks, rows))
    fall_gain = np.zeros((blocks, rows))
    rise_step = np.zeros(blocks)
    fall_step = np.zeros(blocks)
    for block in range(blocks):
        lo, hi = block * rows, block * rows + rows
        own = slice(lo, hi)
        rise_part = np.zeros(rows)
        fall_part = np.zeros(rows)
        alpha = np.zeros(rows)
        beta = np.zeros(rows)
        if block > 0:
            ref = hi if block < blocks - 1 else lo
            alpha = inv[own, lo - 1] / inv[ref, lo - 1]
            rise_step[block] = inv[ref, lo - 1] / inv[lo, lo - 1]
            fall_part = inv[lo - 1, own]
        if block < blocks - 1:
            ref = lo - 1 if block > 0 else hi - 1
            beta = inv[own, hi] / inv[ref, hi]
            fall_step[block] = inv[ref, hi] / inv[hi - 1, hi]
            rise_part = inv[hi, own]
        local = inv[own, own] - np.outer(alpha, rise_part) - np.outer(beta, fall_part)
        rows_stencil = stencil[own, lo - pad + 3 : hi + pad + 3]
        outside = stencil[own].copy()
        outside[:, lo - pad + 3 : hi + pad + 3] = 0.0
        assert not outside.any()
        combine[block, :rows] = scale[own, None] * (local @ rows_stencil)
        combine[block, rows] = rise_part @ rows_stencil
        combine[block, rows + 1] = fall_part @ rows_stencil
        rise_gain[block] = scale[own] * alpha
        fall_gain[block] = scale[own] * beta
    return combine, rise_gain, fall_gain, rise_step, fall_step


def scan_rounds(blocks):
    rounds = []
    stride = 1
    while stride < blocks:
        radix = min(2, -(-blocks // stride))
        rounds.append((stride, list(range(1, radix))))
        stride *= radix
    return rounds


def scan_coefs(rise_step, fall_step, shift):
    blocks = rise_step.shape[0]
    rise = np.zeros(blocks)
    fall = np.zeros(blocks)
    for block in range(blocks):
        if block - shift >= 0:
            rise[block] = np.prod(rise_step[block - shift + 1 : block + 1])
        if block + shift <= blocks - 1:
            fall[block] = np.prod(fall_step[block : block + shift])
    return rise, fall


class TableBank:
    def __init__(self):
        self.parts = []
        self.width = 0

    def add(self, table):
        table = np.asarray(table, np.float64)
        handle = (self.width, table.shape[1:])
        self.parts.append(table.reshape(table.shape[0], -1))
        self.width += self.parts[-1].shape[1]
        return handle

    def lookup(self, position):
        whole = jnp.asarray(np.concatenate(self.parts, axis=1), jnp.float32)
        self.row = lax.dynamic_index_in_dim(whole, position, 0, keepdims=False)

    def get(self, handle):
        start, shape = handle
        return self.row[start : start + int(np.prod(shape))].reshape(shape)


def plan_wall(bank, kinds_sizes, points, rows, pad):
    tables = [wall_tables(kind, points, rows, pad) for kind, _ in kinds_sizes]
    groups = [
        (bank.add(table[0]), bank.add(table[1]), bank.add(table[2])) for table in tables
    ]
    blocks = points // rows
    rounds = []
    for stride, multiples in scan_rounds(blocks):
        entries = []
        for multiple in multiples:
            shift = stride * multiple
            coefs = [scan_coefs(table[3], table[4], shift) for table in tables]
            rise = np.concatenate(
                [np.repeat(c[0][:, None], n, 1) for c, (_, n) in zip(coefs, kinds_sizes)], 1
            )
            fall = np.concatenate(
                [np.repeat(c[1][:, None], n, 1) for c, (_, n) in zip(coefs, kinds_sizes)], 1
            )
            entries.append((shift, bank.add(rise), bank.add(fall)))
        rounds.append(entries)
    return groups, rounds


def wall_apply(bank, plan, padded_groups, rows, pad):
    count = lax.axis_size("gy")
    groups, rounds = plan

    def taps(padded, combine):
        summed = None
        for tap in range(rows + 2 * pad):
            term = combine[:, tap, None, None] * padded[:, None, tap]
            summed = term if summed is None else summed + term
        return summed

    partials = [
        taps(padded, bank.get(handles[0])[rows:])
        for padded, handles in zip(padded_groups, groups)
    ]
    sizes = [padded.shape[0] for padded in padded_groups]
    rise = jnp.concatenate([part[:, 0] for part in partials], axis=0)
    fall = jnp.concatenate([part[:, 1] for part in partials], axis=0)
    core = lax.axis_index("pa")
    first_core = core == 0
    swap = [(0, 1), (1, 0)]
    sent = lax.ppermute(jnp.where(first_core, fall, rise), "pa", swap)
    kept = jnp.where(first_core, rise, fall)
    carry = jnp.where(first_core, jnp.stack([kept, sent]), jnp.stack([sent, kept]))
    for entries in rounds:
        update = carry
        for shift, rise_handle, fall_handle in entries:
            pairs = [(2 * i, 2 * (i + shift)) for i in range(count - shift)]
            pairs += [(2 * (i + shift) + 1, 2 * i + 1) for i in range(count - shift)]
            arrived = lax.ppermute(carry, ("gy", "pa"), pairs)
            coef = jnp.where(first_core, bank.get(rise_handle), bank.get(fall_handle))
            update = update + coef[None, :, None, None] * arrived
        carry = update
    back = lax.ppermute(jnp.where(first_core, carry[1], carry[0]), "pa", swap)
    rise = jnp.where(first_core, carry[0], back)
    fall = jnp.where(first_core, back, carry[1])
    results = []
    first = 0
    for padded, handles, size in zip(padded_groups, groups, sizes):
        local = taps(padded, bank.get(handles[0])[:rows])
        rise_gain = bank.get(handles[1])
        fall_gain = bank.get(handles[2])
        results.append(
            local
            + rise_gain[None, :, None, None] * rise[first : first + size, None]
            + fall_gain[None, :, None, None] * fall[first : first + size, None]
        )
        first += size
    return results


def halo(block, width):
    count = lax.axis_size("gy")
    up_pairs = [(i, i + 1) for i in range(count - 1)]
    down_pairs = [(i + 1, i) for i in range(count - 1)]
    below = lax.ppermute(block[:, block.shape[1] - width :], "gy", up_pairs)
    above = lax.ppermute(block[:, :width], "gy", down_pairs)
    return jnp.concatenate([below, block, above], axis=1)


def stream_slope(fields, stream_matrix):
    flat_rows = fields.reshape(-1, stream_matrix.shape[0])
    return jnp.dot(
        flat_rows, stream_matrix, precision=HIGHEST, preferred_element_type=jnp.float32
    ).reshape(fields.shape)


def span_slope(fields, own_block, other_block):
    other = lax.ppermute(fields, "pa", [(0, 1), (1, 0)])
    return jnp.einsum("fyzx,zw->fywx", fields, own_block, precision=HIGHEST) + jnp.einsum(
        "fyzx,zw->fywx", other, other_block, precision=HIGHEST
    )


def flux_along(direction, momentum, energy, speed, push, gradients):
    divergence = gradients[0][0] + gradients[1][1] + gradients[2][2]
    conduct = VISCOSITY * GAMMA_GAS / ((GAMMA_GAS - 1.0) * PRANDTL)
    rows_out = [momentum[direction]]
    energy_flux = (energy + push) * speed[direction]
    for component in range(3):
        stress = VISCOSITY * (gradients[direction][component] + gradients[component][direction])
        if component == direction:
            stress = stress - 2.0 / 3.0 * VISCOSITY * divergence
            rows_out.append(momentum[component] * speed[direction] + push - stress)
        else:
            rows_out.append(momentum[component] * speed[direction] - stress)
        energy_flux = energy_flux - speed[component] * stress
    energy_flux = energy_flux - conduct * gradients[direction][3]
    rows_out.append(energy_flux)
    return jnp.stack(rows_out)


def per_device(mass_per_volume, mass_flux_vector, total_heat_content):
    rows, span_own, stream_cells = mass_per_volume.shape
    count = lax.axis_size("gy")
    points = rows * count
    position = lax.axis_index("gy")
    span_total = span_own * lax.axis_size("pa")
    stream_matrix = jnp.asarray(periodic_matrix(stream_cells, STREAM_STEP), jnp.float32)
    span_full = periodic_matrix(span_total, SPAN_STEP)
    own_block = jnp.asarray(span_full[:span_own, :span_own], jnp.float32)
    other_block = jnp.asarray(span_full[span_own : 2 * span_own, :span_own], jnp.float32)

    bank = TableBank()
    first_plan = plan_wall(bank, [("slope", 4), ("smooth", 5)], points, rows, 3)
    second_plan = plan_wall(bank, [("slope", 5)], points, rows, 2)
    bank.lookup(position)

    state = jnp.concatenate(
        [mass_per_volume[None], mass_flux_vector, total_heat_content[None]], axis=0
    )
    padded = halo(state, 3)
    global_rows = position * rows - 3 + jnp.arange(rows + 6)
    inside = ((global_rows >= 0) & (global_rows < points))[:, None, None]
    density = jnp.where(inside, padded[0], 1.0)
    speed_pad = padded[1:4] / density[None]
    kinetic = 0.5 * jnp.sum(speed_pad * padded[1:4], axis=0)
    push_pad = (GAMMA_GAS - 1.0) * (padded[4] - kinetic)
    warmth_pad = push_pad / density
    basic_pad = jnp.concatenate([speed_pad, warmth_pad[None]], axis=0)

    wall_grad, smoothed = wall_apply(bank, first_plan, [basic_pad, padded], rows, 3)

    basic = basic_pad[:, 3 : 3 + rows]
    speed = basic[:3]
    push = push_pad[3 : 3 + rows]
    grad_stream = stream_slope(basic, stream_matrix)
    grad_span = span_slope(basic, own_block, other_block)
    gradients = [grad_stream, wall_grad, grad_span]
    momentum = mass_flux_vector
    energy = total_heat_content

    flux_wall = flux_along(1, momentum, energy, speed, push, gradients)
    (wall_term,) = wall_apply(bank, second_plan, [halo(flux_wall, 2)], rows, 2)
    stream_term = stream_slope(
        flux_along(0, momentum, energy, speed, push, gradients), stream_matrix
    )
    span_term = span_slope(
        flux_along(2, momentum, energy, speed, push, gradients), own_block, other_block
    )
    time_rate = -(stream_term + wall_term + span_term)
    own_rows = position * rows + jnp.arange(rows)
    at_wall = ((own_rows == 0) | (own_rows == points - 1))[None, :, None, None]
    held = jnp.where(at_wall, 0.0, time_rate[1:4])
    time_rate = jnp.concatenate([time_rate[:1], held, time_rate[4:]], axis=0)
    return (time_rate, smoothed)


def solution(mesh):
    placed = (P("gy", "pa", None), P(None, "gy", "pa", None), P("gy", "pa", None))
    return jax.shard_map(
        per_device,
        mesh=mesh,
        in_specs=placed,
        out_specs=(P(None, "gy", "pa", None), P(None, "gy", "pa", None)),
        check_vma=False,
    )
```

```python
import functools

import jax
import jax.numpy as jnp
import numpy as np
from jax import lax
from jax.sharding import PartitionSpec as P

GAMMA_GAS = 1.4
PRANDTL = 0.72
VISCOSITY = 0.25
ALPHA_FILTER = 0.499
ALPHA_SLOPE = 0.498
STRETCH = 1.2
STREAM_STEP = 1.0
SPAN_STEP = 0.5
HIGHEST = lax.Precision.HIGHEST


def slope_weights():
    near_weight = (2.0 + ALPHA_SLOPE) / 3.0
    far_weight = (4.0 * ALPHA_SLOPE - 1.0) / 12.0
    return (near_weight, far_weight)


def system_rows(system_kind, points):
    lower = np.zeros(points)
    middle = np.ones(points)
    upper = np.zeros(points)
    weights = np.zeros((7, points))
    if system_kind == "slope":
        near_weight, far_weight = slope_weights()
        lower[:] = ALPHA_SLOPE
        upper[:] = ALPHA_SLOPE
        weights[1] = -far_weight
        weights[2] = -near_weight
        weights[4] = near_weight
        weights[5] = far_weight
        for edge_row in (1, points - 2):
            lower[edge_row] = 0.25
            upper[edge_row] = 0.25
            weights[:, edge_row] = 0.0
            weights[2, edge_row] = -0.75
            weights[4, edge_row] = 0.75
        lower[0] = 0.0
        upper[0] = 2.0
        weights[:, 0] = 0.0
        weights[3, 0] = -2.5
        weights[4, 0] = 2.0
        weights[5, 0] = 0.5
        lower[points - 1] = 2.0
        upper[points - 1] = 0.0
        weights[:, points - 1] = 0.0
        weights[3, points - 1] = 2.5
        weights[2, points - 1] = -2.0
        weights[1, points - 1] = -0.5
    else:
        strength = ALPHA_FILTER
        lower[:] = strength
        upper[:] = strength
        weights[3] = 11.0 / 16.0 + 5.0 * strength / 8.0
        weights[2] = 15.0 / 64.0 + 17.0 * strength / 32.0
        weights[4] = weights[2]
        weights[1] = -3.0 / 32.0 + 3.0 * strength / 16.0
        weights[5] = weights[1]
        weights[0] = 1.0 / 64.0 - strength / 32.0
        weights[6] = weights[0]
        for edge_row in (2, points - 3):
            weights[:, edge_row] = 0.0
            weights[3, edge_row] = 5.0 / 8.0 + 3.0 * strength / 4.0
            weights[2, edge_row] = 0.25 + strength / 2.0
            weights[4, edge_row] = 0.25 + strength / 2.0
            weights[1, edge_row] = -1.0 / 16.0 + strength / 8.0
            weights[5, edge_row] = -1.0 / 16.0 + strength / 8.0
        for edge_row in (1, points - 2):
            weights[:, edge_row] = 0.0
            weights[3, edge_row] = 0.5 + strength
            weights[2, edge_row] = 0.25 + strength / 2.0
            weights[4, edge_row] = 0.25 + strength / 2.0
        for edge_row in (0, points - 1):
            lower[edge_row] = 0.0
            upper[edge_row] = 0.0
            weights[:, edge_row] = 0.0
            weights[3, edge_row] = 1.0
    return (lower, middle, upper, weights)


def inverse_metric(points):
    places = 2.0 * np.arange(points) / (points - 1) - 1.0
    growth = np.exp(STRETCH * places)
    cosh_values = 0.5 * (growth + 1.0 / growth)
    edge_growth = np.exp(STRETCH)
    tanh_value = (edge_growth - 1.0 / edge_growth) / (edge_growth + 1.0 / edge_growth)
    return tanh_value * cosh_values**2 / (0.64 * STRETCH)


def periodic_matrix(points, spacing):
    near_weight, far_weight = slope_weights()
    wave_numbers = np.arange(1, points // 2)
    angles = 2.0 * np.pi * wave_numbers / points
    modified = (2.0 * near_weight * np.sin(angles) + 2.0 * far_weight * np.sin(2.0 * angles)) / (
        1.0 + 2.0 * ALPHA_SLOPE * np.cos(angles)
    )
    phases = np.arange(points)[:, None] * wave_numbers[None, :] % points
    circulant = -2.0 / (points * spacing) * (np.sin(2.0 * np.pi * phases / points) @ modified)
    shifts = (np.arange(points)[:, None] - np.arange(points)[None, :]) % points
    return circulant[shifts].T


@functools.lru_cache(maxsize=None)
def wall_tables(kind, points, rows, pad):
    lower, middle, upper, weights = system_rows(kind, points)
    system = np.diag(middle) + np.diag(lower[1:], -1) + np.diag(upper[:-1], 1)
    inv = np.linalg.inv(system)
    stencil = np.zeros((points, points + 6))
    for row in range(points):
        for offset in range(-3, 4):
            if weights[3 + offset, row] != 0.0:
                assert abs(offset) <= pad and 0 <= row + offset < points
                stencil[row, row + offset + 3] = weights[3 + offset, row]
    scale = inverse_metric(points) if kind == "slope" else np.ones(points)
    blocks = points // rows
    combine = np.zeros((blocks, rows + 2, rows + 2 * pad))
    rise_gain = np.zeros((blocks, rows))
    fall_gain = np.zeros((blocks, rows))
    rise_step = np.zeros(blocks)
    fall_step = np.zeros(blocks)
    for block in range(blocks):
        lo, hi = block * rows, block * rows + rows
        own = slice(lo, hi)
        rise_part = np.zeros(rows)
        fall_part = np.zeros(rows)
        alpha = np.zeros(rows)
        beta = np.zeros(rows)
        if block > 0:
            ref = hi if block < blocks - 1 else lo
            alpha = inv[own, lo - 1] / inv[ref, lo - 1]
            rise_step[block] = inv[ref, lo - 1] / inv[lo, lo - 1]
            fall_part = inv[lo - 1, own]
        if block < blocks - 1:
            ref = lo - 1 if block > 0 else hi - 1
            beta = inv[own, hi] / inv[ref, hi]
            fall_step[block] = inv[ref, hi] / inv[hi - 1, hi]
            rise_part = inv[hi, own]
        local = inv[own, own] - np.outer(alpha, rise_part) - np.outer(beta, fall_part)
        rows_stencil = stencil[own, lo - pad + 3 : hi + pad + 3]
        outside = stencil[own].copy()
        outside[:, lo - pad + 3 : hi + pad + 3] = 0.0
        assert not outside.any()
        combine[block, :rows] = scale[own, None] * (local @ rows_stencil)
        combine[block, rows] = rise_part @ rows_stencil
        combine[block, rows + 1] = fall_part @ rows_stencil
        rise_gain[block] = scale[own] * alpha
        fall_gain[block] = scale[own] * beta
    return combine, rise_gain, fall_gain, rise_step, fall_step


def scan_rounds(blocks):
    rounds = []
    stride = 1
    while stride < blocks:
        radix = min(2, -(-blocks // stride))
        rounds.append((stride, list(range(1, radix))))
        stride *= radix
    return rounds


def scan_coefs(rise_step, fall_step, shift):
    blocks = rise_step.shape[0]
    rise = np.zeros(blocks)
    fall = np.zeros(blocks)
    for block in range(blocks):
        if block - shift >= 0:
            rise[block] = np.prod(rise_step[block - shift + 1 : block + 1])
        if block + shift <= blocks - 1:
            fall[block] = np.prod(fall_step[block : block + shift])
    return rise, fall


class TableBank:
    def __init__(self):
        self.parts = []
        self.width = 0

    def add(self, table):
        table = np.asarray(table, np.float64)
        handle = (self.width, table.shape[1:])
        self.parts.append(table.reshape(table.shape[0], -1))
        self.width += self.parts[-1].shape[1]
        return handle

    def lookup(self, position):
        whole = jnp.asarray(np.concatenate(self.parts, axis=1), jnp.float32)
        self.row = lax.dynamic_index_in_dim(whole, position, 0, keepdims=False)

    def get(self, handle):
        start, shape = handle
        return self.row[start : start + int(np.prod(shape))].reshape(shape)


def plan_wall(bank, kinds_sizes, points, rows, pad):
    tables = [wall_tables(kind, points, rows, pad) for kind, _ in kinds_sizes]
    groups = [
        (bank.add(table[0]), bank.add(table[1]), bank.add(table[2])) for table in tables
    ]
    blocks = points // rows
    rounds = []
    for stride, multiples in scan_rounds(blocks):
        entries = []
        for multiple in multiples:
            shift = stride * multiple
            coefs = [scan_coefs(table[3], table[4], shift) for table in tables]
            rise = np.concatenate(
                [np.repeat(c[0][:, None], n, 1) for c, (_, n) in zip(coefs, kinds_sizes)], 1
            )
            fall = np.concatenate(
                [np.repeat(c[1][:, None], n, 1) for c, (_, n) in zip(coefs, kinds_sizes)], 1
            )
            entries.append((shift, bank.add(rise), bank.add(fall)))
        rounds.append(entries)
    return groups, rounds


def wall_apply(bank, plan, padded_groups, rows, pad):
    count = lax.axis_size("gy")
    groups, rounds = plan

    def taps(padded, combine):
        summed = None
        for tap in range(rows + 2 * pad):
            term = combine[:, tap, None, None] * padded[:, None, tap]
            summed = term if summed is None else summed + term
        return summed

    partials = [
        taps(padded, bank.get(handles[0])[rows:])
        for padded, handles in zip(padded_groups, groups)
    ]
    sizes = [padded.shape[0] for padded in padded_groups]
    rise = jnp.concatenate([part[:, 0] for part in partials], axis=0)
    fall = jnp.concatenate([part[:, 1] for part in partials], axis=0)
    for entries in rounds:
        rise_next, fall_next = rise, fall
        for shift, rise_handle, fall_handle in entries:
            up_pairs = [(i, i + shift) for i in range(count - shift)]
            down_pairs = [(i + shift, i) for i in range(count - shift)]
            from_below = lax.ppermute(rise, "gy", up_pairs)
            from_above = lax.ppermute(fall, "gy", down_pairs)
            rise_next = rise_next + bank.get(rise_handle)[:, None, None] * from_below
            fall_next = fall_next + bank.get(fall_handle)[:, None, None] * from_above
        rise, fall = rise_next, fall_next
    results = []
    first = 0
    for padded, handles, size in zip(padded_groups, groups, sizes):
        local = taps(padded, bank.get(handles[0])[:rows])
        rise_gain = bank.get(handles[1])
        fall_gain = bank.get(handles[2])
        results.append(
            local
            + rise_gain[None, :, None, None] * rise[first : first + size, None]
            + fall_gain[None, :, None, None] * fall[first : first + size, None]
        )
        first += size
    return results


def halo(block, width):
    count = lax.axis_size("gy")
    up_pairs = [(i, i + 1) for i in range(count - 1)]
    down_pairs = [(i + 1, i) for i in range(count - 1)]
    below = lax.ppermute(block[:, block.shape[1] - width :], "gy", up_pairs)
    above = lax.ppermute(block[:, :width], "gy", down_pairs)
    return jnp.concatenate([below, block, above], axis=1)


def stream_slope(fields, stream_matrix):
    flat_rows = fields.reshape(-1, stream_matrix.shape[0])
    return jnp.dot(
        flat_rows, stream_matrix, precision=HIGHEST, preferred_element_type=jnp.float32
    ).reshape(fields.shape)


def span_slope(fields, own_block, other_block):
    other = lax.ppermute(fields, "pa", [(0, 1), (1, 0)])
    return jnp.einsum("fyzx,zw->fywx", fields, own_block, precision=HIGHEST) + jnp.einsum(
        "fyzx,zw->fywx", other, other_block, precision=HIGHEST
    )


def flux_along(direction, momentum, energy, speed, push, gradients):
    divergence = gradients[0][0] + gradients[1][1] + gradients[2][2]
    conduct = VISCOSITY * GAMMA_GAS / ((GAMMA_GAS - 1.0) * PRANDTL)
    rows_out = [momentum[direction]]
    energy_flux = (energy + push) * speed[direction]
    for component in range(3):
        stress = VISCOSITY * (gradients[direction][component] + gradients[component][direction])
        if component == direction:
            stress = stress - 2.0 / 3.0 * VISCOSITY * divergence
            rows_out.append(momentum[component] * speed[direction] + push - stress)
        else:
            rows_out.append(momentum[component] * speed[direction] - stress)
        energy_flux = energy_flux - speed[component] * stress
    energy_flux = energy_flux - conduct * gradients[direction][3]
    rows_out.append(energy_flux)
    return jnp.stack(rows_out)


def per_device(mass_per_volume, mass_flux_vector, total_heat_content):
    rows, span_own, stream_cells = mass_per_volume.shape
    count = lax.axis_size("gy")
    points = rows * count
    position = lax.axis_index("gy")
    span_total = span_own * lax.axis_size("pa")
    stream_matrix = jnp.asarray(periodic_matrix(stream_cells, STREAM_STEP), jnp.float32)
    span_full = periodic_matrix(span_total, SPAN_STEP)
    own_block = jnp.asarray(span_full[:span_own, :span_own], jnp.float32)
    other_block = jnp.asarray(span_full[span_own : 2 * span_own, :span_own], jnp.float32)

    bank = TableBank()
    first_plan = plan_wall(bank, [("slope", 4), ("smooth", 5)], points, rows, 3)
    second_plan = plan_wall(bank, [("slope", 5)], points, rows, 2)
    bank.lookup(position)

    state = jnp.concatenate(
        [mass_per_volume[None], mass_flux_vector, total_heat_content[None]], axis=0
    )
    padded = halo(state, 3)
    global_rows = position * rows - 3 + jnp.arange(rows + 6)
    inside = ((global_rows >= 0) & (global_rows < points))[:, None, None]
    density = jnp.where(inside, padded[0], 1.0)
    speed_pad = padded[1:4] / density[None]
    kinetic = 0.5 * jnp.sum(speed_pad * padded[1:4], axis=0)
    push_pad = (GAMMA_GAS - 1.0) * (padded[4] - kinetic)
    warmth_pad = push_pad / density
    basic_pad = jnp.concatenate([speed_pad, warmth_pad[None]], axis=0)

    wall_grad, smoothed = wall_apply(bank, first_plan, [basic_pad, padded], rows, 3)

    basic = basic_pad[:, 3 : 3 + rows]
    speed = basic[:3]
    push = push_pad[3 : 3 + rows]
    grad_stream = stream_slope(basic, stream_matrix)
    grad_span = span_slope(basic, own_block, other_block)
    gradients = [grad_stream, wall_grad, grad_span]
    momentum = mass_flux_vector
    energy = total_heat_content

    flux_wall = flux_along(1, momentum, energy, speed, push, gradients)
    (wall_term,) = wall_apply(bank, second_plan, [halo(flux_wall, 2)], rows, 2)
    stream_term = stream_slope(
        flux_along(0, momentum, energy, speed, push, gradients), stream_matrix
    )
    span_term = span_slope(
        flux_along(2, momentum, energy, speed, push, gradients), own_block, other_block
    )
    time_rate = -(stream_term + wall_term + span_term)
    own_rows = position * rows + jnp.arange(rows)
    at_wall = ((own_rows == 0) | (own_rows == points - 1))[None, :, None, None]
    held = jnp.where(at_wall, 0.0, time_rate[1:4])
    time_rate = jnp.concatenate([time_rate[:1], held, time_rate[4:]], axis=0)
    return (time_rate, smoothed)


def solution(mesh):
    placed = (P("gy", "pa", None), P(None, "gy", "pa", None), P("gy", "pa", None))
    return jax.shard_map(
        per_device,
        mesh=mesh,
        in_specs=placed,
        out_specs=(P(None, "gy", "pa", None), P(None, "gy", "pa", None)),
        check_vma=False,
    )
```

```python
import functools

import jax
import jax.numpy as jnp
import numpy as np
from jax import lax
from jax.sharding import PartitionSpec as P

GAMMA_GAS = 1.4
PRANDTL = 0.72
VISCOSITY = 0.25
ALPHA_FILTER = 0.499
ALPHA_SLOPE = 0.498
STRETCH = 1.2
STREAM_STEP = 1.0
SPAN_STEP = 0.5
HIGHEST = lax.Precision.HIGHEST


def slope_weights():
    near_weight = (2.0 + ALPHA_SLOPE) / 3.0
    far_weight = (4.0 * ALPHA_SLOPE - 1.0) / 12.0
    return (near_weight, far_weight)


def system_rows(system_kind, points):
    lower = np.zeros(points)
    middle = np.ones(points)
    upper = np.zeros(points)
    weights = np.zeros((7, points))
    if system_kind == "slope":
        near_weight, far_weight = slope_weights()
        lower[:] = ALPHA_SLOPE
        upper[:] = ALPHA_SLOPE
        weights[1] = -far_weight
        weights[2] = -near_weight
        weights[4] = near_weight
        weights[5] = far_weight
        for edge_row in (1, points - 2):
            lower[edge_row] = 0.25
            upper[edge_row] = 0.25
            weights[:, edge_row] = 0.0
            weights[2, edge_row] = -0.75
            weights[4, edge_row] = 0.75
        lower[0] = 0.0
        upper[0] = 2.0
        weights[:, 0] = 0.0
        weights[3, 0] = -2.5
        weights[4, 0] = 2.0
        weights[5, 0] = 0.5
        lower[points - 1] = 2.0
        upper[points - 1] = 0.0
        weights[:, points - 1] = 0.0
        weights[3, points - 1] = 2.5
        weights[2, points - 1] = -2.0
        weights[1, points - 1] = -0.5
    else:
        strength = ALPHA_FILTER
        lower[:] = strength
        upper[:] = strength
        weights[3] = 11.0 / 16.0 + 5.0 * strength / 8.0
        weights[2] = 15.0 / 64.0 + 17.0 * strength / 32.0
        weights[4] = weights[2]
        weights[1] = -3.0 / 32.0 + 3.0 * strength / 16.0
        weights[5] = weights[1]
        weights[0] = 1.0 / 64.0 - strength / 32.0
        weights[6] = weights[0]
        for edge_row in (2, points - 3):
            weights[:, edge_row] = 0.0
            weights[3, edge_row] = 5.0 / 8.0 + 3.0 * strength / 4.0
            weights[2, edge_row] = 0.25 + strength / 2.0
            weights[4, edge_row] = 0.25 + strength / 2.0
            weights[1, edge_row] = -1.0 / 16.0 + strength / 8.0
            weights[5, edge_row] = -1.0 / 16.0 + strength / 8.0
        for edge_row in (1, points - 2):
            weights[:, edge_row] = 0.0
            weights[3, edge_row] = 0.5 + strength
            weights[2, edge_row] = 0.25 + strength / 2.0
            weights[4, edge_row] = 0.25 + strength / 2.0
        for edge_row in (0, points - 1):
            lower[edge_row] = 0.0
            upper[edge_row] = 0.0
            weights[:, edge_row] = 0.0
            weights[3, edge_row] = 1.0
    return (lower, middle, upper, weights)


def inverse_metric(points):
    places = 2.0 * np.arange(points) / (points - 1) - 1.0
    growth = np.exp(STRETCH * places)
    cosh_values = 0.5 * (growth + 1.0 / growth)
    edge_growth = np.exp(STRETCH)
    tanh_value = (edge_growth - 1.0 / edge_growth) / (edge_growth + 1.0 / edge_growth)
    return tanh_value * cosh_values**2 / (0.64 * STRETCH)


def periodic_matrix(points, spacing):
    near_weight, far_weight = slope_weights()
    wave_numbers = np.arange(1, points // 2)
    angles = 2.0 * np.pi * wave_numbers / points
    modified = (2.0 * near_weight * np.sin(angles) + 2.0 * far_weight * np.sin(2.0 * angles)) / (
        1.0 + 2.0 * ALPHA_SLOPE * np.cos(angles)
    )
    phases = np.arange(points)[:, None] * wave_numbers[None, :] % points
    circulant = -2.0 / (points * spacing) * (np.sin(2.0 * np.pi * phases / points) @ modified)
    shifts = (np.arange(points)[:, None] - np.arange(points)[None, :]) % points
    return circulant[shifts].T


@functools.lru_cache(maxsize=None)
def wall_tables(kind, points, rows, pad, extra=0):
    assert extra == 0 or kind == "slope"
    lower, middle, upper, weights = system_rows(kind, points)
    system = np.diag(middle) + np.diag(lower[1:], -1) + np.diag(upper[:-1], 1)
    inv = np.linalg.inv(system)
    stencil = np.zeros((points, points + 6))
    for row in range(points):
        for offset in range(-3, 4):
            if weights[3 + offset, row] != 0.0:
                assert abs(offset) <= pad and 0 <= row + offset < points
                stencil[row, row + offset + 3] = weights[3 + offset, row]
    scale = inverse_metric(points) if kind == "slope" else np.ones(points)
    blocks = points // rows
    outputs = rows + 2 * extra
    combine = np.zeros((blocks, outputs + 2, rows + 2 * pad))
    rise_gain = np.zeros((blocks, outputs))
    fall_gain = np.zeros((blocks, outputs))
    rise_step = np.zeros(blocks)
    fall_step = np.zeros(blocks)
    for block in range(blocks):
        lo, hi = block * rows, block * rows + rows
        own = slice(lo, hi)
        window = slice(lo - pad + 3, hi + pad + 3)
        rise_part = np.zeros(rows)
        fall_part = np.zeros(rows)
        rise_ref = hi if block < blocks - 1 else lo
        fall_ref = lo - 1 if block > 0 else hi - 1
        if block > 0:
            rise_step[block] = inv[rise_ref, lo - 1] / inv[lo, lo - 1]
            fall_part = inv[lo - 1, own]
        if block < blocks - 1:
            fall_step[block] = inv[fall_ref, hi] / inv[hi - 1, hi]
            rise_part = inv[hi, own]
        for out, row in enumerate(range(lo - extra, hi + extra)):
            if row < 0 or row >= points:
                continue
            alpha = beta = 0.0
            if block > 0 or row >= hi:
                column = lo - 1 if lo <= row < hi else min(row, rise_ref) - 1
                alpha = inv[row, column] / inv[rise_ref, column]
            if block < blocks - 1:
                column = hi if row < hi else row + 1
                beta = inv[row, column] / inv[fall_ref, column]
            coef = np.zeros(points + 6)
            coef += (inv[row, own] - alpha * rise_part - beta * fall_part) @ stencil[own]
            if row == lo - 2:
                model = inv[row, row - 1] / inv[lo - 1, row - 1] * inv[lo - 1, lo - 1]
                coef += (inv[row, lo - 1] - model) * stencil[lo - 1]
            if row == hi + 1:
                model = inv[row, row + 1] / inv[hi, row + 1] * inv[hi, hi]
                coef += (inv[row, hi] - model) * stencil[hi]
            outside = coef.copy()
            outside[window] = 0.0
            assert not outside.any()
            combine[block, out] = scale[row] * coef[window]
            rise_gain[block, out] = scale[row] * alpha
            fall_gain[block, out] = scale[row] * beta
        rows_stencil = stencil[own, window]
        combine[block, outputs] = rise_part @ rows_stencil
        combine[block, outputs + 1] = fall_part @ rows_stencil
    return combine, rise_gain, fall_gain, rise_step, fall_step


def scan_rounds(blocks):
    rounds = []
    stride = 1
    while stride < blocks:
        radix = min(2, -(-blocks // stride))
        rounds.append((stride, list(range(1, radix))))
        stride *= radix
    return rounds


def scan_coefs(rise_step, fall_step, shift):
    blocks = rise_step.shape[0]
    rise = np.zeros(blocks)
    fall = np.zeros(blocks)
    for block in range(blocks):
        if block - shift >= 0:
            rise[block] = np.prod(rise_step[block - shift + 1 : block + 1])
        if block + shift <= blocks - 1:
            fall[block] = np.prod(fall_step[block : block + shift])
    return rise, fall


class TableBank:
    def __init__(self):
        self.parts = []
        self.width = 0

    def add(self, table):
        table = np.asarray(table, np.float64)
        handle = (self.width, table.shape[1:])
        self.parts.append(table.reshape(table.shape[0], -1))
        self.width += self.parts[-1].shape[1]
        return handle

    def lookup(self, position):
        whole = jnp.asarray(np.concatenate(self.parts, axis=1), jnp.float32)
        self.row = lax.dynamic_index_in_dim(whole, position, 0, keepdims=False)

    def get(self, handle):
        start, shape = handle
        return self.row[start : start + int(np.prod(shape))].reshape(shape)


def plan_wall(bank, kinds_sizes, points, rows, pad, extras):
    tables = [
        wall_tables(kind, points, rows, pad, extra)
        for (kind, _), extra in zip(kinds_sizes, extras)
    ]
    groups = [
        (bank.add(table[0]), bank.add(table[1]), bank.add(table[2]), table[1].shape[1])
        for table in tables
    ]
    blocks = points // rows
    rounds = []
    for stride, multiples in scan_rounds(blocks):
        entries = []
        for multiple in multiples:
            shift = stride * multiple
            coefs = [scan_coefs(table[3], table[4], shift) for table in tables]
            rise = np.concatenate(
                [np.repeat(c[0][:, None], n, 1) for c, (_, n) in zip(coefs, kinds_sizes)], 1
            )
            fall = np.concatenate(
                [np.repeat(c[1][:, None], n, 1) for c, (_, n) in zip(coefs, kinds_sizes)], 1
            )
            entries.append((shift, bank.add(rise), bank.add(fall)))
        rounds.append(entries)
    return groups, rounds


def wall_apply(bank, plan, padded_groups, rows, pad):
    count = lax.axis_size("gy")
    groups, rounds = plan

    def taps(padded, combine):
        summed = None
        for tap in range(rows + 2 * pad):
            term = combine[:, tap, None, None] * padded[:, None, tap]
            summed = term if summed is None else summed + term
        return summed

    partials = [
        taps(padded, bank.get(handles[0])[handles[3] :])
        for padded, handles in zip(padded_groups, groups)
    ]
    sizes = [padded.shape[0] for padded in padded_groups]
    rise = jnp.concatenate([part[:, 0] for part in partials], axis=0)
    fall = jnp.concatenate([part[:, 1] for part in partials], axis=0)
    for entries in rounds:
        rise_next, fall_next = rise, fall
        for shift, rise_handle, fall_handle in entries:
            up_pairs = [(i, i + shift) for i in range(count - shift)]
            down_pairs = [(i + shift, i) for i in range(count - shift)]
            from_below = lax.ppermute(rise, "gy", up_pairs)
            from_above = lax.ppermute(fall, "gy", down_pairs)
            rise_next = rise_next + bank.get(rise_handle)[:, None, None] * from_below
            fall_next = fall_next + bank.get(fall_handle)[:, None, None] * from_above
        rise, fall = rise_next, fall_next
    results = []
    first = 0
    for padded, handles, size in zip(padded_groups, groups, sizes):
        local = taps(padded, bank.get(handles[0])[: handles[3]])
        rise_gain = bank.get(handles[1])
        fall_gain = bank.get(handles[2])
        results.append(
            local
            + rise_gain[None, :, None, None] * rise[first : first + size, None]
            + fall_gain[None, :, None, None] * fall[first : first + size, None]
        )
        first += size
    return results


def halo(block, width):
    count = lax.axis_size("gy")
    up_pairs = [(i, i + 1) for i in range(count - 1)]
    down_pairs = [(i + 1, i) for i in range(count - 1)]
    below = lax.ppermute(block[:, block.shape[1] - width :], "gy", up_pairs)
    above = lax.ppermute(block[:, :width], "gy", down_pairs)
    return jnp.concatenate([below, block, above], axis=1)


def stream_slope(fields, stream_matrix):
    flat_rows = fields.reshape(-1, stream_matrix.shape[0])
    return jnp.dot(
        flat_rows, stream_matrix, precision=HIGHEST, preferred_element_type=jnp.float32
    ).reshape(fields.shape)


def span_slope(fields, own_block, other_block):
    other = lax.ppermute(fields, "pa", [(0, 1), (1, 0)])
    return jnp.einsum("fyzx,zw->fywx", fields, own_block, precision=HIGHEST) + jnp.einsum(
        "fyzx,zw->fywx", other, other_block, precision=HIGHEST
    )


def flux_along(direction, momentum, energy, speed, push, gradients):
    divergence = gradients[0][0] + gradients[1][1] + gradients[2][2]
    conduct = VISCOSITY * GAMMA_GAS / ((GAMMA_GAS - 1.0) * PRANDTL)
    rows_out = [momentum[direction]]
    energy_flux = (energy + push) * speed[direction]
    for component in range(3):
        stress = VISCOSITY * (gradients[direction][component] + gradients[component][direction])
        if component == direction:
            stress = stress - 2.0 / 3.0 * VISCOSITY * divergence
            rows_out.append(momentum[component] * speed[direction] + push - stress)
        else:
            rows_out.append(momentum[component] * speed[direction] - stress)
        energy_flux = energy_flux - speed[component] * stress
    energy_flux = energy_flux - conduct * gradients[direction][3]
    rows_out.append(energy_flux)
    return jnp.stack(rows_out)


def per_device(mass_per_volume, mass_flux_vector, total_heat_content):
    rows, span_own, stream_cells = mass_per_volume.shape
    count = lax.axis_size("gy")
    points = rows * count
    position = lax.axis_index("gy")
    span_total = span_own * lax.axis_size("pa")
    stream_matrix = jnp.asarray(periodic_matrix(stream_cells, STREAM_STEP), jnp.float32)
    span_full = periodic_matrix(span_total, SPAN_STEP)
    own_block = jnp.asarray(span_full[:span_own, :span_own], jnp.float32)
    other_block = jnp.asarray(span_full[span_own : 2 * span_own, :span_own], jnp.float32)

    bank = TableBank()
    first_plan = plan_wall(bank, [("slope", 4), ("smooth", 5)], points, rows, 3, (2, 0))
    second_plan = plan_wall(bank, [("slope", 5)], points, rows, 2, (0,))
    bank.lookup(position)

    state = jnp.concatenate(
        [mass_per_volume[None], mass_flux_vector, total_heat_content[None]], axis=0
    )
    padded = halo(state, 3)
    global_rows = position * rows - 3 + jnp.arange(rows + 6)
    inside = ((global_rows >= 0) & (global_rows < points))[:, None, None]
    density = jnp.where(inside, padded[0], 1.0)
    speed_pad = padded[1:4] / density[None]
    kinetic = 0.5 * jnp.sum(speed_pad * padded[1:4], axis=0)
    push_pad = (GAMMA_GAS - 1.0) * (padded[4] - kinetic)
    warmth_pad = push_pad / density
    basic_pad = jnp.concatenate([speed_pad, warmth_pad[None]], axis=0)

    wall_grad, smoothed = wall_apply(bank, first_plan, [basic_pad, padded], rows, 3)

    basic = basic_pad[:, 1 : rows + 5]
    speed = basic[:3]
    push = push_pad[1 : rows + 5]
    momentum = padded[1:4, 1 : rows + 5]
    energy = padded[4, 1 : rows + 5]
    grad_stream = stream_slope(basic, stream_matrix)
    grad_span = span_slope(basic, own_block, other_block)
    gradients = [grad_stream, wall_grad, grad_span]
    flux_wall = flux_along(1, momentum, energy, speed, push, gradients)
    (wall_term,) = wall_apply(bank, second_plan, [flux_wall], rows, 2)
    own = slice(2, 2 + rows)
    gradients = [[part[own] for part in grad] for grad in gradients]
    speed, push = speed[:, own], push[own]
    momentum, energy = mass_flux_vector, total_heat_content
    stream_term = stream_slope(
        flux_along(0, momentum, energy, speed, push, gradients), stream_matrix
    )
    span_term = span_slope(
        flux_along(2, momentum, energy, speed, push, gradients), own_block, other_block
    )
    time_rate = -(stream_term + wall_term + span_term)
    own_rows = position * rows + jnp.arange(rows)
    at_wall = ((own_rows == 0) | (own_rows == points - 1))[None, :, None, None]
    held = jnp.where(at_wall, 0.0, time_rate[1:4])
    time_rate = jnp.concatenate([time_rate[:1], held, time_rate[4:]], axis=0)
    return (time_rate, smoothed)


def solution(mesh):
    placed = (P("gy", "pa", None), P(None, "gy", "pa", None), P("gy", "pa", None))
    return jax.shard_map(
        per_device,
        mesh=mesh,
        in_specs=placed,
        out_specs=(P(None, "gy", "pa", None), P(None, "gy", "pa", None)),
        check_vma=False,
    )
```

```python
import functools

import jax
import jax.numpy as jnp
import numpy as np
from jax import lax
from jax.sharding import PartitionSpec as P

GAMMA_GAS = 1.4
PRANDTL = 0.72
VISCOSITY = 0.25
ALPHA_FILTER = 0.499
ALPHA_SLOPE = 0.498
STRETCH = 1.2
STREAM_STEP = 1.0
SPAN_STEP = 0.5
HIGHEST = lax.Precision.HIGHEST


def slope_weights():
    near_weight = (2.0 + ALPHA_SLOPE) / 3.0
    far_weight = (4.0 * ALPHA_SLOPE - 1.0) / 12.0
    return (near_weight, far_weight)


def system_rows(system_kind, points):
    lower = np.zeros(points)
    middle = np.ones(points)
    upper = np.zeros(points)
    weights = np.zeros((7, points))
    if system_kind == "slope":
        near_weight, far_weight = slope_weights()
        lower[:] = ALPHA_SLOPE
        upper[:] = ALPHA_SLOPE
        weights[1] = -far_weight
        weights[2] = -near_weight
        weights[4] = near_weight
        weights[5] = far_weight
        for edge_row in (1, points - 2):
            lower[edge_row] = 0.25
            upper[edge_row] = 0.25
            weights[:, edge_row] = 0.0
            weights[2, edge_row] = -0.75
            weights[4, edge_row] = 0.75
        lower[0] = 0.0
        upper[0] = 2.0
        weights[:, 0] = 0.0
        weights[3, 0] = -2.5
        weights[4, 0] = 2.0
        weights[5, 0] = 0.5
        lower[points - 1] = 2.0
        upper[points - 1] = 0.0
        weights[:, points - 1] = 0.0
        weights[3, points - 1] = 2.5
        weights[2, points - 1] = -2.0
        weights[1, points - 1] = -0.5
    else:
        strength = ALPHA_FILTER
        lower[:] = strength
        upper[:] = strength
        weights[3] = 11.0 / 16.0 + 5.0 * strength / 8.0
        weights[2] = 15.0 / 64.0 + 17.0 * strength / 32.0
        weights[4] = weights[2]
        weights[1] = -3.0 / 32.0 + 3.0 * strength / 16.0
        weights[5] = weights[1]
        weights[0] = 1.0 / 64.0 - strength / 32.0
        weights[6] = weights[0]
        for edge_row in (2, points - 3):
            weights[:, edge_row] = 0.0
            weights[3, edge_row] = 5.0 / 8.0 + 3.0 * strength / 4.0
            weights[2, edge_row] = 0.25 + strength / 2.0
            weights[4, edge_row] = 0.25 + strength / 2.0
            weights[1, edge_row] = -1.0 / 16.0 + strength / 8.0
            weights[5, edge_row] = -1.0 / 16.0 + strength / 8.0
        for edge_row in (1, points - 2):
            weights[:, edge_row] = 0.0
            weights[3, edge_row] = 0.5 + strength
            weights[2, edge_row] = 0.25 + strength / 2.0
            weights[4, edge_row] = 0.25 + strength / 2.0
        for edge_row in (0, points - 1):
            lower[edge_row] = 0.0
            upper[edge_row] = 0.0
            weights[:, edge_row] = 0.0
            weights[3, edge_row] = 1.0
    return (lower, middle, upper, weights)


def inverse_metric(points):
    places = 2.0 * np.arange(points) / (points - 1) - 1.0
    growth = np.exp(STRETCH * places)
    cosh_values = 0.5 * (growth + 1.0 / growth)
    edge_growth = np.exp(STRETCH)
    tanh_value = (edge_growth - 1.0 / edge_growth) / (edge_growth + 1.0 / edge_growth)
    return tanh_value * cosh_values**2 / (0.64 * STRETCH)


def periodic_matrix(points, spacing):
    near_weight, far_weight = slope_weights()
    wave_numbers = np.arange(1, points // 2)
    angles = 2.0 * np.pi * wave_numbers / points
    modified = (2.0 * near_weight * np.sin(angles) + 2.0 * far_weight * np.sin(2.0 * angles)) / (
        1.0 + 2.0 * ALPHA_SLOPE * np.cos(angles)
    )
    phases = np.arange(points)[:, None] * wave_numbers[None, :] % points
    circulant = -2.0 / (points * spacing) * (np.sin(2.0 * np.pi * phases / points) @ modified)
    shifts = (np.arange(points)[:, None] - np.arange(points)[None, :]) % points
    return circulant[shifts].T


@functools.lru_cache(maxsize=None)
def wall_tables(kind, points, rows, pad, extra=0):
    assert extra == 0 or kind == "slope"
    lower, middle, upper, weights = system_rows(kind, points)
    system = np.diag(middle) + np.diag(lower[1:], -1) + np.diag(upper[:-1], 1)
    inv = np.linalg.inv(system)
    stencil = np.zeros((points, points + 6))
    for row in range(points):
        for offset in range(-3, 4):
            if weights[3 + offset, row] != 0.0:
                assert abs(offset) <= pad and 0 <= row + offset < points
                stencil[row, row + offset + 3] = weights[3 + offset, row]
    scale = inverse_metric(points) if kind == "slope" else np.ones(points)
    blocks = points // rows
    outputs = rows + 2 * extra
    combine = np.zeros((blocks, outputs + 2, rows + 2 * pad))
    rise_gain = np.zeros((blocks, outputs))
    fall_gain = np.zeros((blocks, outputs))
    rise_step = np.zeros(blocks)
    fall_step = np.zeros(blocks)
    for block in range(blocks):
        lo, hi = block * rows, block * rows + rows
        own = slice(lo, hi)
        window = slice(lo - pad + 3, hi + pad + 3)
        rise_part = np.zeros(rows)
        fall_part = np.zeros(rows)
        rise_ref = hi if block < blocks - 1 else lo
        fall_ref = lo - 1 if block > 0 else hi - 1
        if block > 0:
            rise_step[block] = inv[rise_ref, lo - 1] / inv[lo, lo - 1]
            fall_part = inv[lo - 1, own]
        if block < blocks - 1:
            fall_step[block] = inv[fall_ref, hi] / inv[hi - 1, hi]
            rise_part = inv[hi, own]
        for out, row in enumerate(range(lo - extra, hi + extra)):
            if row < 0 or row >= points:
                continue
            alpha = beta = 0.0
            if block > 0 or row >= hi:
                column = lo - 1 if lo <= row < hi else min(row, rise_ref) - 1
                alpha = inv[row, column] / inv[rise_ref, column]
            if block < blocks - 1:
                column = hi if row < hi else row + 1
                beta = inv[row, column] / inv[fall_ref, column]
            coef = np.zeros(points + 6)
            coef += (inv[row, own] - alpha * rise_part - beta * fall_part) @ stencil[own]
            if row == lo - 2:
                model = inv[row, row - 1] / inv[lo - 1, row - 1] * inv[lo - 1, lo - 1]
                coef += (inv[row, lo - 1] - model) * stencil[lo - 1]
            if row == hi + 1:
                model = inv[row, row + 1] / inv[hi, row + 1] * inv[hi, hi]
                coef += (inv[row, hi] - model) * stencil[hi]
            outside = coef.copy()
            outside[window] = 0.0
            assert not outside.any()
            combine[block, out] = scale[row] * coef[window]
            rise_gain[block, out] = scale[row] * alpha
            fall_gain[block, out] = scale[row] * beta
        rows_stencil = stencil[own, window]
        combine[block, outputs] = rise_part @ rows_stencil
        combine[block, outputs + 1] = fall_part @ rows_stencil
    rise_rows = combine[:, outputs].copy()
    fall_rows = combine[:, outputs + 1].copy()
    bottom = slice(pad, 2 * pad)
    top = slice(rows, rows + pad)
    below, above = slice(0, pad), slice(rows + pad, rows + 2 * pad)
    for block in range(blocks):
        rise_own = np.zeros(rows + 2 * pad)
        fall_own = np.zeros(rows + 2 * pad)
        rise_own[pad : pad + rows] = rise_rows[block, pad : pad + rows]
        fall_own[pad : pad + rows] = fall_rows[block, pad : pad + rows]
        rise_left = np.zeros(rows + 2 * pad)
        fall_left = np.zeros(rows + 2 * pad)
        if block + 1 < blocks:
            rise_own[top] += rise_rows[block + 1, below] / rise_step[block + 1]
            rise_left[top] -= rise_rows[block + 1, below] / rise_step[block + 1]
            fall_own[top] += fall_step[block] * fall_rows[block + 1, below]
        if block > 0:
            rise_own[bottom] += rise_step[block] * rise_rows[block - 1, above]
            fall_own[bottom] += fall_rows[block - 1, above] / fall_step[block - 1]
            fall_left[bottom] -= fall_rows[block - 1, above] / fall_step[block - 1]
        rise_left[above] += rise_rows[block, above]
        fall_left[below] += fall_rows[block, below]
        combine[block, :outputs] += np.outer(rise_gain[block], rise_left)
        combine[block, :outputs] += np.outer(fall_gain[block], fall_left)
        combine[block, outputs] = rise_own
        combine[block, outputs + 1] = fall_own
    return combine, rise_gain, fall_gain, rise_step, fall_step


def scan_rounds(blocks):
    rounds = []
    stride = 1
    while stride < blocks:
        radix = min(2, -(-blocks // stride))
        rounds.append((stride, list(range(1, radix))))
        stride *= radix
    return rounds


def scan_coefs(rise_step, fall_step, shift):
    blocks = rise_step.shape[0]
    rise = np.zeros(blocks)
    fall = np.zeros(blocks)
    for block in range(blocks):
        if block - shift >= 0:
            rise[block] = np.prod(rise_step[block - shift + 1 : block + 1])
        if block + shift <= blocks - 1:
            fall[block] = np.prod(fall_step[block : block + shift])
    return rise, fall


class TableBank:
    def __init__(self):
        self.parts = []
        self.width = 0

    def add(self, table):
        table = np.asarray(table, np.float64)
        handle = (self.width, table.shape[1:])
        self.parts.append(table.reshape(table.shape[0], -1))
        self.width += self.parts[-1].shape[1]
        return handle

    def lookup(self, position):
        whole = jnp.asarray(np.concatenate(self.parts, axis=1), jnp.float32)
        self.row = lax.dynamic_index_in_dim(whole, position, 0, keepdims=False)

    def get(self, handle):
        start, shape = handle
        return self.row[start : start + int(np.prod(shape))].reshape(shape)


def plan_wall(bank, kinds_sizes, points, rows, pad, extras):
    tables = [
        wall_tables(kind, points, rows, pad, extra)
        for (kind, _), extra in zip(kinds_sizes, extras)
    ]
    groups = [
        (bank.add(table[0]), bank.add(table[1]), bank.add(table[2]), table[1].shape[1])
        for table in tables
    ]
    blocks = points // rows
    rounds = []
    for stride, multiples in scan_rounds(blocks):
        entries = []
        for multiple in multiples:
            shift = stride * multiple
            coefs = [scan_coefs(table[3], table[4], shift) for table in tables]
            rise = np.concatenate(
                [np.repeat(c[0][:, None], n, 1) for c, (_, n) in zip(coefs, kinds_sizes)], 1
            )
            fall = np.concatenate(
                [np.repeat(c[1][:, None], n, 1) for c, (_, n) in zip(coefs, kinds_sizes)], 1
            )
            entries.append((shift, bank.add(rise), bank.add(fall)))
        rounds.append(entries)
    return groups, rounds


def wall_apply(bank, plan, padded_groups, own_groups, rows, pad):
    count = lax.axis_size("gy")
    groups, rounds = plan

    def taps(padded, combine):
        summed = None
        for tap in range(combine.shape[1]):
            term = combine[:, tap, None, None] * padded[:, None, tap]
            summed = term if summed is None else summed + term
        return summed

    partials = [
        taps(own, bank.get(handles[0])[handles[3] :, pad : pad + rows])
        for own, handles in zip(own_groups, groups)
    ]
    sizes = [padded.shape[0] for padded in padded_groups]
    rise = jnp.concatenate([part[:, 0] for part in partials], axis=0)
    fall = jnp.concatenate([part[:, 1] for part in partials], axis=0)
    for entries in rounds:
        rise_next, fall_next = rise, fall
        for shift, rise_handle, fall_handle in entries:
            up_pairs = [(i, i + shift) for i in range(count - shift)]
            down_pairs = [(i + shift, i) for i in range(count - shift)]
            from_below = lax.ppermute(rise, "gy", up_pairs)
            from_above = lax.ppermute(fall, "gy", down_pairs)
            rise_next = rise_next + bank.get(rise_handle)[:, None, None] * from_below
            fall_next = fall_next + bank.get(fall_handle)[:, None, None] * from_above
        rise, fall = rise_next, fall_next
    results = []
    first = 0
    for padded, handles, size in zip(padded_groups, groups, sizes):
        local = taps(padded, bank.get(handles[0])[: handles[3]])
        rise_gain = bank.get(handles[1])
        fall_gain = bank.get(handles[2])
        results.append(
            local
            + rise_gain[None, :, None, None] * rise[first : first + size, None]
            + fall_gain[None, :, None, None] * fall[first : first + size, None]
        )
        first += size
    return results


def halo(block, width):
    count = lax.axis_size("gy")
    up_pairs = [(i, i + 1) for i in range(count - 1)]
    down_pairs = [(i + 1, i) for i in range(count - 1)]
    below = lax.ppermute(block[:, block.shape[1] - width :], "gy", up_pairs)
    above = lax.ppermute(block[:, :width], "gy", down_pairs)
    return jnp.concatenate([below, block, above], axis=1)


def stream_slope(fields, stream_matrix):
    flat_rows = fields.reshape(-1, stream_matrix.shape[0])
    return jnp.dot(
        flat_rows, stream_matrix, precision=HIGHEST, preferred_element_type=jnp.float32
    ).reshape(fields.shape)


def span_slope(fields, own_block, other_block):
    other = lax.ppermute(fields, "pa", [(0, 1), (1, 0)])
    return jnp.einsum("fyzx,zw->fywx", fields, own_block, precision=HIGHEST) + jnp.einsum(
        "fyzx,zw->fywx", other, other_block, precision=HIGHEST
    )


def flux_along(direction, momentum, energy, speed, push, gradients):
    divergence = gradients[0][0] + gradients[1][1] + gradients[2][2]
    conduct = VISCOSITY * GAMMA_GAS / ((GAMMA_GAS - 1.0) * PRANDTL)
    rows_out = [momentum[direction]]
    energy_flux = (energy + push) * speed[direction]
    for component in range(3):
        stress = VISCOSITY * (gradients[direction][component] + gradients[component][direction])
        if component == direction:
            stress = stress - 2.0 / 3.0 * VISCOSITY * divergence
            rows_out.append(momentum[component] * speed[direction] + push - stress)
        else:
            rows_out.append(momentum[component] * speed[direction] - stress)
        energy_flux = energy_flux - speed[component] * stress
    energy_flux = energy_flux - conduct * gradients[direction][3]
    rows_out.append(energy_flux)
    return jnp.stack(rows_out)


def per_device(mass_per_volume, mass_flux_vector, total_heat_content):
    rows, span_own, stream_cells = mass_per_volume.shape
    count = lax.axis_size("gy")
    points = rows * count
    position = lax.axis_index("gy")
    span_total = span_own * lax.axis_size("pa")
    stream_matrix = jnp.asarray(periodic_matrix(stream_cells, STREAM_STEP), jnp.float32)
    span_full = periodic_matrix(span_total, SPAN_STEP)
    own_block = jnp.asarray(span_full[:span_own, :span_own], jnp.float32)
    other_block = jnp.asarray(span_full[span_own : 2 * span_own, :span_own], jnp.float32)

    bank = TableBank()
    first_plan = plan_wall(bank, [("slope", 4), ("smooth", 5)], points, rows, 3, (2, 0))
    second_plan = plan_wall(bank, [("slope", 5)], points, rows, 2, (0,))
    bank.lookup(position)

    state = jnp.concatenate(
        [mass_per_volume[None], mass_flux_vector, total_heat_content[None]], axis=0
    )
    padded = halo(state, 3)
    global_rows = position * rows - 3 + jnp.arange(rows + 6)
    inside = ((global_rows >= 0) & (global_rows < points))[:, None, None]
    density = jnp.where(inside, padded[0], 1.0)
    speed_pad = padded[1:4] / density[None]
    kinetic = 0.5 * jnp.sum(speed_pad * padded[1:4], axis=0)
    push_pad = (GAMMA_GAS - 1.0) * (padded[4] - kinetic)
    warmth_pad = push_pad / density
    basic_pad = jnp.concatenate([speed_pad, warmth_pad[None]], axis=0)

    speed_own = mass_flux_vector / mass_per_volume[None]
    kinetic_own = 0.5 * jnp.sum(speed_own * mass_flux_vector, axis=0)
    push_own = (GAMMA_GAS - 1.0) * (total_heat_content - kinetic_own)
    basic_own = jnp.concatenate([speed_own, (push_own / mass_per_volume)[None]], axis=0)
    wall_grad, smoothed = wall_apply(
        bank, first_plan, [basic_pad, padded], [basic_own, state], rows, 3
    )

    basic = basic_pad[:, 1 : rows + 5]
    speed = basic[:3]
    push = push_pad[1 : rows + 5]
    momentum = padded[1:4, 1 : rows + 5]
    energy = padded[4, 1 : rows + 5]
    grad_stream = stream_slope(basic, stream_matrix)
    grad_span = span_slope(basic, own_block, other_block)
    gradients = [grad_stream, wall_grad, grad_span]
    flux_wall = flux_along(1, momentum, energy, speed, push, gradients)
    (wall_term,) = wall_apply(bank, second_plan, [flux_wall], [flux_wall[:, 2 : 2 + rows]], rows, 2)
    own = slice(2, 2 + rows)
    gradients = [[part[own] for part in grad] for grad in gradients]
    speed, push = speed[:, own], push[own]
    momentum, energy = mass_flux_vector, total_heat_content
    stream_term = stream_slope(
        flux_along(0, momentum, energy, speed, push, gradients), stream_matrix
    )
    span_term = span_slope(
        flux_along(2, momentum, energy, speed, push, gradients), own_block, other_block
    )
    time_rate = -(stream_term + wall_term + span_term)
    own_rows = position * rows + jnp.arange(rows)
    at_wall = ((own_rows == 0) | (own_rows == points - 1))[None, :, None, None]
    held = jnp.where(at_wall, 0.0, time_rate[1:4])
    time_rate = jnp.concatenate([time_rate[:1], held, time_rate[4:]], axis=0)
    return (time_rate, smoothed)


def solution(mesh):
    placed = (P("gy", "pa", None), P(None, "gy", "pa", None), P("gy", "pa", None))
    return jax.shard_map(
        per_device,
        mesh=mesh,
        in_specs=placed,
        out_specs=(P(None, "gy", "pa", None), P(None, "gy", "pa", None)),
        check_vma=False,
    )
```

```python
import functools

import jax
import jax.numpy as jnp
import numpy as np
from jax import lax
from jax.sharding import PartitionSpec as P

GAMMA_GAS = 1.4
PRANDTL = 0.72
VISCOSITY = 0.25
ALPHA_FILTER = 0.499
ALPHA_SLOPE = 0.498
STRETCH = 1.2
STREAM_STEP = 1.0
SPAN_STEP = 0.5
HIGHEST = lax.Precision.HIGHEST


def slope_weights():
    near_weight = (2.0 + ALPHA_SLOPE) / 3.0
    far_weight = (4.0 * ALPHA_SLOPE - 1.0) / 12.0
    return (near_weight, far_weight)


def system_rows(system_kind, points):
    lower = np.zeros(points)
    middle = np.ones(points)
    upper = np.zeros(points)
    weights = np.zeros((7, points))
    if system_kind == "slope":
        near_weight, far_weight = slope_weights()
        lower[:] = ALPHA_SLOPE
        upper[:] = ALPHA_SLOPE
        weights[1] = -far_weight
        weights[2] = -near_weight
        weights[4] = near_weight
        weights[5] = far_weight
        for edge_row in (1, points - 2):
            lower[edge_row] = 0.25
            upper[edge_row] = 0.25
            weights[:, edge_row] = 0.0
            weights[2, edge_row] = -0.75
            weights[4, edge_row] = 0.75
        lower[0] = 0.0
        upper[0] = 2.0
        weights[:, 0] = 0.0
        weights[3, 0] = -2.5
        weights[4, 0] = 2.0
        weights[5, 0] = 0.5
        lower[points - 1] = 2.0
        upper[points - 1] = 0.0
        weights[:, points - 1] = 0.0
        weights[3, points - 1] = 2.5
        weights[2, points - 1] = -2.0
        weights[1, points - 1] = -0.5
    else:
        strength = ALPHA_FILTER
        lower[:] = strength
        upper[:] = strength
        weights[3] = 11.0 / 16.0 + 5.0 * strength / 8.0
        weights[2] = 15.0 / 64.0 + 17.0 * strength / 32.0
        weights[4] = weights[2]
        weights[1] = -3.0 / 32.0 + 3.0 * strength / 16.0
        weights[5] = weights[1]
        weights[0] = 1.0 / 64.0 - strength / 32.0
        weights[6] = weights[0]
        for edge_row in (2, points - 3):
            weights[:, edge_row] = 0.0
            weights[3, edge_row] = 5.0 / 8.0 + 3.0 * strength / 4.0
            weights[2, edge_row] = 0.25 + strength / 2.0
            weights[4, edge_row] = 0.25 + strength / 2.0
            weights[1, edge_row] = -1.0 / 16.0 + strength / 8.0
            weights[5, edge_row] = -1.0 / 16.0 + strength / 8.0
        for edge_row in (1, points - 2):
            weights[:, edge_row] = 0.0
            weights[3, edge_row] = 0.5 + strength
            weights[2, edge_row] = 0.25 + strength / 2.0
            weights[4, edge_row] = 0.25 + strength / 2.0
        for edge_row in (0, points - 1):
            lower[edge_row] = 0.0
            upper[edge_row] = 0.0
            weights[:, edge_row] = 0.0
            weights[3, edge_row] = 1.0
    return (lower, middle, upper, weights)


def inverse_metric(points):
    places = 2.0 * np.arange(points) / (points - 1) - 1.0
    growth = np.exp(STRETCH * places)
    cosh_values = 0.5 * (growth + 1.0 / growth)
    edge_growth = np.exp(STRETCH)
    tanh_value = (edge_growth - 1.0 / edge_growth) / (edge_growth + 1.0 / edge_growth)
    return tanh_value * cosh_values**2 / (0.64 * STRETCH)


def periodic_matrix(points, spacing):
    near_weight, far_weight = slope_weights()
    wave_numbers = np.arange(1, points // 2)
    angles = 2.0 * np.pi * wave_numbers / points
    modified = (2.0 * near_weight * np.sin(angles) + 2.0 * far_weight * np.sin(2.0 * angles)) / (
        1.0 + 2.0 * ALPHA_SLOPE * np.cos(angles)
    )
    phases = np.arange(points)[:, None] * wave_numbers[None, :] % points
    circulant = -2.0 / (points * spacing) * (np.sin(2.0 * np.pi * phases / points) @ modified)
    shifts = (np.arange(points)[:, None] - np.arange(points)[None, :]) % points
    return circulant[shifts].T


@functools.lru_cache(maxsize=None)
def wall_tables(kind, points, rows, pad, extra=0):
    assert extra == 0 or kind == "slope"
    lower, middle, upper, weights = system_rows(kind, points)
    system = np.diag(middle) + np.diag(lower[1:], -1) + np.diag(upper[:-1], 1)
    inv = np.linalg.inv(system)
    stencil = np.zeros((points, points + 6))
    for row in range(points):
        for offset in range(-3, 4):
            if weights[3 + offset, row] != 0.0:
                assert abs(offset) <= pad and 0 <= row + offset < points
                stencil[row, row + offset + 3] = weights[3 + offset, row]
    scale = inverse_metric(points) if kind == "slope" else np.ones(points)
    blocks = points // rows
    outputs = rows + 2 * extra
    combine = np.zeros((blocks, outputs + 2, rows + 2 * pad))
    rise_gain = np.zeros((blocks, outputs))
    fall_gain = np.zeros((blocks, outputs))
    rise_step = np.zeros(blocks)
    fall_step = np.zeros(blocks)
    for block in range(blocks):
        lo, hi = block * rows, block * rows + rows
        own = slice(lo, hi)
        window = slice(lo - pad + 3, hi + pad + 3)
        rise_part = np.zeros(rows)
        fall_part = np.zeros(rows)
        rise_ref = hi if block < blocks - 1 else lo
        fall_ref = lo - 1 if block > 0 else hi - 1
        if block > 0:
            rise_step[block] = inv[rise_ref, lo - 1] / inv[lo, lo - 1]
            fall_part = inv[lo - 1, own]
        if block < blocks - 1:
            fall_step[block] = inv[fall_ref, hi] / inv[hi - 1, hi]
            rise_part = inv[hi, own]
        for out, row in enumerate(range(lo - extra, hi + extra)):
            if row < 0 or row >= points:
                continue
            alpha = beta = 0.0
            if block > 0 or row >= hi:
                column = lo - 1 if lo <= row < hi else min(row, rise_ref) - 1
                alpha = inv[row, column] / inv[rise_ref, column]
            if block < blocks - 1:
                column = hi if row < hi else row + 1
                beta = inv[row, column] / inv[fall_ref, column]
            coef = np.zeros(points + 6)
            coef += (inv[row, own] - alpha * rise_part - beta * fall_part) @ stencil[own]
            if row == lo - 2:
                model = inv[row, row - 1] / inv[lo - 1, row - 1] * inv[lo - 1, lo - 1]
                coef += (inv[row, lo - 1] - model) * stencil[lo - 1]
            if row == hi + 1:
                model = inv[row, row + 1] / inv[hi, row + 1] * inv[hi, hi]
                coef += (inv[row, hi] - model) * stencil[hi]
            outside = coef.copy()
            outside[window] = 0.0
            assert not outside.any()
            combine[block, out] = scale[row] * coef[window]
            rise_gain[block, out] = scale[row] * alpha
            fall_gain[block, out] = scale[row] * beta
        rows_stencil = stencil[own, window]
        combine[block, outputs] = rise_part @ rows_stencil
        combine[block, outputs + 1] = fall_part @ rows_stencil
    rise_rows = combine[:, outputs].copy()
    fall_rows = combine[:, outputs + 1].copy()
    bottom = slice(pad, 2 * pad)
    top = slice(rows, rows + pad)
    below, above = slice(0, pad), slice(rows + pad, rows + 2 * pad)
    for block in range(blocks):
        rise_own = np.zeros(rows + 2 * pad)
        fall_own = np.zeros(rows + 2 * pad)
        rise_own[pad : pad + rows] = rise_rows[block, pad : pad + rows]
        fall_own[pad : pad + rows] = fall_rows[block, pad : pad + rows]
        rise_left = np.zeros(rows + 2 * pad)
        fall_left = np.zeros(rows + 2 * pad)
        if block + 1 < blocks:
            rise_own[top] += rise_rows[block + 1, below] / rise_step[block + 1]
            rise_left[top] -= rise_rows[block + 1, below] / rise_step[block + 1]
            fall_own[top] += fall_step[block] * fall_rows[block + 1, below]
        if block > 0:
            rise_own[bottom] += rise_step[block] * rise_rows[block - 1, above]
            fall_own[bottom] += fall_rows[block - 1, above] / fall_step[block - 1]
            fall_left[bottom] -= fall_rows[block - 1, above] / fall_step[block - 1]
        rise_left[above] += rise_rows[block, above]
        fall_left[below] += fall_rows[block, below]
        combine[block, :outputs] += np.outer(rise_gain[block], rise_left)
        combine[block, :outputs] += np.outer(fall_gain[block], fall_left)
        combine[block, outputs] = rise_own
        combine[block, outputs + 1] = fall_own
    return combine, rise_gain, fall_gain, rise_step, fall_step


def scan_rounds(blocks):
    rounds = []
    stride = 1
    while stride < blocks:
        radix = min(2, -(-blocks // stride))
        rounds.append((stride, list(range(1, radix))))
        stride *= radix
    return rounds


def scan_coefs(rise_step, fall_step, shift):
    blocks = rise_step.shape[0]
    rise = np.zeros(blocks)
    fall = np.zeros(blocks)
    for block in range(blocks):
        if block - shift >= 0:
            rise[block] = np.prod(rise_step[block - shift + 1 : block + 1])
        if block + shift <= blocks - 1:
            fall[block] = np.prod(fall_step[block : block + shift])
    return rise, fall


class TableBank:
    def __init__(self):
        self.parts = []
        self.width = 0

    def add(self, table):
        table = np.asarray(table, np.float64)
        handle = (self.width, table.shape[1:])
        self.parts.append(table.reshape(table.shape[0], -1))
        self.width += self.parts[-1].shape[1]
        return handle

    def lookup(self, position):
        whole = jnp.asarray(np.concatenate(self.parts, axis=1), jnp.float32)
        self.row = lax.dynamic_index_in_dim(whole, position, 0, keepdims=False)

    def get(self, handle):
        start, shape = handle
        return self.row[start : start + int(np.prod(shape))].reshape(shape)


def plan_wall(bank, kinds_sizes, points, rows, pad, extras):
    tables = [
        wall_tables(kind, points, rows, pad, extra)
        for (kind, _), extra in zip(kinds_sizes, extras)
    ]
    groups = [
        (
            bank.add(table[0].transpose(0, 2, 1)),
            bank.add(table[1]),
            bank.add(table[2]),
            table[1].shape[1],
        )
        for table in tables
    ]
    blocks = points // rows
    rounds = []
    for stride, multiples in scan_rounds(blocks):
        entries = []
        for multiple in multiples:
            shift = stride * multiple
            coefs = [scan_coefs(table[3], table[4], shift) for table in tables]
            rise = np.concatenate(
                [np.repeat(c[0][:, None], n, 1) for c, (_, n) in zip(coefs, kinds_sizes)], 1
            )
            fall = np.concatenate(
                [np.repeat(c[1][:, None], n, 1) for c, (_, n) in zip(coefs, kinds_sizes)], 1
            )
            entries.append((shift, bank.add(rise), bank.add(fall)))
        rounds.append(entries)
    return groups, rounds


def wall_apply(bank, plan, padded_groups, own_groups, rows, pad):
    count = lax.axis_size("gy")
    groups, rounds = plan

    def taps(padded, by_tap):
        summed = None
        for tap in range(by_tap.shape[0]):
            term = by_tap[tap][:, None, None] * padded[:, None, tap]
            summed = term if summed is None else summed + term
        return summed

    partials = [
        taps(own, bank.get(handles[0])[pad : pad + rows, handles[3] :])
        for own, handles in zip(own_groups, groups)
    ]
    sizes = [padded.shape[0] for padded in padded_groups]
    rise = jnp.concatenate([part[:, 0] for part in partials], axis=0)
    fall = jnp.concatenate([part[:, 1] for part in partials], axis=0)
    for entries in rounds:
        rise_next, fall_next = rise, fall
        for shift, rise_handle, fall_handle in entries:
            up_pairs = [(i, i + shift) for i in range(count - shift)]
            down_pairs = [(i + shift, i) for i in range(count - shift)]
            from_below = lax.ppermute(rise, "gy", up_pairs)
            from_above = lax.ppermute(fall, "gy", down_pairs)
            rise_next = rise_next + bank.get(rise_handle)[:, None, None] * from_below
            fall_next = fall_next + bank.get(fall_handle)[:, None, None] * from_above
        rise, fall = rise_next, fall_next
    results = []
    first = 0
    for padded, handles, size in zip(padded_groups, groups, sizes):
        local = taps(padded, bank.get(handles[0])[:, : handles[3]])
        rise_gain = bank.get(handles[1])
        fall_gain = bank.get(handles[2])
        results.append(
            local
            + rise_gain[None, :, None, None] * rise[first : first + size, None]
            + fall_gain[None, :, None, None] * fall[first : first + size, None]
        )
        first += size
    return results


def halo(block, width):
    count = lax.axis_size("gy")
    up_pairs = [(i, i + 1) for i in range(count - 1)]
    down_pairs = [(i + 1, i) for i in range(count - 1)]
    below = lax.ppermute(block[:, block.shape[1] - width :], "gy", up_pairs)
    above = lax.ppermute(block[:, :width], "gy", down_pairs)
    return jnp.concatenate([below, block, above], axis=1)


def stream_slope(fields, stream_matrix):
    flat_rows = fields.reshape(-1, stream_matrix.shape[0])
    return jnp.dot(
        flat_rows, stream_matrix, precision=HIGHEST, preferred_element_type=jnp.float32
    ).reshape(fields.shape)


def span_slope(fields, own_block, other_block):
    other = lax.ppermute(fields, "pa", [(0, 1), (1, 0)])
    return jnp.einsum("fyzx,zw->fywx", fields, own_block, precision=HIGHEST) + jnp.einsum(
        "fyzx,zw->fywx", other, other_block, precision=HIGHEST
    )


def flux_along(direction, momentum, energy, speed, push, gradients):
    divergence = gradients[0][0] + gradients[1][1] + gradients[2][2]
    conduct = VISCOSITY * GAMMA_GAS / ((GAMMA_GAS - 1.0) * PRANDTL)
    rows_out = [momentum[direction]]
    energy_flux = (energy + push) * speed[direction]
    for component in range(3):
        stress = VISCOSITY * (gradients[direction][component] + gradients[component][direction])
        if component == direction:
            stress = stress - 2.0 / 3.0 * VISCOSITY * divergence
            rows_out.append(momentum[component] * speed[direction] + push - stress)
        else:
            rows_out.append(momentum[component] * speed[direction] - stress)
        energy_flux = energy_flux - speed[component] * stress
    energy_flux = energy_flux - conduct * gradients[direction][3]
    rows_out.append(energy_flux)
    return jnp.stack(rows_out)


def per_device(mass_per_volume, mass_flux_vector, total_heat_content):
    rows, span_own, stream_cells = mass_per_volume.shape
    count = lax.axis_size("gy")
    points = rows * count
    position = lax.axis_index("gy")
    span_total = span_own * lax.axis_size("pa")
    stream_matrix = jnp.asarray(periodic_matrix(stream_cells, STREAM_STEP), jnp.float32)
    span_full = periodic_matrix(span_total, SPAN_STEP)
    own_block = jnp.asarray(span_full[:span_own, :span_own], jnp.float32)
    other_block = jnp.asarray(span_full[span_own : 2 * span_own, :span_own], jnp.float32)

    bank = TableBank()
    first_plan = plan_wall(bank, [("slope", 4), ("smooth", 5)], points, rows, 3, (2, 0))
    second_plan = plan_wall(bank, [("slope", 5)], points, rows, 2, (0,))
    bank.lookup(position)

    state = jnp.concatenate(
        [mass_per_volume[None], mass_flux_vector, total_heat_content[None]], axis=0
    )
    padded = halo(state, 3)
    global_rows = position * rows - 3 + jnp.arange(rows + 6)
    inside = ((global_rows >= 0) & (global_rows < points))[:, None, None]
    density = jnp.where(inside, padded[0], 1.0)
    speed_pad = padded[1:4] / density[None]
    kinetic = 0.5 * jnp.sum(speed_pad * padded[1:4], axis=0)
    push_pad = (GAMMA_GAS - 1.0) * (padded[4] - kinetic)
    warmth_pad = push_pad / density
    basic_pad = jnp.concatenate([speed_pad, warmth_pad[None]], axis=0)

    speed_own = mass_flux_vector / mass_per_volume[None]
    kinetic_own = 0.5 * jnp.sum(speed_own * mass_flux_vector, axis=0)
    push_own = (GAMMA_GAS - 1.0) * (total_heat_content - kinetic_own)
    basic_own = jnp.concatenate([speed_own, (push_own / mass_per_volume)[None]], axis=0)
    wall_grad, smoothed = wall_apply(
        bank, first_plan, [basic_pad, padded], [basic_own, state], rows, 3
    )

    basic = basic_pad[:, 1 : rows + 5]
    speed = basic[:3]
    push = push_pad[1 : rows + 5]
    momentum = padded[1:4, 1 : rows + 5]
    energy = padded[4, 1 : rows + 5]
    grad_stream = stream_slope(basic, stream_matrix)
    grad_span = span_slope(basic, own_block, other_block)
    gradients = [grad_stream, wall_grad, grad_span]
    flux_wall = flux_along(1, momentum, energy, speed, push, gradients)
    (wall_term,) = wall_apply(bank, second_plan, [flux_wall], [flux_wall[:, 2 : 2 + rows]], rows, 2)
    own = slice(2, 2 + rows)
    gradients = [[part[own] for part in grad] for grad in gradients]
    speed, push = speed[:, own], push[own]
    momentum, energy = mass_flux_vector, total_heat_content
    stream_term = stream_slope(
        flux_along(0, momentum, energy, speed, push, gradients), stream_matrix
    )
    span_term = span_slope(
        flux_along(2, momentum, energy, speed, push, gradients), own_block, other_block
    )
    time_rate = -(stream_term + wall_term + span_term)
    own_rows = position * rows + jnp.arange(rows)
    at_wall = ((own_rows == 0) | (own_rows == points - 1))[None, :, None, None]
    held = jnp.where(at_wall, 0.0, time_rate[1:4])
    time_rate = jnp.concatenate([time_rate[:1], held, time_rate[4:]], axis=0)
    return (time_rate, smoothed)


def solution(mesh):
    placed = (P("gy", "pa", None), P(None, "gy", "pa", None), P("gy", "pa", None))
    return jax.shard_map(
        per_device,
        mesh=mesh,
        in_specs=placed,
        out_specs=(P(None, "gy", "pa", None), P(None, "gy", "pa", None)),
        check_vma=False,
    )
```

```python
import functools

import jax
import jax.numpy as jnp
import numpy as np
from jax import lax
from jax.sharding import PartitionSpec as P

GAMMA_GAS = 1.4
PRANDTL = 0.72
VISCOSITY = 0.25
ALPHA_FILTER = 0.499
ALPHA_SLOPE = 0.498
STRETCH = 1.2
STREAM_STEP = 1.0
SPAN_STEP = 0.5
HIGHEST = lax.Precision.HIGHEST


def slope_weights():
    near_weight = (2.0 + ALPHA_SLOPE) / 3.0
    far_weight = (4.0 * ALPHA_SLOPE - 1.0) / 12.0
    return (near_weight, far_weight)


def system_rows(system_kind, points):
    lower = np.zeros(points)
    middle = np.ones(points)
    upper = np.zeros(points)
    weights = np.zeros((7, points))
    if system_kind == "slope":
        near_weight, far_weight = slope_weights()
        lower[:] = ALPHA_SLOPE
        upper[:] = ALPHA_SLOPE
        weights[1] = -far_weight
        weights[2] = -near_weight
        weights[4] = near_weight
        weights[5] = far_weight
        for edge_row in (1, points - 2):
            lower[edge_row] = 0.25
            upper[edge_row] = 0.25
            weights[:, edge_row] = 0.0
            weights[2, edge_row] = -0.75
            weights[4, edge_row] = 0.75
        lower[0] = 0.0
        upper[0] = 2.0
        weights[:, 0] = 0.0
        weights[3, 0] = -2.5
        weights[4, 0] = 2.0
        weights[5, 0] = 0.5
        lower[points - 1] = 2.0
        upper[points - 1] = 0.0
        weights[:, points - 1] = 0.0
        weights[3, points - 1] = 2.5
        weights[2, points - 1] = -2.0
        weights[1, points - 1] = -0.5
    else:
        strength = ALPHA_FILTER
        lower[:] = strength
        upper[:] = strength
        weights[3] = 11.0 / 16.0 + 5.0 * strength / 8.0
        weights[2] = 15.0 / 64.0 + 17.0 * strength / 32.0
        weights[4] = weights[2]
        weights[1] = -3.0 / 32.0 + 3.0 * strength / 16.0
        weights[5] = weights[1]
        weights[0] = 1.0 / 64.0 - strength / 32.0
        weights[6] = weights[0]
        for edge_row in (2, points - 3):
            weights[:, edge_row] = 0.0
            weights[3, edge_row] = 5.0 / 8.0 + 3.0 * strength / 4.0
            weights[2, edge_row] = 0.25 + strength / 2.0
            weights[4, edge_row] = 0.25 + strength / 2.0
            weights[1, edge_row] = -1.0 / 16.0 + strength / 8.0
            weights[5, edge_row] = -1.0 / 16.0 + strength / 8.0
        for edge_row in (1, points - 2):
            weights[:, edge_row] = 0.0
            weights[3, edge_row] = 0.5 + strength
            weights[2, edge_row] = 0.25 + strength / 2.0
            weights[4, edge_row] = 0.25 + strength / 2.0
        for edge_row in (0, points - 1):
            lower[edge_row] = 0.0
            upper[edge_row] = 0.0
            weights[:, edge_row] = 0.0
            weights[3, edge_row] = 1.0
    return (lower, middle, upper, weights)


def inverse_metric(points):
    places = 2.0 * np.arange(points) / (points - 1) - 1.0
    growth = np.exp(STRETCH * places)
    cosh_values = 0.5 * (growth + 1.0 / growth)
    edge_growth = np.exp(STRETCH)
    tanh_value = (edge_growth - 1.0 / edge_growth) / (edge_growth + 1.0 / edge_growth)
    return tanh_value * cosh_values**2 / (0.64 * STRETCH)


def periodic_matrix(points, spacing):
    near_weight, far_weight = slope_weights()
    wave_numbers = np.arange(1, points // 2)
    angles = 2.0 * np.pi * wave_numbers / points
    modified = (2.0 * near_weight * np.sin(angles) + 2.0 * far_weight * np.sin(2.0 * angles)) / (
        1.0 + 2.0 * ALPHA_SLOPE * np.cos(angles)
    )
    phases = np.arange(points)[:, None] * wave_numbers[None, :] % points
    circulant = -2.0 / (points * spacing) * (np.sin(2.0 * np.pi * phases / points) @ modified)
    shifts = (np.arange(points)[:, None] - np.arange(points)[None, :]) % points
    return circulant[shifts].T


@functools.lru_cache(maxsize=None)
def wall_tables(kind, points, rows, pad, extra=0):
    assert extra == 0 or kind == "slope"
    lower, middle, upper, weights = system_rows(kind, points)
    system = np.diag(middle) + np.diag(lower[1:], -1) + np.diag(upper[:-1], 1)
    inv = np.linalg.inv(system)
    stencil = np.zeros((points, points + 6))
    for row in range(points):
        for offset in range(-3, 4):
            if weights[3 + offset, row] != 0.0:
                assert abs(offset) <= pad and 0 <= row + offset < points
                stencil[row, row + offset + 3] = weights[3 + offset, row]
    scale = inverse_metric(points) if kind == "slope" else np.ones(points)
    blocks = points // rows
    outputs = rows + 2 * extra
    combine = np.zeros((blocks, outputs + 2, rows + 2 * pad))
    rise_gain = np.zeros((blocks, outputs))
    fall_gain = np.zeros((blocks, outputs))
    rise_step = np.zeros(blocks)
    fall_step = np.zeros(blocks)
    for block in range(blocks):
        lo, hi = block * rows, block * rows + rows
        own = slice(lo, hi)
        window = slice(lo - pad + 3, hi + pad + 3)
        rise_part = np.zeros(rows)
        fall_part = np.zeros(rows)
        rise_ref = hi if block < blocks - 1 else lo
        fall_ref = lo - 1 if block > 0 else hi - 1
        if block > 0:
            rise_step[block] = inv[rise_ref, lo - 1] / inv[lo, lo - 1]
            fall_part = inv[lo - 1, own]
        if block < blocks - 1:
            fall_step[block] = inv[fall_ref, hi] / inv[hi - 1, hi]
            rise_part = inv[hi, own]
        for out, row in enumerate(range(lo - extra, hi + extra)):
            if row < 0 or row >= points:
                continue
            alpha = beta = 0.0
            if block > 0 or row >= hi:
                column = lo - 1 if lo <= row < hi else min(row, rise_ref) - 1
                alpha = inv[row, column] / inv[rise_ref, column]
            if block < blocks - 1:
                column = hi if row < hi else row + 1
                beta = inv[row, column] / inv[fall_ref, column]
            coef = np.zeros(points + 6)
            coef += (inv[row, own] - alpha * rise_part - beta * fall_part) @ stencil[own]
            if row == lo - 2:
                model = inv[row, row - 1] / inv[lo - 1, row - 1] * inv[lo - 1, lo - 1]
                coef += (inv[row, lo - 1] - model) * stencil[lo - 1]
            if row == hi + 1:
                model = inv[row, row + 1] / inv[hi, row + 1] * inv[hi, hi]
                coef += (inv[row, hi] - model) * stencil[hi]
            outside = coef.copy()
            outside[window] = 0.0
            assert not outside.any()
            combine[block, out] = scale[row] * coef[window]
            rise_gain[block, out] = scale[row] * alpha
            fall_gain[block, out] = scale[row] * beta
        rows_stencil = stencil[own, window]
        combine[block, outputs] = rise_part @ rows_stencil
        combine[block, outputs + 1] = fall_part @ rows_stencil
    return combine, rise_gain, fall_gain, rise_step, fall_step


def scan_rounds(blocks):
    rounds = []
    stride = 1
    while stride < blocks:
        radix = min(2, -(-blocks // stride))
        rounds.append((stride, list(range(1, radix))))
        stride *= radix
    return rounds


def scan_coefs(rise_step, fall_step, shift):
    blocks = rise_step.shape[0]
    rise = np.zeros(blocks)
    fall = np.zeros(blocks)
    for block in range(blocks):
        if block - shift >= 0:
            rise[block] = np.prod(rise_step[block - shift + 1 : block + 1])
        if block + shift <= blocks - 1:
            fall[block] = np.prod(fall_step[block : block + shift])
    return rise, fall


class TableBank:
    def __init__(self):
        self.parts = []
        self.width = 0

    def add(self, table):
        table = np.asarray(table, np.float64)
        handle = (self.width, table.shape[1:])
        self.parts.append(table.reshape(table.shape[0], -1))
        self.width += self.parts[-1].shape[1]
        return handle

    def lookup(self, position):
        whole = jnp.asarray(np.concatenate(self.parts, axis=1), jnp.float32)
        self.row = lax.dynamic_index_in_dim(whole, position, 0, keepdims=False)

    def get(self, handle):
        start, shape = handle
        return self.row[start : start + int(np.prod(shape))].reshape(shape)


def plan_wall(bank, kinds_sizes, points, rows, pad, extras):
    tables = [
        wall_tables(kind, points, rows, pad, extra)
        for (kind, _), extra in zip(kinds_sizes, extras)
    ]
    groups = [
        (
            bank.add(table[0].transpose(0, 2, 1)),
            bank.add(table[1]),
            bank.add(table[2]),
            table[1].shape[1],
        )
        for table in tables
    ]
    blocks = points // rows
    rounds = []
    for stride, multiples in scan_rounds(blocks):
        entries = []
        for multiple in multiples:
            shift = stride * multiple
            coefs = [scan_coefs(table[3], table[4], shift) for table in tables]
            rise = np.concatenate(
                [np.repeat(c[0][:, None], n, 1) for c, (_, n) in zip(coefs, kinds_sizes)], 1
            )
            fall = np.concatenate(
                [np.repeat(c[1][:, None], n, 1) for c, (_, n) in zip(coefs, kinds_sizes)], 1
            )
            entries.append((shift, bank.add(rise), bank.add(fall)))
        rounds.append(entries)
    return groups, rounds


def wall_apply(bank, plan, padded_groups, rows, pad):
    count = lax.axis_size("gy")
    groups, rounds = plan

    def taps(padded, by_tap):
        summed = None
        for tap in range(by_tap.shape[0]):
            term = by_tap[tap][:, None, None] * padded[:, None, tap]
            summed = term if summed is None else summed + term
        return summed

    partials = [
        taps(padded, bank.get(handles[0])[:, handles[3] :])
        for padded, handles in zip(padded_groups, groups)
    ]
    sizes = [padded.shape[0] for padded in padded_groups]
    rise = jnp.concatenate([part[:, 0] for part in partials], axis=0)
    fall = jnp.concatenate([part[:, 1] for part in partials], axis=0)
    for entries in rounds:
        rise_next, fall_next = rise, fall
        for shift, rise_handle, fall_handle in entries:
            up_pairs = [(i, i + shift) for i in range(count - shift)]
            down_pairs = [(i + shift, i) for i in range(count - shift)]
            from_below = lax.ppermute(rise, "gy", up_pairs)
            from_above = lax.ppermute(fall, "gy", down_pairs)
            rise_next = rise_next + bank.get(rise_handle)[:, None, None] * from_below
            fall_next = fall_next + bank.get(fall_handle)[:, None, None] * from_above
        rise, fall = rise_next, fall_next
    results = []
    first = 0
    for padded, handles, size in zip(padded_groups, groups, sizes):
        local = taps(padded, bank.get(handles[0])[:, : handles[3]])
        rise_gain = bank.get(handles[1])
        fall_gain = bank.get(handles[2])
        results.append(
            local
            + rise_gain[None, :, None, None] * rise[first : first + size, None]
            + fall_gain[None, :, None, None] * fall[first : first + size, None]
        )
        first += size
    return results


def halo(block, width):
    count = lax.axis_size("gy")
    up_pairs = [(i, i + 1) for i in range(count - 1)]
    down_pairs = [(i + 1, i) for i in range(count - 1)]
    below = lax.ppermute(block[:, block.shape[1] - width :], "gy", up_pairs)
    above = lax.ppermute(block[:, :width], "gy", down_pairs)
    return jnp.concatenate([below, block, above], axis=1)


def stream_slope(fields, stream_matrix):
    flat_rows = fields.reshape(-1, stream_matrix.shape[0])
    return jnp.dot(
        flat_rows, stream_matrix, precision=HIGHEST, preferred_element_type=jnp.float32
    ).reshape(fields.shape)


def span_slope(fields, own_block, other_block):
    other = lax.ppermute(fields, "pa", [(0, 1), (1, 0)])
    return jnp.einsum("fyzx,zw->fywx", fields, own_block, precision=HIGHEST) + jnp.einsum(
        "fyzx,zw->fywx", other, other_block, precision=HIGHEST
    )


def flux_along(direction, momentum, energy, speed, push, gradients):
    divergence = gradients[0][0] + gradients[1][1] + gradients[2][2]
    conduct = VISCOSITY * GAMMA_GAS / ((GAMMA_GAS - 1.0) * PRANDTL)
    rows_out = [momentum[direction]]
    energy_flux = (energy + push) * speed[direction]
    for component in range(3):
        stress = VISCOSITY * (gradients[direction][component] + gradients[component][direction])
        if component == direction:
            stress = stress - 2.0 / 3.0 * VISCOSITY * divergence
            rows_out.append(momentum[component] * speed[direction] + push - stress)
        else:
            rows_out.append(momentum[component] * speed[direction] - stress)
        energy_flux = energy_flux - speed[component] * stress
    energy_flux = energy_flux - conduct * gradients[direction][3]
    rows_out.append(energy_flux)
    return jnp.stack(rows_out)


def per_device(mass_per_volume, mass_flux_vector, total_heat_content):
    rows, span_own, stream_cells = mass_per_volume.shape
    count = lax.axis_size("gy")
    points = rows * count
    position = lax.axis_index("gy")
    span_total = span_own * lax.axis_size("pa")
    stream_matrix = jnp.asarray(periodic_matrix(stream_cells, STREAM_STEP), jnp.float32)
    span_full = periodic_matrix(span_total, SPAN_STEP)
    own_block = jnp.asarray(span_full[:span_own, :span_own], jnp.float32)
    other_block = jnp.asarray(span_full[span_own : 2 * span_own, :span_own], jnp.float32)

    bank = TableBank()
    first_plan = plan_wall(bank, [("slope", 4), ("smooth", 5)], points, rows, 3, (2, 0))
    second_plan = plan_wall(bank, [("slope", 5)], points, rows, 2, (0,))
    bank.lookup(position)

    state = jnp.concatenate(
        [mass_per_volume[None], mass_flux_vector, total_heat_content[None]], axis=0
    )
    padded = halo(state, 3)
    global_rows = position * rows - 3 + jnp.arange(rows + 6)
    inside = ((global_rows >= 0) & (global_rows < points))[:, None, None]
    density = jnp.where(inside, padded[0], 1.0)
    speed_pad = padded[1:4] / density[None]
    kinetic = 0.5 * jnp.sum(speed_pad * padded[1:4], axis=0)
    push_pad = (GAMMA_GAS - 1.0) * (padded[4] - kinetic)
    warmth_pad = push_pad / density
    basic_pad = jnp.concatenate([speed_pad, warmth_pad[None]], axis=0)

    wall_grad, smoothed = wall_apply(bank, first_plan, [basic_pad, padded], rows, 3)

    basic = basic_pad[:, 1 : rows + 5]
    speed = basic[:3]
    push = push_pad[1 : rows + 5]
    momentum = padded[1:4, 1 : rows + 5]
    energy = padded[4, 1 : rows + 5]
    grad_stream = stream_slope(basic, stream_matrix)
    grad_span = span_slope(basic, own_block, other_block)
    gradients = [grad_stream, wall_grad, grad_span]
    flux_wall = flux_along(1, momentum, energy, speed, push, gradients)
    (wall_term,) = wall_apply(bank, second_plan, [flux_wall], rows, 2)
    own = slice(2, 2 + rows)
    gradients = [[part[own] for part in grad] for grad in gradients]
    speed, push = speed[:, own], push[own]
    momentum, energy = mass_flux_vector, total_heat_content
    stream_term = stream_slope(
        flux_along(0, momentum, energy, speed, push, gradients), stream_matrix
    )
    span_term = span_slope(
        flux_along(2, momentum, energy, speed, push, gradients), own_block, other_block
    )
    time_rate = -(stream_term + wall_term + span_term)
    own_rows = position * rows + jnp.arange(rows)
    at_wall = ((own_rows == 0) | (own_rows == points - 1))[None, :, None, None]
    held = jnp.where(at_wall, 0.0, time_rate[1:4])
    time_rate = jnp.concatenate([time_rate[:1], held, time_rate[4:]], axis=0)
    return (time_rate, smoothed)


def solution(mesh):
    placed = (P("gy", "pa", None), P(None, "gy", "pa", None), P("gy", "pa", None))
    return jax.shard_map(
        per_device,
        mesh=mesh,
        in_specs=placed,
        out_specs=(P(None, "gy", "pa", None), P(None, "gy", "pa", None)),
        check_vma=False,
    )
```

```python
import functools

import jax
import jax.numpy as jnp
import numpy as np
from jax import lax
from jax.sharding import PartitionSpec as P

GAMMA_GAS = 1.4
PRANDTL = 0.72
VISCOSITY = 0.25
ALPHA_FILTER = 0.499
ALPHA_SLOPE = 0.498
STRETCH = 1.2
STREAM_STEP = 1.0
SPAN_STEP = 0.5
HIGHEST = lax.Precision.HIGHEST
LEVEL_AXES = ("gx", "gm", "gz")
WALL_AXES = ("gz", "gm", "gx")


def slope_weights():
    near_weight = (2.0 + ALPHA_SLOPE) / 3.0
    far_weight = (4.0 * ALPHA_SLOPE - 1.0) / 12.0
    return (near_weight, far_weight)


def system_rows(system_kind, points):
    lower = np.zeros(points)
    middle = np.ones(points)
    upper = np.zeros(points)
    weights = np.zeros((7, points))
    if system_kind == "slope":
        near_weight, far_weight = slope_weights()
        lower[:] = ALPHA_SLOPE
        upper[:] = ALPHA_SLOPE
        weights[1] = -far_weight
        weights[2] = -near_weight
        weights[4] = near_weight
        weights[5] = far_weight
        for edge_row in (1, points - 2):
            lower[edge_row] = 0.25
            upper[edge_row] = 0.25
            weights[:, edge_row] = 0.0
            weights[2, edge_row] = -0.75
            weights[4, edge_row] = 0.75
        lower[0] = 0.0
        upper[0] = 2.0
        weights[:, 0] = 0.0
        weights[3, 0] = -2.5
        weights[4, 0] = 2.0
        weights[5, 0] = 0.5
        lower[points - 1] = 2.0
        upper[points - 1] = 0.0
        weights[:, points - 1] = 0.0
        weights[3, points - 1] = 2.5
        weights[2, points - 1] = -2.0
        weights[1, points - 1] = -0.5
    else:
        strength = ALPHA_FILTER
        lower[:] = strength
        upper[:] = strength
        weights[3] = 11.0 / 16.0 + 5.0 * strength / 8.0
        weights[2] = 15.0 / 64.0 + 17.0 * strength / 32.0
        weights[4] = weights[2]
        weights[1] = -3.0 / 32.0 + 3.0 * strength / 16.0
        weights[5] = weights[1]
        weights[0] = 1.0 / 64.0 - strength / 32.0
        weights[6] = weights[0]
        for edge_row in (2, points - 3):
            weights[:, edge_row] = 0.0
            weights[3, edge_row] = 5.0 / 8.0 + 3.0 * strength / 4.0
            weights[2, edge_row] = 0.25 + strength / 2.0
            weights[4, edge_row] = 0.25 + strength / 2.0
            weights[1, edge_row] = -1.0 / 16.0 + strength / 8.0
            weights[5, edge_row] = -1.0 / 16.0 + strength / 8.0
        for edge_row in (1, points - 2):
            weights[:, edge_row] = 0.0
            weights[3, edge_row] = 0.5 + strength
            weights[2, edge_row] = 0.25 + strength / 2.0
            weights[4, edge_row] = 0.25 + strength / 2.0
        for edge_row in (0, points - 1):
            lower[edge_row] = 0.0
            upper[edge_row] = 0.0
            weights[:, edge_row] = 0.0
            weights[3, edge_row] = 1.0
    return (lower, middle, upper, weights)


def inverse_metric(points):
    places = 2.0 * np.arange(points) / (points - 1) - 1.0
    growth = np.exp(STRETCH * places)
    cosh_values = 0.5 * (growth + 1.0 / growth)
    edge_growth = np.exp(STRETCH)
    tanh_value = (edge_growth - 1.0 / edge_growth) / (edge_growth + 1.0 / edge_growth)
    return tanh_value * cosh_values**2 / (0.64 * STRETCH)


def periodic_matrix(points, spacing):
    near_weight, far_weight = slope_weights()
    wave_numbers = np.arange(1, points // 2)
    angles = 2.0 * np.pi * wave_numbers / points
    modified = (2.0 * near_weight * np.sin(angles) + 2.0 * far_weight * np.sin(2.0 * angles)) / (
        1.0 + 2.0 * ALPHA_SLOPE * np.cos(angles)
    )
    phases = np.arange(points)[:, None] * wave_numbers[None, :] % points
    circulant = -2.0 / (points * spacing) * (np.sin(2.0 * np.pi * phases / points) @ modified)
    shifts = (np.arange(points)[:, None] - np.arange(points)[None, :]) % points
    return circulant[shifts].T


@functools.lru_cache(maxsize=None)
def wall_tables(kind, points, rows, pad, extra=0):
    assert extra == 0 or kind == "slope"
    lower, middle, upper, weights = system_rows(kind, points)
    system = np.diag(middle) + np.diag(lower[1:], -1) + np.diag(upper[:-1], 1)
    inv = np.linalg.inv(system)
    stencil = np.zeros((points, points + 6))
    for row in range(points):
        for offset in range(-3, 4):
            if weights[3 + offset, row] != 0.0:
                assert abs(offset) <= pad and 0 <= row + offset < points
                stencil[row, row + offset + 3] = weights[3 + offset, row]
    scale = inverse_metric(points) if kind == "slope" else np.ones(points)
    blocks = points // rows
    outputs = rows + 2 * extra
    combine = np.zeros((blocks, outputs + 2, rows + 2 * pad))
    rise_gain = np.zeros((blocks, outputs))
    fall_gain = np.zeros((blocks, outputs))
    rise_step = np.zeros(blocks)
    fall_step = np.zeros(blocks)
    for block in range(blocks):
        lo, hi = block * rows, block * rows + rows
        own = slice(lo, hi)
        window = slice(lo - pad + 3, hi + pad + 3)
        rise_part = np.zeros(rows)
        fall_part = np.zeros(rows)
        rise_ref = hi if block < blocks - 1 else lo
        fall_ref = lo - 1 if block > 0 else hi - 1
        if block > 0:
            rise_step[block] = inv[rise_ref, lo - 1] / inv[lo, lo - 1]
            fall_part = inv[lo - 1, own]
        if block < blocks - 1:
            fall_step[block] = inv[fall_ref, hi] / inv[hi - 1, hi]
            rise_part = inv[hi, own]
        for out, row in enumerate(range(lo - extra, hi + extra)):
            if row < 0 or row >= points:
                continue
            alpha = beta = 0.0
            if block > 0 or row >= hi:
                column = lo - 1 if lo <= row < hi else min(row, rise_ref) - 1
                alpha = inv[row, column] / inv[rise_ref, column]
            if block < blocks - 1:
                column = hi if row < hi else row + 1
                beta = inv[row, column] / inv[fall_ref, column]
            coef = np.zeros(points + 6)
            coef += (inv[row, own] - alpha * rise_part - beta * fall_part) @ stencil[own]
            if row == lo - 2:
                model = inv[row, row - 1] / inv[lo - 1, row - 1] * inv[lo - 1, lo - 1]
                coef += (inv[row, lo - 1] - model) * stencil[lo - 1]
            if row == hi + 1:
                model = inv[row, row + 1] / inv[hi, row + 1] * inv[hi, hi]
                coef += (inv[row, hi] - model) * stencil[hi]
            outside = coef.copy()
            outside[window] = 0.0
            assert not outside.any()
            combine[block, out] = scale[row] * coef[window]
            rise_gain[block, out] = scale[row] * alpha
            fall_gain[block, out] = scale[row] * beta
        rows_stencil = stencil[own, window]
        combine[block, outputs] = rise_part @ rows_stencil
        combine[block, outputs + 1] = fall_part @ rows_stencil
    return combine, rise_gain, fall_gain, rise_step, fall_step


def scan_rounds(blocks):
    rounds = []
    stride = 1
    while stride < blocks:
        radix = min(2, -(-blocks // stride))
        rounds.append((stride, list(range(1, radix))))
        stride *= radix
    return rounds[::-1]


def scan_coefs(rise_step, fall_step, shift):
    blocks = rise_step.shape[0]
    rise = np.zeros(blocks)
    fall = np.zeros(blocks)
    for block in range(blocks):
        if block - shift >= 0:
            rise[block] = np.prod(rise_step[block - shift + 1 : block + 1])
        if block + shift <= blocks - 1:
            fall[block] = np.prod(fall_step[block : block + shift])
    return rise, fall


def level_tables(rise_step, fall_step, sizes):
    blocks = rise_step.shape[0]

    def rise_weight(source, target):
        return np.prod(rise_step[source + 1 : target + 1]) if source <= target else 0.0

    def fall_weight(source, target):
        return np.prod(fall_step[target:source]) if source >= target else 0.0

    levels = []
    stride = 1
    for level, size in enumerate(sizes):
        span = stride * size
        rise_own = np.zeros((blocks, size))
        rise_total = np.zeros((blocks, size))
        fall_own = np.zeros((blocks, size))
        fall_total = np.zeros((blocks, size))
        for block in range(blocks):
            base = block // span * span
            mine = block // stride % size
            last, first = base + span - 1, base
            for member in range(size):
                group_first = base + member * stride
                group_last = group_first + stride - 1
                if level == 0 or member < mine:
                    rise_own[block, member] = rise_weight(group_last, block)
                if level == 0 or member > mine:
                    fall_own[block, member] = fall_weight(group_first, block)
                rise_total[block, member] = rise_weight(group_last, last)
                fall_total[block, member] = fall_weight(group_first, first)
        levels.append((rise_own, rise_total, fall_own, fall_total))
        stride = span
    return levels


class TableBank:
    def __init__(self):
        self.parts = []
        self.width = 0

    def add(self, table):
        table = np.asarray(table, np.float64)
        handle = (self.width, table.shape[1:])
        self.parts.append(table.reshape(table.shape[0], -1))
        self.width += self.parts[-1].shape[1]
        return handle

    def lookup(self, position):
        whole = jnp.asarray(np.concatenate(self.parts, axis=1), jnp.float32)
        self.row = lax.dynamic_index_in_dim(whole, position, 0, keepdims=False)

    def get(self, handle):
        start, shape = handle
        return self.row[start : start + int(np.prod(shape))].reshape(shape)


def plan_wall(bank, kinds_sizes, points, rows, pad, extras, sizes):
    tables = [
        wall_tables(kind, points, rows, pad, extra)
        for (kind, _), extra in zip(kinds_sizes, extras)
    ]
    groups = [
        (
            bank.add(table[0].transpose(0, 2, 1)),
            bank.add(table[1]),
            bank.add(table[2]),
            table[1].shape[1],
        )
        for table in tables
    ]
    blocks = points // rows
    rounds = []
    for stride, multiples in scan_rounds(blocks):
        entries = []
        for multiple in multiples:
            shift = stride * multiple
            coefs = [scan_coefs(table[3], table[4], shift) for table in tables]
            rise = np.concatenate(
                [np.repeat(c[0][:, None], n, 1) for c, (_, n) in zip(coefs, kinds_sizes)], 1
            )
            fall = np.concatenate(
                [np.repeat(c[1][:, None], n, 1) for c, (_, n) in zip(coefs, kinds_sizes)], 1
            )
            entries.append((shift, bank.add(rise), bank.add(fall)))
        rounds.append(entries)
    return groups, rounds, sizes


def plan_gathered(bank, kind, fields, points, rows, pad, sizes):
    table = wall_tables(kind, points, rows, pad)
    handles = (
        bank.add(table[0].transpose(0, 2, 1)),
        bank.add(table[1]),
        bank.add(table[2]),
        table[1].shape[1],
    )
    levels = [
        [bank.add(np.repeat(part[:, :, None], fields, 2)) for part in level]
        for level in level_tables(table[3], table[4], sizes)
    ]
    return handles, levels


def taps(padded, by_tap):
    summed = None
    for tap in range(by_tap.shape[0]):
        term = by_tap[tap][:, None, None] * padded[:, None, tap]
        summed = term if summed is None else summed + term
    return summed


def gathered_apply(bank, plan, padded):
    handles, levels = plan
    outputs = handles[3]
    partial = taps(padded, bank.get(handles[0])[:, outputs:])
    rise_total, fall_total = partial[:, 0], partial[:, 1]
    rise = fall = None
    for axis, level in zip(LEVEL_AXES, levels):
        gathered = lax.all_gather(jnp.stack([rise_total, fall_total]), axis)
        weights = [bank.get(handle)[:, :, None, None] for handle in level]
        rise_part = jnp.sum(weights[0] * gathered[:, 0], axis=0)
        fall_part = jnp.sum(weights[2] * gathered[:, 1], axis=0)
        rise = rise_part if rise is None else rise + rise_part
        fall = fall_part if fall is None else fall + fall_part
        rise_total = jnp.sum(weights[1] * gathered[:, 0], axis=0)
        fall_total = jnp.sum(weights[3] * gathered[:, 1], axis=0)
    local = taps(padded, bank.get(handles[0])[:, :outputs])
    return (
        local
        + bank.get(handles[1])[None, :, None, None] * rise[:, None]
        + bank.get(handles[2])[None, :, None, None] * fall[:, None]
    )


def wall_apply(bank, plan, padded_groups, rows, pad):
    count = int(np.prod(plan[2]))
    groups, rounds, _ = plan

    partials = [
        taps(padded, bank.get(handles[0])[:, handles[3] :])
        for padded, handles in zip(padded_groups, groups)
    ]
    sizes = [padded.shape[0] for padded in padded_groups]
    rise = jnp.concatenate([part[:, 0] for part in partials], axis=0)
    fall = jnp.concatenate([part[:, 1] for part in partials], axis=0)
    for entries in rounds:
        rise_next, fall_next = rise, fall
        for shift, rise_handle, fall_handle in entries:
            up_pairs = [(i, i + shift) for i in range(count - shift)]
            down_pairs = [(i + shift, i) for i in range(count - shift)]
            from_below = lax.ppermute(rise, WALL_AXES, up_pairs)
            from_above = lax.ppermute(fall, WALL_AXES, down_pairs)
            rise_next = rise_next + bank.get(rise_handle)[:, None, None] * from_below
            fall_next = fall_next + bank.get(fall_handle)[:, None, None] * from_above
        rise, fall = rise_next, fall_next
    results = []
    first = 0
    for padded, handles, size in zip(padded_groups, groups, sizes):
        local = taps(padded, bank.get(handles[0])[:, : handles[3]])
        rise_gain = bank.get(handles[1])
        fall_gain = bank.get(handles[2])
        results.append(
            local
            + rise_gain[None, :, None, None] * rise[first : first + size, None]
            + fall_gain[None, :, None, None] * fall[first : first + size, None]
        )
        first += size
    return results


def halo(block, width, count):
    up_pairs = [(i, i + 1) for i in range(count - 1)]
    down_pairs = [(i + 1, i) for i in range(count - 1)]
    below = lax.ppermute(block[:, block.shape[1] - width :], WALL_AXES, up_pairs)
    above = lax.ppermute(block[:, :width], WALL_AXES, down_pairs)
    return jnp.concatenate([below, block, above], axis=1)


def stream_slope(fields, stream_matrix):
    flat_rows = fields.reshape(-1, stream_matrix.shape[0])
    return jnp.dot(
        flat_rows, stream_matrix, precision=HIGHEST, preferred_element_type=jnp.float32
    ).reshape(fields.shape)


def span_slope(fields, own_block, other_block):
    other = lax.ppermute(fields, "pa", [(0, 1), (1, 0)])
    return jnp.einsum("fyzx,zw->fywx", fields, own_block, precision=HIGHEST) + jnp.einsum(
        "fyzx,zw->fywx", other, other_block, precision=HIGHEST
    )


def flux_along(direction, momentum, energy, speed, push, gradients):
    divergence = gradients[0][0] + gradients[1][1] + gradients[2][2]
    conduct = VISCOSITY * GAMMA_GAS / ((GAMMA_GAS - 1.0) * PRANDTL)
    rows_out = [momentum[direction]]
    energy_flux = (energy + push) * speed[direction]
    for component in range(3):
        stress = VISCOSITY * (gradients[direction][component] + gradients[component][direction])
        if component == direction:
            stress = stress - 2.0 / 3.0 * VISCOSITY * divergence
            rows_out.append(momentum[component] * speed[direction] + push - stress)
        else:
            rows_out.append(momentum[component] * speed[direction] - stress)
        energy_flux = energy_flux - speed[component] * stress
    energy_flux = energy_flux - conduct * gradients[direction][3]
    rows_out.append(energy_flux)
    return jnp.stack(rows_out)


def per_device(level_sizes, mass_per_volume, mass_flux_vector, total_heat_content):
    rows, span_own, stream_cells = mass_per_volume.shape
    count = int(np.prod(level_sizes))
    points = rows * count
    position = lax.axis_index(WALL_AXES)
    span_total = span_own * lax.axis_size("pa")
    stream_matrix = jnp.asarray(periodic_matrix(stream_cells, STREAM_STEP), jnp.float32)
    span_full = periodic_matrix(span_total, SPAN_STEP)
    own_block = jnp.asarray(span_full[:span_own, :span_own], jnp.float32)
    other_block = jnp.asarray(span_full[span_own : 2 * span_own, :span_own], jnp.float32)

    bank = TableBank()
    first_plan = plan_wall(bank, [("slope", 4)], points, rows, 3, (2,), level_sizes)
    smooth_plan = plan_gathered(bank, "smooth", 5, points, rows, 3, level_sizes)
    second_plan = plan_wall(bank, [("slope", 5)], points, rows, 2, (0,), level_sizes)
    bank.lookup(position)

    state = jnp.concatenate(
        [mass_per_volume[None], mass_flux_vector, total_heat_content[None]], axis=0
    )
    padded = halo(state, 3, count)
    global_rows = position * rows - 3 + jnp.arange(rows + 6)
    inside = ((global_rows >= 0) & (global_rows < points))[:, None, None]
    density = jnp.where(inside, padded[0], 1.0)
    speed_pad = padded[1:4] / density[None]
    kinetic = 0.5 * jnp.sum(speed_pad * padded[1:4], axis=0)
    push_pad = (GAMMA_GAS - 1.0) * (padded[4] - kinetic)
    warmth_pad = push_pad / density
    basic_pad = jnp.concatenate([speed_pad, warmth_pad[None]], axis=0)

    smoothed = gathered_apply(bank, smooth_plan, padded)
    (wall_grad,) = wall_apply(bank, first_plan, [basic_pad], rows, 3)

    basic = basic_pad[:, 1 : rows + 5]
    speed = basic[:3]
    push = push_pad[1 : rows + 5]
    momentum = padded[1:4, 1 : rows + 5]
    energy = padded[4, 1 : rows + 5]
    grad_stream = stream_slope(basic, stream_matrix)
    grad_span = span_slope(basic, own_block, other_block)
    gradients = [grad_stream, wall_grad, grad_span]
    flux_wall = flux_along(1, momentum, energy, speed, push, gradients)
    (wall_term,) = wall_apply(bank, second_plan, [flux_wall], rows, 2)
    own = slice(2, 2 + rows)
    gradients = [[part[own] for part in grad] for grad in gradients]
    speed, push = speed[:, own], push[own]
    momentum, energy = mass_flux_vector, total_heat_content
    stream_term = stream_slope(
        flux_along(0, momentum, energy, speed, push, gradients), stream_matrix
    )
    span_term = span_slope(
        flux_along(2, momentum, energy, speed, push, gradients), own_block, other_block
    )
    time_rate = -(stream_term + wall_term + span_term)
    own_rows = position * rows + jnp.arange(rows)
    at_wall = ((own_rows == 0) | (own_rows == points - 1))[None, :, None, None]
    held = jnp.where(at_wall, 0.0, time_rate[1:4])
    time_rate = jnp.concatenate([time_rate[:1], held, time_rate[4:]], axis=0)
    return (time_rate, smoothed)


def solution(mesh):
    rows_devices = mesh.shape["gy"]
    fast = int(np.gcd(rows_devices, 4))
    middle = int(np.gcd(rows_devices // fast, 4))
    slow = rows_devices // fast // middle
    split = jax.sharding.Mesh(
        mesh.devices.reshape(slow, middle, fast, mesh.shape["pa"]), WALL_AXES + ("pa",)
    )
    placed = (
        P(WALL_AXES, "pa", None),
        P(None, WALL_AXES, "pa", None),
        P(WALL_AXES, "pa", None),
    )
    return jax.shard_map(
        functools.partial(per_device, (fast, middle, slow)),
        mesh=split,
        in_specs=placed,
        out_specs=(P(None, WALL_AXES, "pa", None), P(None, WALL_AXES, "pa", None)),
        check_vma=False,
    )
```

```python
import functools

import jax
import jax.numpy as jnp
import numpy as np
from jax import lax
from jax.sharding import PartitionSpec as P

GAMMA_GAS = 1.4
PRANDTL = 0.72
VISCOSITY = 0.25
ALPHA_FILTER = 0.499
ALPHA_SLOPE = 0.498
STRETCH = 1.2
STREAM_STEP = 1.0
SPAN_STEP = 0.5
HIGHEST = lax.Precision.HIGHEST


def slope_weights():
    near_weight = (2.0 + ALPHA_SLOPE) / 3.0
    far_weight = (4.0 * ALPHA_SLOPE - 1.0) / 12.0
    return (near_weight, far_weight)


def system_rows(system_kind, points):
    lower = np.zeros(points)
    middle = np.ones(points)
    upper = np.zeros(points)
    weights = np.zeros((7, points))
    if system_kind == "slope":
        near_weight, far_weight = slope_weights()
        lower[:] = ALPHA_SLOPE
        upper[:] = ALPHA_SLOPE
        weights[1] = -far_weight
        weights[2] = -near_weight
        weights[4] = near_weight
        weights[5] = far_weight
        for edge_row in (1, points - 2):
            lower[edge_row] = 0.25
            upper[edge_row] = 0.25
            weights[:, edge_row] = 0.0
            weights[2, edge_row] = -0.75
            weights[4, edge_row] = 0.75
        lower[0] = 0.0
        upper[0] = 2.0
        weights[:, 0] = 0.0
        weights[3, 0] = -2.5
        weights[4, 0] = 2.0
        weights[5, 0] = 0.5
        lower[points - 1] = 2.0
        upper[points - 1] = 0.0
        weights[:, points - 1] = 0.0
        weights[3, points - 1] = 2.5
        weights[2, points - 1] = -2.0
        weights[1, points - 1] = -0.5
    else:
        strength = ALPHA_FILTER
        lower[:] = strength
        upper[:] = strength
        weights[3] = 11.0 / 16.0 + 5.0 * strength / 8.0
        weights[2] = 15.0 / 64.0 + 17.0 * strength / 32.0
        weights[4] = weights[2]
        weights[1] = -3.0 / 32.0 + 3.0 * strength / 16.0
        weights[5] = weights[1]
        weights[0] = 1.0 / 64.0 - strength / 32.0
        weights[6] = weights[0]
        for edge_row in (2, points - 3):
            weights[:, edge_row] = 0.0
            weights[3, edge_row] = 5.0 / 8.0 + 3.0 * strength / 4.0
            weights[2, edge_row] = 0.25 + strength / 2.0
            weights[4, edge_row] = 0.25 + strength / 2.0
            weights[1, edge_row] = -1.0 / 16.0 + strength / 8.0
            weights[5, edge_row] = -1.0 / 16.0 + strength / 8.0
        for edge_row in (1, points - 2):
            weights[:, edge_row] = 0.0
            weights[3, edge_row] = 0.5 + strength
            weights[2, edge_row] = 0.25 + strength / 2.0
            weights[4, edge_row] = 0.25 + strength / 2.0
        for edge_row in (0, points - 1):
            lower[edge_row] = 0.0
            upper[edge_row] = 0.0
            weights[:, edge_row] = 0.0
            weights[3, edge_row] = 1.0
    return (lower, middle, upper, weights)


def inverse_metric(points):
    places = 2.0 * np.arange(points) / (points - 1) - 1.0
    growth = np.exp(STRETCH * places)
    cosh_values = 0.5 * (growth + 1.0 / growth)
    edge_growth = np.exp(STRETCH)
    tanh_value = (edge_growth - 1.0 / edge_growth) / (edge_growth + 1.0 / edge_growth)
    return tanh_value * cosh_values**2 / (0.64 * STRETCH)


def periodic_matrix(points, spacing):
    near_weight, far_weight = slope_weights()
    wave_numbers = np.arange(1, points // 2)
    angles = 2.0 * np.pi * wave_numbers / points
    modified = (2.0 * near_weight * np.sin(angles) + 2.0 * far_weight * np.sin(2.0 * angles)) / (
        1.0 + 2.0 * ALPHA_SLOPE * np.cos(angles)
    )
    phases = np.arange(points)[:, None] * wave_numbers[None, :] % points
    circulant = -2.0 / (points * spacing) * (np.sin(2.0 * np.pi * phases / points) @ modified)
    shifts = (np.arange(points)[:, None] - np.arange(points)[None, :]) % points
    return circulant[shifts].T


@functools.lru_cache(maxsize=None)
def wall_tables(kind, points, rows, pad, extra=0):
    assert extra == 0 or kind == "slope"
    lower, middle, upper, weights = system_rows(kind, points)
    system = np.diag(middle) + np.diag(lower[1:], -1) + np.diag(upper[:-1], 1)
    inv = np.linalg.inv(system)
    stencil = np.zeros((points, points + 6))
    for row in range(points):
        for offset in range(-3, 4):
            if weights[3 + offset, row] != 0.0:
                assert abs(offset) <= pad and 0 <= row + offset < points
                stencil[row, row + offset + 3] = weights[3 + offset, row]
    scale = inverse_metric(points) if kind == "slope" else np.ones(points)
    blocks = points // rows
    outputs = rows + 2 * extra
    combine = np.zeros((blocks, outputs + 2, rows + 2 * pad))
    rise_gain = np.zeros((blocks, outputs))
    fall_gain = np.zeros((blocks, outputs))
    rise_step = np.zeros(blocks)
    fall_step = np.zeros(blocks)
    for block in range(blocks):
        lo, hi = block * rows, block * rows + rows
        own = slice(lo, hi)
        window = slice(lo - pad + 3, hi + pad + 3)
        rise_part = np.zeros(rows)
        fall_part = np.zeros(rows)
        rise_ref = hi if block < blocks - 1 else lo
        fall_ref = lo - 1 if block > 0 else hi - 1
        if block > 0:
            rise_step[block] = inv[rise_ref, lo - 1] / inv[lo, lo - 1]
            fall_part = inv[lo - 1, own]
        if block < blocks - 1:
            fall_step[block] = inv[fall_ref, hi] / inv[hi - 1, hi]
            rise_part = inv[hi, own]
        for out, row in enumerate(range(lo - extra, hi + extra)):
            if row < 0 or row >= points:
                continue
            alpha = beta = 0.0
            if block > 0 or row >= hi:
                column = lo - 1 if lo <= row < hi else min(row, rise_ref) - 1
                alpha = inv[row, column] / inv[rise_ref, column]
            if block < blocks - 1:
                column = hi if row < hi else row + 1
                beta = inv[row, column] / inv[fall_ref, column]
            coef = np.zeros(points + 6)
            coef += (inv[row, own] - alpha * rise_part - beta * fall_part) @ stencil[own]
            if row == lo - 2:
                model = inv[row, row - 1] / inv[lo - 1, row - 1] * inv[lo - 1, lo - 1]
                coef += (inv[row, lo - 1] - model) * stencil[lo - 1]
            if row == hi + 1:
                model = inv[row, row + 1] / inv[hi, row + 1] * inv[hi, hi]
                coef += (inv[row, hi] - model) * stencil[hi]
            outside = coef.copy()
            outside[window] = 0.0
            assert not outside.any()
            combine[block, out] = scale[row] * coef[window]
            rise_gain[block, out] = scale[row] * alpha
            fall_gain[block, out] = scale[row] * beta
        rows_stencil = stencil[own, window]
        combine[block, outputs] = rise_part @ rows_stencil
        combine[block, outputs + 1] = fall_part @ rows_stencil
    return combine, rise_gain, fall_gain, rise_step, fall_step


def scan_rounds(blocks):
    rounds = []
    stride = 1
    while stride < blocks:
        radix = min(2, -(-blocks // stride))
        rounds.append((stride, list(range(1, radix))))
        stride *= radix
    return rounds[::-1]


def scan_coefs(rise_step, fall_step, shift):
    blocks = rise_step.shape[0]
    rise = np.zeros(blocks)
    fall = np.zeros(blocks)
    for block in range(blocks):
        if block - shift >= 0:
            rise[block] = np.prod(rise_step[block - shift + 1 : block + 1])
        if block + shift <= blocks - 1:
            fall[block] = np.prod(fall_step[block : block + shift])
    return rise, fall


class TableBank:
    def __init__(self):
        self.parts = []
        self.width = 0

    def add(self, table):
        table = np.asarray(table, np.float64)
        handle = (self.width, table.shape[1:])
        self.parts.append(table.reshape(table.shape[0], -1))
        self.width += self.parts[-1].shape[1]
        return handle

    def lookup(self, position):
        whole = jnp.asarray(np.concatenate(self.parts, axis=1), jnp.float32)
        self.row = lax.dynamic_index_in_dim(whole, position, 0, keepdims=False)

    def get(self, handle):
        start, shape = handle
        return self.row[start : start + int(np.prod(shape))].reshape(shape)


def plan_wall(bank, kinds_sizes, points, rows, pad, extras):
    tables = [
        wall_tables(kind, points, rows, pad, extra)
        for (kind, _), extra in zip(kinds_sizes, extras)
    ]
    groups = [
        (
            bank.add(table[0].transpose(0, 2, 1)),
            bank.add(table[1]),
            bank.add(table[2]),
            table[1].shape[1],
        )
        for table in tables
    ]
    blocks = points // rows
    rounds = []
    for stride, multiples in scan_rounds(blocks):
        entries = []
        for multiple in multiples:
            shift = stride * multiple
            coefs = [scan_coefs(table[3], table[4], shift) for table in tables]
            rise = np.concatenate(
                [np.repeat(c[0][:, None], n, 1) for c, (_, n) in zip(coefs, kinds_sizes)], 1
            )
            fall = np.concatenate(
                [np.repeat(c[1][:, None], n, 1) for c, (_, n) in zip(coefs, kinds_sizes)], 1
            )
            entries.append((shift, bank.add(rise), bank.add(fall)))
        rounds.append(entries)
    return groups, rounds


def wall_apply(bank, plan, padded_groups, rows, pad):
    count = lax.axis_size("gy")
    groups, rounds = plan

    def taps(padded, by_tap):
        summed = None
        for tap in range(by_tap.shape[0]):
            term = by_tap[tap][:, None, None] * padded[:, None, tap]
            summed = term if summed is None else summed + term
        return summed

    partials = [
        taps(padded, bank.get(handles[0])[:, handles[3] :])
        for padded, handles in zip(padded_groups, groups)
    ]
    sizes = [padded.shape[0] for padded in padded_groups]
    rise = jnp.concatenate([part[:, 0] for part in partials], axis=0)
    fall = jnp.concatenate([part[:, 1] for part in partials], axis=0)
    for entries in rounds:
        rise_next, fall_next = rise, fall
        for shift, rise_handle, fall_handle in entries:
            up_pairs = [(i, i + shift) for i in range(count - shift)]
            down_pairs = [(i + shift, i) for i in range(count - shift)]
            from_below = lax.ppermute(rise, "gy", up_pairs)
            from_above = lax.ppermute(fall, "gy", down_pairs)
            rise_next = rise_next + bank.get(rise_handle)[:, None, None] * from_below
            fall_next = fall_next + bank.get(fall_handle)[:, None, None] * from_above
        rise, fall = rise_next, fall_next
    results = []
    first = 0
    for padded, handles, size in zip(padded_groups, groups, sizes):
        local = taps(padded, bank.get(handles[0])[:, : handles[3]])
        rise_gain = bank.get(handles[1])
        fall_gain = bank.get(handles[2])
        results.append(
            local
            + rise_gain[None, :, None, None] * rise[first : first + size, None]
            + fall_gain[None, :, None, None] * fall[first : first + size, None]
        )
        first += size
    return results


def halo(block, width):
    count = lax.axis_size("gy")
    up_pairs = [(i, i + 1) for i in range(count - 1)]
    down_pairs = [(i + 1, i) for i in range(count - 1)]
    below = lax.ppermute(block[:, block.shape[1] - width :], "gy", up_pairs)
    above = lax.ppermute(block[:, :width], "gy", down_pairs)
    return jnp.concatenate([below, block, above], axis=1)


def stream_slope(fields, stream_matrix):
    flat_rows = fields.reshape(-1, stream_matrix.shape[0])
    return jnp.dot(
        flat_rows, stream_matrix, precision=HIGHEST, preferred_element_type=jnp.float32
    ).reshape(fields.shape)


def span_slope(fields, own_block, other_block):
    other = lax.ppermute(fields, "pa", [(0, 1), (1, 0)])
    return jnp.einsum("fyzx,zw->fywx", fields, own_block, precision=HIGHEST) + jnp.einsum(
        "fyzx,zw->fywx", other, other_block, precision=HIGHEST
    )


def flux_along(direction, momentum, energy, speed, push, gradients):
    divergence = gradients[0][0] + gradients[1][1] + gradients[2][2]
    conduct = VISCOSITY * GAMMA_GAS / ((GAMMA_GAS - 1.0) * PRANDTL)
    rows_out = [momentum[direction]]
    energy_flux = (energy + push) * speed[direction]
    for component in range(3):
        stress = VISCOSITY * (gradients[direction][component] + gradients[component][direction])
        if component == direction:
            stress = stress - 2.0 / 3.0 * VISCOSITY * divergence
            rows_out.append(momentum[component] * speed[direction] + push - stress)
        else:
            rows_out.append(momentum[component] * speed[direction] - stress)
        energy_flux = energy_flux - speed[component] * stress
    energy_flux = energy_flux - conduct * gradients[direction][3]
    rows_out.append(energy_flux)
    return jnp.stack(rows_out)


def per_device(mass_per_volume, mass_flux_vector, total_heat_content):
    rows, span_own, stream_cells = mass_per_volume.shape
    count = lax.axis_size("gy")
    points = rows * count
    position = lax.axis_index("gy")
    span_total = span_own * lax.axis_size("pa")
    stream_matrix = jnp.asarray(periodic_matrix(stream_cells, STREAM_STEP), jnp.float32)
    span_full = periodic_matrix(span_total, SPAN_STEP)
    own_block = jnp.asarray(span_full[:span_own, :span_own], jnp.float32)
    other_block = jnp.asarray(span_full[span_own : 2 * span_own, :span_own], jnp.float32)

    bank = TableBank()
    first_plan = plan_wall(bank, [("slope", 4), ("smooth", 5)], points, rows, 3, (2, 0))
    second_plan = plan_wall(bank, [("slope", 5)], points, rows, 2, (0,))
    bank.lookup(position)

    state = jnp.concatenate(
        [mass_per_volume[None], mass_flux_vector, total_heat_content[None]], axis=0
    )
    padded = halo(state, 3)
    global_rows = position * rows - 3 + jnp.arange(rows + 6)
    inside = ((global_rows >= 0) & (global_rows < points))[:, None, None]
    density = jnp.where(inside, padded[0], 1.0)
    speed_pad = padded[1:4] / density[None]
    kinetic = 0.5 * jnp.sum(speed_pad * padded[1:4], axis=0)
    push_pad = (GAMMA_GAS - 1.0) * (padded[4] - kinetic)
    warmth_pad = push_pad / density
    basic_pad = jnp.concatenate([speed_pad, warmth_pad[None]], axis=0)

    wall_grad, smoothed = wall_apply(bank, first_plan, [basic_pad, padded], rows, 3)

    basic = basic_pad[:, 1 : rows + 5]
    speed = basic[:3]
    push = push_pad[1 : rows + 5]
    momentum = padded[1:4, 1 : rows + 5]
    energy = padded[4, 1 : rows + 5]
    grad_stream = stream_slope(basic, stream_matrix)
    grad_span = span_slope(basic, own_block, other_block)
    gradients = [grad_stream, wall_grad, grad_span]
    flux_wall = flux_along(1, momentum, energy, speed, push, gradients)
    (wall_term,) = wall_apply(bank, second_plan, [flux_wall], rows, 2)
    own = slice(2, 2 + rows)
    gradients = [[part[own] for part in grad] for grad in gradients]
    speed, push = speed[:, own], push[own]
    momentum, energy = mass_flux_vector, total_heat_content
    stream_term = stream_slope(
        flux_along(0, momentum, energy, speed, push, gradients), stream_matrix
    )
    span_term = span_slope(
        flux_along(2, momentum, energy, speed, push, gradients), own_block, other_block
    )
    time_rate = -(stream_term + wall_term + span_term)
    own_rows = position * rows + jnp.arange(rows)
    at_wall = ((own_rows == 0) | (own_rows == points - 1))[None, :, None, None]
    held = jnp.where(at_wall, 0.0, time_rate[1:4])
    time_rate = jnp.concatenate([time_rate[:1], held, time_rate[4:]], axis=0)
    return (time_rate, smoothed)


def solution(mesh):
    placed = (P("gy", "pa", None), P(None, "gy", "pa", None), P("gy", "pa", None))
    return jax.shard_map(
        per_device,
        mesh=mesh,
        in_specs=placed,
        out_specs=(P(None, "gy", "pa", None), P(None, "gy", "pa", None)),
        check_vma=False,
    )
```

```python
import functools

import jax
import jax.numpy as jnp
import numpy as np
from jax import lax
from jax.sharding import PartitionSpec as P

GAMMA_GAS = 1.4
PRANDTL = 0.72
VISCOSITY = 0.25
ALPHA_FILTER = 0.499
ALPHA_SLOPE = 0.498
STRETCH = 1.2
STREAM_STEP = 1.0
SPAN_STEP = 0.5
HIGHEST = lax.Precision.HIGHEST


def slope_weights():
    near_weight = (2.0 + ALPHA_SLOPE) / 3.0
    far_weight = (4.0 * ALPHA_SLOPE - 1.0) / 12.0
    return (near_weight, far_weight)


def system_rows(system_kind, points):
    lower = np.zeros(points)
    middle = np.ones(points)
    upper = np.zeros(points)
    weights = np.zeros((7, points))
    if system_kind == "slope":
        near_weight, far_weight = slope_weights()
        lower[:] = ALPHA_SLOPE
        upper[:] = ALPHA_SLOPE
        weights[1] = -far_weight
        weights[2] = -near_weight
        weights[4] = near_weight
        weights[5] = far_weight
        for edge_row in (1, points - 2):
            lower[edge_row] = 0.25
            upper[edge_row] = 0.25
            weights[:, edge_row] = 0.0
            weights[2, edge_row] = -0.75
            weights[4, edge_row] = 0.75
        lower[0] = 0.0
        upper[0] = 2.0
        weights[:, 0] = 0.0
        weights[3, 0] = -2.5
        weights[4, 0] = 2.0
        weights[5, 0] = 0.5
        lower[points - 1] = 2.0
        upper[points - 1] = 0.0
        weights[:, points - 1] = 0.0
        weights[3, points - 1] = 2.5
        weights[2, points - 1] = -2.0
        weights[1, points - 1] = -0.5
    else:
        strength = ALPHA_FILTER
        lower[:] = strength
        upper[:] = strength
        weights[3] = 11.0 / 16.0 + 5.0 * strength / 8.0
        weights[2] = 15.0 / 64.0 + 17.0 * strength / 32.0
        weights[4] = weights[2]
        weights[1] = -3.0 / 32.0 + 3.0 * strength / 16.0
        weights[5] = weights[1]
        weights[0] = 1.0 / 64.0 - strength / 32.0
        weights[6] = weights[0]
        for edge_row in (2, points - 3):
            weights[:, edge_row] = 0.0
            weights[3, edge_row] = 5.0 / 8.0 + 3.0 * strength / 4.0
            weights[2, edge_row] = 0.25 + strength / 2.0
            weights[4, edge_row] = 0.25 + strength / 2.0
            weights[1, edge_row] = -1.0 / 16.0 + strength / 8.0
            weights[5, edge_row] = -1.0 / 16.0 + strength / 8.0
        for edge_row in (1, points - 2):
            weights[:, edge_row] = 0.0
            weights[3, edge_row] = 0.5 + strength
            weights[2, edge_row] = 0.25 + strength / 2.0
            weights[4, edge_row] = 0.25 + strength / 2.0
        for edge_row in (0, points - 1):
            lower[edge_row] = 0.0
            upper[edge_row] = 0.0
            weights[:, edge_row] = 0.0
            weights[3, edge_row] = 1.0
    return (lower, middle, upper, weights)


def inverse_metric(points):
    places = 2.0 * np.arange(points) / (points - 1) - 1.0
    growth = np.exp(STRETCH * places)
    cosh_values = 0.5 * (growth + 1.0 / growth)
    edge_growth = np.exp(STRETCH)
    tanh_value = (edge_growth - 1.0 / edge_growth) / (edge_growth + 1.0 / edge_growth)
    return tanh_value * cosh_values**2 / (0.64 * STRETCH)


def periodic_matrix(points, spacing):
    near_weight, far_weight = slope_weights()
    wave_numbers = np.arange(1, points // 2)
    angles = 2.0 * np.pi * wave_numbers / points
    modified = (2.0 * near_weight * np.sin(angles) + 2.0 * far_weight * np.sin(2.0 * angles)) / (
        1.0 + 2.0 * ALPHA_SLOPE * np.cos(angles)
    )
    phases = np.arange(points)[:, None] * wave_numbers[None, :] % points
    circulant = -2.0 / (points * spacing) * (np.sin(2.0 * np.pi * phases / points) @ modified)
    shifts = (np.arange(points)[:, None] - np.arange(points)[None, :]) % points
    return circulant[shifts].T


@functools.lru_cache(maxsize=None)
def wall_tables(kind, points, rows, pad, extra=0):
    assert extra == 0 or kind == "slope"
    lower, middle, upper, weights = system_rows(kind, points)
    system = np.diag(middle) + np.diag(lower[1:], -1) + np.diag(upper[:-1], 1)
    inv = np.linalg.inv(system)
    stencil = np.zeros((points, points + 6))
    for row in range(points):
        for offset in range(-3, 4):
            if weights[3 + offset, row] != 0.0:
                assert abs(offset) <= pad and 0 <= row + offset < points
                stencil[row, row + offset + 3] = weights[3 + offset, row]
    scale = inverse_metric(points) if kind == "slope" else np.ones(points)
    blocks = points // rows
    outputs = rows + 2 * extra
    combine = np.zeros((blocks, outputs + 2, rows + 2 * pad))
    rise_gain = np.zeros((blocks, outputs))
    fall_gain = np.zeros((blocks, outputs))
    rise_step = np.zeros(blocks)
    fall_step = np.zeros(blocks)
    for block in range(blocks):
        lo, hi = block * rows, block * rows + rows
        own = slice(lo, hi)
        window = slice(lo - pad + 3, hi + pad + 3)
        rise_part = np.zeros(rows)
        fall_part = np.zeros(rows)
        rise_ref = hi if block < blocks - 1 else lo
        fall_ref = lo - 1 if block > 0 else hi - 1
        if block > 0:
            rise_step[block] = inv[rise_ref, lo - 1] / inv[lo, lo - 1]
            fall_part = inv[lo - 1, own]
        if block < blocks - 1:
            fall_step[block] = inv[fall_ref, hi] / inv[hi - 1, hi]
            rise_part = inv[hi, own]
        for out, row in enumerate(range(lo - extra, hi + extra)):
            if row < 0 or row >= points:
                continue
            alpha = beta = 0.0
            if block > 0 or row >= hi:
                column = lo - 1 if lo <= row < hi else min(row, rise_ref) - 1
                alpha = inv[row, column] / inv[rise_ref, column]
            if block < blocks - 1:
                column = hi if row < hi else row + 1
                beta = inv[row, column] / inv[fall_ref, column]
            coef = np.zeros(points + 6)
            coef += (inv[row, own] - alpha * rise_part - beta * fall_part) @ stencil[own]
            if row == lo - 2:
                model = inv[row, row - 1] / inv[lo - 1, row - 1] * inv[lo - 1, lo - 1]
                coef += (inv[row, lo - 1] - model) * stencil[lo - 1]
            if row == hi + 1:
                model = inv[row, row + 1] / inv[hi, row + 1] * inv[hi, hi]
                coef += (inv[row, hi] - model) * stencil[hi]
            outside = coef.copy()
            outside[window] = 0.0
            assert not outside.any()
            combine[block, out] = scale[row] * coef[window]
            rise_gain[block, out] = scale[row] * alpha
            fall_gain[block, out] = scale[row] * beta
        rows_stencil = stencil[own, window]
        combine[block, outputs] = rise_part @ rows_stencil
        combine[block, outputs + 1] = fall_part @ rows_stencil
    rise_rows = combine[:, outputs].copy()
    fall_rows = combine[:, outputs + 1].copy()
    bottom = slice(pad, 2 * pad)
    top = slice(rows, rows + pad)
    below, above = slice(0, pad), slice(rows + pad, rows + 2 * pad)
    for block in range(blocks):
        rise_own = np.zeros(rows + 2 * pad)
        fall_own = np.zeros(rows + 2 * pad)
        rise_own[pad : pad + rows] = rise_rows[block, pad : pad + rows]
        fall_own[pad : pad + rows] = fall_rows[block, pad : pad + rows]
        rise_left = np.zeros(rows + 2 * pad)
        fall_left = np.zeros(rows + 2 * pad)
        if block + 1 < blocks:
            rise_own[top] += rise_rows[block + 1, below] / rise_step[block + 1]
            rise_left[top] -= rise_rows[block + 1, below] / rise_step[block + 1]
            fall_own[top] += fall_step[block] * fall_rows[block + 1, below]
        if block > 0:
            rise_own[bottom] += rise_step[block] * rise_rows[block - 1, above]
            fall_own[bottom] += fall_rows[block - 1, above] / fall_step[block - 1]
            fall_left[bottom] -= fall_rows[block - 1, above] / fall_step[block - 1]
        rise_left[above] += rise_rows[block, above]
        fall_left[below] += fall_rows[block, below]
        combine[block, :outputs] += np.outer(rise_gain[block], rise_left)
        combine[block, :outputs] += np.outer(fall_gain[block], fall_left)
        combine[block, outputs] = rise_own
        combine[block, outputs + 1] = fall_own
    return combine, rise_gain, fall_gain, rise_step, fall_step


def scan_rounds(blocks):
    rounds = []
    stride = 1
    while stride < blocks:
        radix = min(2, -(-blocks // stride))
        rounds.append((stride, list(range(1, radix))))
        stride *= radix
    return rounds[::-1]


def scan_coefs(rise_step, fall_step, shift):
    blocks = rise_step.shape[0]
    rise = np.zeros(blocks)
    fall = np.zeros(blocks)
    for block in range(blocks):
        if block - shift >= 0:
            rise[block] = np.prod(rise_step[block - shift + 1 : block + 1])
        if block + shift <= blocks - 1:
            fall[block] = np.prod(fall_step[block : block + shift])
    return rise, fall


class TableBank:
    def __init__(self):
        self.parts = []
        self.width = 0

    def add(self, table):
        table = np.asarray(table, np.float64)
        handle = (self.width, table.shape[1:])
        self.parts.append(table.reshape(table.shape[0], -1))
        self.width += self.parts[-1].shape[1]
        return handle

    def lookup(self, position):
        whole = jnp.asarray(np.concatenate(self.parts, axis=1), jnp.float32)
        self.row = lax.dynamic_index_in_dim(whole, position, 0, keepdims=False)

    def get(self, handle):
        start, shape = handle
        return self.row[start : start + int(np.prod(shape))].reshape(shape)


def plan_wall(bank, kinds_sizes, points, rows, pad, extras):
    tables = [
        wall_tables(kind, points, rows, pad, extra)
        for (kind, _), extra in zip(kinds_sizes, extras)
    ]
    groups = [
        (
            bank.add(table[0].transpose(0, 2, 1)),
            bank.add(table[1]),
            bank.add(table[2]),
            table[1].shape[1],
        )
        for table in tables
    ]
    blocks = points // rows
    rounds = []
    for stride, multiples in scan_rounds(blocks):
        entries = []
        for multiple in multiples:
            shift = stride * multiple
            coefs = [scan_coefs(table[3], table[4], shift) for table in tables]
            rise = np.concatenate(
                [np.repeat(c[0][:, None], n, 1) for c, (_, n) in zip(coefs, kinds_sizes)], 1
            )
            fall = np.concatenate(
                [np.repeat(c[1][:, None], n, 1) for c, (_, n) in zip(coefs, kinds_sizes)], 1
            )
            entries.append((shift, bank.add(rise), bank.add(fall)))
        rounds.append(entries)
    return groups, rounds


def wall_apply(bank, plan, padded_groups, own_groups, rows, pad):
    count = lax.axis_size("gy")
    groups, rounds = plan

    def taps(padded, by_tap):
        summed = None
        for tap in range(by_tap.shape[0]):
            term = by_tap[tap][:, None, None] * padded[:, None, tap]
            summed = term if summed is None else summed + term
        return summed

    partials = [
        taps(own, bank.get(handles[0])[pad : pad + rows, handles[3] :])
        for own, handles in zip(own_groups, groups)
    ]
    sizes = [padded.shape[0] for padded in padded_groups]
    rise = jnp.concatenate([part[:, 0] for part in partials], axis=0)
    fall = jnp.concatenate([part[:, 1] for part in partials], axis=0)
    for entries in rounds:
        rise_next, fall_next = rise, fall
        for shift, rise_handle, fall_handle in entries:
            up_pairs = [(i, i + shift) for i in range(count - shift)]
            down_pairs = [(i + shift, i) for i in range(count - shift)]
            from_below = lax.ppermute(rise, "gy", up_pairs)
            from_above = lax.ppermute(fall, "gy", down_pairs)
            rise_next = rise_next + bank.get(rise_handle)[:, None, None] * from_below
            fall_next = fall_next + bank.get(fall_handle)[:, None, None] * from_above
        rise, fall = rise_next, fall_next
    results = []
    first = 0
    for padded, handles, size in zip(padded_groups, groups, sizes):
        local = taps(padded, bank.get(handles[0])[:, : handles[3]])
        rise_gain = bank.get(handles[1])
        fall_gain = bank.get(handles[2])
        results.append(
            local
            + rise_gain[None, :, None, None] * rise[first : first + size, None]
            + fall_gain[None, :, None, None] * fall[first : first + size, None]
        )
        first += size
    return results


def halo(block, width):
    count = lax.axis_size("gy")
    up_pairs = [(i, i + 1) for i in range(count - 1)]
    down_pairs = [(i + 1, i) for i in range(count - 1)]
    below = lax.ppermute(block[:, block.shape[1] - width :], "gy", up_pairs)
    above = lax.ppermute(block[:, :width], "gy", down_pairs)
    return jnp.concatenate([below, block, above], axis=1)


def stream_slope(fields, stream_matrix):
    flat_rows = fields.reshape(-1, stream_matrix.shape[0])
    return jnp.dot(
        flat_rows, stream_matrix, precision=HIGHEST, preferred_element_type=jnp.float32
    ).reshape(fields.shape)


def span_slope(fields, own_block, other_block):
    other = lax.ppermute(fields, "pa", [(0, 1), (1, 0)])
    return jnp.einsum("fyzx,zw->fywx", fields, own_block, precision=HIGHEST) + jnp.einsum(
        "fyzx,zw->fywx", other, other_block, precision=HIGHEST
    )


def flux_along(direction, momentum, energy, speed, push, gradients):
    divergence = gradients[0][0] + gradients[1][1] + gradients[2][2]
    conduct = VISCOSITY * GAMMA_GAS / ((GAMMA_GAS - 1.0) * PRANDTL)
    rows_out = [momentum[direction]]
    energy_flux = (energy + push) * speed[direction]
    for component in range(3):
        stress = VISCOSITY * (gradients[direction][component] + gradients[component][direction])
        if component == direction:
            stress = stress - 2.0 / 3.0 * VISCOSITY * divergence
            rows_out.append(momentum[component] * speed[direction] + push - stress)
        else:
            rows_out.append(momentum[component] * speed[direction] - stress)
        energy_flux = energy_flux - speed[component] * stress
    energy_flux = energy_flux - conduct * gradients[direction][3]
    rows_out.append(energy_flux)
    return jnp.stack(rows_out)


def per_device(mass_per_volume, mass_flux_vector, total_heat_content):
    rows, span_own, stream_cells = mass_per_volume.shape
    count = lax.axis_size("gy")
    points = rows * count
    position = lax.axis_index("gy")
    span_total = span_own * lax.axis_size("pa")
    stream_matrix = jnp.asarray(periodic_matrix(stream_cells, STREAM_STEP), jnp.float32)
    span_full = periodic_matrix(span_total, SPAN_STEP)
    own_block = jnp.asarray(span_full[:span_own, :span_own], jnp.float32)
    other_block = jnp.asarray(span_full[span_own : 2 * span_own, :span_own], jnp.float32)

    bank = TableBank()
    first_plan = plan_wall(bank, [("slope", 4), ("smooth", 5)], points, rows, 3, (2, 0))
    second_plan = plan_wall(bank, [("slope", 5)], points, rows, 2, (0,))
    bank.lookup(position)

    state = jnp.concatenate(
        [mass_per_volume[None], mass_flux_vector, total_heat_content[None]], axis=0
    )
    padded = halo(state, 3)
    global_rows = position * rows - 3 + jnp.arange(rows + 6)
    inside = ((global_rows >= 0) & (global_rows < points))[:, None, None]
    density = jnp.where(inside, padded[0], 1.0)
    speed_pad = padded[1:4] / density[None]
    kinetic = 0.5 * jnp.sum(speed_pad * padded[1:4], axis=0)
    push_pad = (GAMMA_GAS - 1.0) * (padded[4] - kinetic)
    warmth_pad = push_pad / density
    basic_pad = jnp.concatenate([speed_pad, warmth_pad[None]], axis=0)

    speed_own = mass_flux_vector / mass_per_volume[None]
    kinetic_own = 0.5 * jnp.sum(speed_own * mass_flux_vector, axis=0)
    push_own = (GAMMA_GAS - 1.0) * (total_heat_content - kinetic_own)
    basic_own = jnp.concatenate([speed_own, (push_own / mass_per_volume)[None]], axis=0)
    wall_grad, smoothed = wall_apply(
        bank, first_plan, [basic_pad, padded], [basic_own, state], rows, 3
    )

    basic = basic_pad[:, 1 : rows + 5]
    speed = basic[:3]
    push = push_pad[1 : rows + 5]
    momentum = padded[1:4, 1 : rows + 5]
    energy = padded[4, 1 : rows + 5]
    grad_stream = stream_slope(basic, stream_matrix)
    grad_span = span_slope(basic, own_block, other_block)
    gradients = [grad_stream, wall_grad, grad_span]
    flux_wall = flux_along(1, momentum, energy, speed, push, gradients)
    (wall_term,) = wall_apply(bank, second_plan, [flux_wall], [flux_wall[:, 2 : 2 + rows]], rows, 2)
    own = slice(2, 2 + rows)
    gradients = [[part[own] for part in grad] for grad in gradients]
    speed, push = speed[:, own], push[own]
    momentum, energy = mass_flux_vector, total_heat_content
    stream_term = stream_slope(
        flux_along(0, momentum, energy, speed, push, gradients), stream_matrix
    )
    span_term = span_slope(
        flux_along(2, momentum, energy, speed, push, gradients), own_block, other_block
    )
    time_rate = -(stream_term + wall_term + span_term)
    own_rows = position * rows + jnp.arange(rows)
    at_wall = ((own_rows == 0) | (own_rows == points - 1))[None, :, None, None]
    held = jnp.where(at_wall, 0.0, time_rate[1:4])
    time_rate = jnp.concatenate([time_rate[:1], held, time_rate[4:]], axis=0)
    return (time_rate, smoothed)


def solution(mesh):
    placed = (P("gy", "pa", None), P(None, "gy", "pa", None), P("gy", "pa", None))
    return jax.shard_map(
        per_device,
        mesh=mesh,
        in_specs=placed,
        out_specs=(P(None, "gy", "pa", None), P(None, "gy", "pa", None)),
        check_vma=False,
    )
```

```python
import functools

import jax
import jax.numpy as jnp
import numpy as np
from jax import lax
from jax.sharding import PartitionSpec as P

GAMMA_GAS = 1.4
PRANDTL = 0.72
VISCOSITY = 0.25
ALPHA_FILTER = 0.499
ALPHA_SLOPE = 0.498
STRETCH = 1.2
STREAM_STEP = 1.0
SPAN_STEP = 0.5
HIGHEST = lax.Precision.HIGHEST


def slope_weights():
    near_weight = (2.0 + ALPHA_SLOPE) / 3.0
    far_weight = (4.0 * ALPHA_SLOPE - 1.0) / 12.0
    return (near_weight, far_weight)


def system_rows(system_kind, points):
    lower = np.zeros(points)
    middle = np.ones(points)
    upper = np.zeros(points)
    weights = np.zeros((7, points))
    if system_kind == "slope":
        near_weight, far_weight = slope_weights()
        lower[:] = ALPHA_SLOPE
        upper[:] = ALPHA_SLOPE
        weights[1] = -far_weight
        weights[2] = -near_weight
        weights[4] = near_weight
        weights[5] = far_weight
        for edge_row in (1, points - 2):
            lower[edge_row] = 0.25
            upper[edge_row] = 0.25
            weights[:, edge_row] = 0.0
            weights[2, edge_row] = -0.75
            weights[4, edge_row] = 0.75
        lower[0] = 0.0
        upper[0] = 2.0
        weights[:, 0] = 0.0
        weights[3, 0] = -2.5
        weights[4, 0] = 2.0
        weights[5, 0] = 0.5
        lower[points - 1] = 2.0
        upper[points - 1] = 0.0
        weights[:, points - 1] = 0.0
        weights[3, points - 1] = 2.5
        weights[2, points - 1] = -2.0
        weights[1, points - 1] = -0.5
    else:
        strength = ALPHA_FILTER
        lower[:] = strength
        upper[:] = strength
        weights[3] = 11.0 / 16.0 + 5.0 * strength / 8.0
        weights[2] = 15.0 / 64.0 + 17.0 * strength / 32.0
        weights[4] = weights[2]
        weights[1] = -3.0 / 32.0 + 3.0 * strength / 16.0
        weights[5] = weights[1]
        weights[0] = 1.0 / 64.0 - strength / 32.0
        weights[6] = weights[0]
        for edge_row in (2, points - 3):
            weights[:, edge_row] = 0.0
            weights[3, edge_row] = 5.0 / 8.0 + 3.0 * strength / 4.0
            weights[2, edge_row] = 0.25 + strength / 2.0
            weights[4, edge_row] = 0.25 + strength / 2.0
            weights[1, edge_row] = -1.0 / 16.0 + strength / 8.0
            weights[5, edge_row] = -1.0 / 16.0 + strength / 8.0
        for edge_row in (1, points - 2):
            weights[:, edge_row] = 0.0
            weights[3, edge_row] = 0.5 + strength
            weights[2, edge_row] = 0.25 + strength / 2.0
            weights[4, edge_row] = 0.25 + strength / 2.0
        for edge_row in (0, points - 1):
            lower[edge_row] = 0.0
            upper[edge_row] = 0.0
            weights[:, edge_row] = 0.0
            weights[3, edge_row] = 1.0
    return (lower, middle, upper, weights)


def inverse_metric(points):
    places = 2.0 * np.arange(points) / (points - 1) - 1.0
    growth = np.exp(STRETCH * places)
    cosh_values = 0.5 * (growth + 1.0 / growth)
    edge_growth = np.exp(STRETCH)
    tanh_value = (edge_growth - 1.0 / edge_growth) / (edge_growth + 1.0 / edge_growth)
    return tanh_value * cosh_values**2 / (0.64 * STRETCH)


def periodic_matrix(points, spacing):
    near_weight, far_weight = slope_weights()
    wave_numbers = np.arange(1, points // 2)
    angles = 2.0 * np.pi * wave_numbers / points
    modified = (2.0 * near_weight * np.sin(angles) + 2.0 * far_weight * np.sin(2.0 * angles)) / (
        1.0 + 2.0 * ALPHA_SLOPE * np.cos(angles)
    )
    phases = np.arange(points)[:, None] * wave_numbers[None, :] % points
    circulant = -2.0 / (points * spacing) * (np.sin(2.0 * np.pi * phases / points) @ modified)
    shifts = (np.arange(points)[:, None] - np.arange(points)[None, :]) % points
    return circulant[shifts].T


@functools.lru_cache(maxsize=None)
def wall_tables(kind, points, rows, pad, extra=0):
    assert extra == 0 or kind == "slope"
    lower, middle, upper, weights = system_rows(kind, points)
    system = np.diag(middle) + np.diag(lower[1:], -1) + np.diag(upper[:-1], 1)
    inv = np.linalg.inv(system)
    stencil = np.zeros((points, points + 6))
    for row in range(points):
        for offset in range(-3, 4):
            if weights[3 + offset, row] != 0.0:
                assert abs(offset) <= pad and 0 <= row + offset < points
                stencil[row, row + offset + 3] = weights[3 + offset, row]
    scale = inverse_metric(points) if kind == "slope" else np.ones(points)
    blocks = points // rows
    outputs = rows + 2 * extra
    combine = np.zeros((blocks, outputs + 2, rows + 2 * pad))
    rise_gain = np.zeros((blocks, outputs))
    fall_gain = np.zeros((blocks, outputs))
    rise_step = np.zeros(blocks)
    fall_step = np.zeros(blocks)
    for block in range(blocks):
        lo, hi = block * rows, block * rows + rows
        own = slice(lo, hi)
        window = slice(lo - pad + 3, hi + pad + 3)
        rise_part = np.zeros(rows)
        fall_part = np.zeros(rows)
        rise_ref = hi if block < blocks - 1 else lo
        fall_ref = lo - 1 if block > 0 else hi - 1
        if block > 0:
            rise_step[block] = inv[rise_ref, lo - 1] / inv[lo, lo - 1]
            fall_part = inv[lo - 1, own]
        if block < blocks - 1:
            fall_step[block] = inv[fall_ref, hi] / inv[hi - 1, hi]
            rise_part = inv[hi, own]
        for out, row in enumerate(range(lo - extra, hi + extra)):
            if row < 0 or row >= points:
                continue
            alpha = beta = 0.0
            if block > 0 or row >= hi:
                column = lo - 1 if lo <= row < hi else min(row, rise_ref) - 1
                alpha = inv[row, column] / inv[rise_ref, column]
            if block < blocks - 1:
                column = hi if row < hi else row + 1
                beta = inv[row, column] / inv[fall_ref, column]
            coef = np.zeros(points + 6)
            coef += (inv[row, own] - alpha * rise_part - beta * fall_part) @ stencil[own]
            if row == lo - 2:
                model = inv[row, row - 1] / inv[lo - 1, row - 1] * inv[lo - 1, lo - 1]
                coef += (inv[row, lo - 1] - model) * stencil[lo - 1]
            if row == hi + 1:
                model = inv[row, row + 1] / inv[hi, row + 1] * inv[hi, hi]
                coef += (inv[row, hi] - model) * stencil[hi]
            outside = coef.copy()
            outside[window] = 0.0
            assert not outside.any()
            combine[block, out] = scale[row] * coef[window]
            rise_gain[block, out] = scale[row] * alpha
            fall_gain[block, out] = scale[row] * beta
        rows_stencil = stencil[own, window]
        combine[block, outputs] = rise_part @ rows_stencil
        combine[block, outputs + 1] = fall_part @ rows_stencil
    return combine, rise_gain, fall_gain, rise_step, fall_step


def scan_rounds(blocks):
    rounds = []
    stride = 1
    while stride < blocks:
        radix = min(2, -(-blocks // stride))
        rounds.append((stride, list(range(1, radix))))
        stride *= radix
    reordered = []
    for first in range(len(rounds) - 2 + len(rounds) % 2, -1, -2):
        reordered += rounds[first : first + 2]
    return reordered


def scan_coefs(rise_step, fall_step, shift):
    blocks = rise_step.shape[0]
    rise = np.zeros(blocks)
    fall = np.zeros(blocks)
    for block in range(blocks):
        if block - shift >= 0:
            rise[block] = np.prod(rise_step[block - shift + 1 : block + 1])
        if block + shift <= blocks - 1:
            fall[block] = np.prod(fall_step[block : block + shift])
    return rise, fall


class TableBank:
    def __init__(self):
        self.parts = []
        self.width = 0

    def add(self, table):
        table = np.asarray(table, np.float64)
        handle = (self.width, table.shape[1:])
        self.parts.append(table.reshape(table.shape[0], -1))
        self.width += self.parts[-1].shape[1]
        return handle

    def lookup(self, position):
        whole = jnp.asarray(np.concatenate(self.parts, axis=1), jnp.float32)
        self.row = lax.dynamic_index_in_dim(whole, position, 0, keepdims=False)

    def get(self, handle):
        start, shape = handle
        return self.row[start : start + int(np.prod(shape))].reshape(shape)


def plan_wall(bank, kinds_sizes, points, rows, pad, extras):
    tables = [
        wall_tables(kind, points, rows, pad, extra)
        for (kind, _), extra in zip(kinds_sizes, extras)
    ]
    groups = [
        (
            bank.add(table[0].transpose(0, 2, 1)),
            bank.add(table[1]),
            bank.add(table[2]),
            table[1].shape[1],
        )
        for table in tables
    ]
    blocks = points // rows
    rounds = []
    for stride, multiples in scan_rounds(blocks):
        entries = []
        for multiple in multiples:
            shift = stride * multiple
            coefs = [scan_coefs(table[3], table[4], shift) for table in tables]
            rise = np.concatenate(
                [np.repeat(c[0][:, None], n, 1) for c, (_, n) in zip(coefs, kinds_sizes)], 1
            )
            fall = np.concatenate(
                [np.repeat(c[1][:, None], n, 1) for c, (_, n) in zip(coefs, kinds_sizes)], 1
            )
            entries.append((shift, bank.add(rise), bank.add(fall)))
        rounds.append(entries)
    return groups, rounds


def wall_apply(bank, plan, padded_groups, rows, pad):
    count = lax.axis_size("gy")
    groups, rounds = plan

    def taps(padded, by_tap):
        summed = None
        for tap in range(by_tap.shape[0]):
            term = by_tap[tap][:, None, None] * padded[:, None, tap]
            summed = term if summed is None else summed + term
        return summed

    partials = [
        taps(padded, bank.get(handles[0])[:, handles[3] :])
        for padded, handles in zip(padded_groups, groups)
    ]
    sizes = [padded.shape[0] for padded in padded_groups]
    rise = jnp.concatenate([part[:, 0] for part in partials], axis=0)
    fall = jnp.concatenate([part[:, 1] for part in partials], axis=0)
    for entries in rounds:
        rise_next, fall_next = rise, fall
        for shift, rise_handle, fall_handle in entries:
            up_pairs = [(i, i + shift) for i in range(count - shift)]
            down_pairs = [(i + shift, i) for i in range(count - shift)]
            from_below = lax.ppermute(rise, "gy", up_pairs)
            from_above = lax.ppermute(fall, "gy", down_pairs)
            rise_next = rise_next + bank.get(rise_handle)[:, None, None] * from_below
            fall_next = fall_next + bank.get(fall_handle)[:, None, None] * from_above
        rise, fall = rise_next, fall_next
    results = []
    first = 0
    for padded, handles, size in zip(padded_groups, groups, sizes):
        local = taps(padded, bank.get(handles[0])[:, : handles[3]])
        rise_gain = bank.get(handles[1])
        fall_gain = bank.get(handles[2])
        results.append(
            local
            + rise_gain[None, :, None, None] * rise[first : first + size, None]
            + fall_gain[None, :, None, None] * fall[first : first + size, None]
        )
        first += size
    return results


def halo(block, width):
    count = lax.axis_size("gy")
    up_pairs = [(i, i + 1) for i in range(count - 1)]
    down_pairs = [(i + 1, i) for i in range(count - 1)]
    below = lax.ppermute(block[:, block.shape[1] - width :], "gy", up_pairs)
    above = lax.ppermute(block[:, :width], "gy", down_pairs)
    return jnp.concatenate([below, block, above], axis=1)


def stream_slope(fields, stream_matrix):
    flat_rows = fields.reshape(-1, stream_matrix.shape[0])
    return jnp.dot(
        flat_rows, stream_matrix, precision=HIGHEST, preferred_element_type=jnp.float32
    ).reshape(fields.shape)


def span_slope(fields, own_block, other_block):
    other = lax.ppermute(fields, "pa", [(0, 1), (1, 0)])
    return jnp.einsum("fyzx,zw->fywx", fields, own_block, precision=HIGHEST) + jnp.einsum(
        "fyzx,zw->fywx", other, other_block, precision=HIGHEST
    )


def flux_along(direction, momentum, energy, speed, push, gradients):
    divergence = gradients[0][0] + gradients[1][1] + gradients[2][2]
    conduct = VISCOSITY * GAMMA_GAS / ((GAMMA_GAS - 1.0) * PRANDTL)
    rows_out = [momentum[direction]]
    energy_flux = (energy + push) * speed[direction]
    for component in range(3):
        stress = VISCOSITY * (gradients[direction][component] + gradients[component][direction])
        if component == direction:
            stress = stress - 2.0 / 3.0 * VISCOSITY * divergence
            rows_out.append(momentum[component] * speed[direction] + push - stress)
        else:
            rows_out.append(momentum[component] * speed[direction] - stress)
        energy_flux = energy_flux - speed[component] * stress
    energy_flux = energy_flux - conduct * gradients[direction][3]
    rows_out.append(energy_flux)
    return jnp.stack(rows_out)


def per_device(mass_per_volume, mass_flux_vector, total_heat_content):
    rows, span_own, stream_cells = mass_per_volume.shape
    count = lax.axis_size("gy")
    points = rows * count
    position = lax.axis_index("gy")
    span_total = span_own * lax.axis_size("pa")
    stream_matrix = jnp.asarray(periodic_matrix(stream_cells, STREAM_STEP), jnp.float32)
    span_full = periodic_matrix(span_total, SPAN_STEP)
    own_block = jnp.asarray(span_full[:span_own, :span_own], jnp.float32)
    other_block = jnp.asarray(span_full[span_own : 2 * span_own, :span_own], jnp.float32)

    bank = TableBank()
    first_plan = plan_wall(bank, [("slope", 4), ("smooth", 5)], points, rows, 3, (2, 0))
    second_plan = plan_wall(bank, [("slope", 5)], points, rows, 2, (0,))
    bank.lookup(position)

    state = jnp.concatenate(
        [mass_per_volume[None], mass_flux_vector, total_heat_content[None]], axis=0
    )
    padded = halo(state, 3)
    global_rows = position * rows - 3 + jnp.arange(rows + 6)
    inside = ((global_rows >= 0) & (global_rows < points))[:, None, None]
    density = jnp.where(inside, padded[0], 1.0)
    speed_pad = padded[1:4] / density[None]
    kinetic = 0.5 * jnp.sum(speed_pad * padded[1:4], axis=0)
    push_pad = (GAMMA_GAS - 1.0) * (padded[4] - kinetic)
    warmth_pad = push_pad / density
    basic_pad = jnp.concatenate([speed_pad, warmth_pad[None]], axis=0)

    wall_grad, smoothed = wall_apply(bank, first_plan, [basic_pad, padded], rows, 3)

    basic = basic_pad[:, 1 : rows + 5]
    speed = basic[:3]
    push = push_pad[1 : rows + 5]
    momentum = padded[1:4, 1 : rows + 5]
    energy = padded[4, 1 : rows + 5]
    grad_stream = stream_slope(basic, stream_matrix)
    grad_span = span_slope(basic, own_block, other_block)
    gradients = [grad_stream, wall_grad, grad_span]
    flux_wall = flux_along(1, momentum, energy, speed, push, gradients)
    (wall_term,) = wall_apply(bank, second_plan, [flux_wall], rows, 2)
    own = slice(2, 2 + rows)
    gradients = [[part[own] for part in grad] for grad in gradients]
    speed, push = speed[:, own], push[own]
    momentum, energy = mass_flux_vector, total_heat_content
    stream_term = stream_slope(
        flux_along(0, momentum, energy, speed, push, gradients), stream_matrix
    )
    span_term = span_slope(
        flux_along(2, momentum, energy, speed, push, gradients), own_block, other_block
    )
    time_rate = -(stream_term + wall_term + span_term)
    own_rows = position * rows + jnp.arange(rows)
    at_wall = ((own_rows == 0) | (own_rows == points - 1))[None, :, None, None]
    held = jnp.where(at_wall, 0.0, time_rate[1:4])
    time_rate = jnp.concatenate([time_rate[:1], held, time_rate[4:]], axis=0)
    return (time_rate, smoothed)


def solution(mesh):
    placed = (P("gy", "pa", None), P(None, "gy", "pa", None), P("gy", "pa", None))
    return jax.shard_map(
        per_device,
        mesh=mesh,
        in_specs=placed,
        out_specs=(P(None, "gy", "pa", None), P(None, "gy", "pa", None)),
        check_vma=False,
    )
```

```python
import functools

import jax
import jax.numpy as jnp
import numpy as np
from jax import lax
from jax.sharding import PartitionSpec as P

GAMMA_GAS = 1.4
PRANDTL = 0.72
VISCOSITY = 0.25
ALPHA_FILTER = 0.499
ALPHA_SLOPE = 0.498
STRETCH = 1.2
STREAM_STEP = 1.0
SPAN_STEP = 0.5
HIGHEST = lax.Precision.HIGHEST


def slope_weights():
    near_weight = (2.0 + ALPHA_SLOPE) / 3.0
    far_weight = (4.0 * ALPHA_SLOPE - 1.0) / 12.0
    return (near_weight, far_weight)


def system_rows(system_kind, points):
    lower = np.zeros(points)
    middle = np.ones(points)
    upper = np.zeros(points)
    weights = np.zeros((7, points))
    if system_kind == "slope":
        near_weight, far_weight = slope_weights()
        lower[:] = ALPHA_SLOPE
        upper[:] = ALPHA_SLOPE
        weights[1] = -far_weight
        weights[2] = -near_weight
        weights[4] = near_weight
        weights[5] = far_weight
        for edge_row in (1, points - 2):
            lower[edge_row] = 0.25
            upper[edge_row] = 0.25
            weights[:, edge_row] = 0.0
            weights[2, edge_row] = -0.75
            weights[4, edge_row] = 0.75
        lower[0] = 0.0
        upper[0] = 2.0
        weights[:, 0] = 0.0
        weights[3, 0] = -2.5
        weights[4, 0] = 2.0
        weights[5, 0] = 0.5
        lower[points - 1] = 2.0
        upper[points - 1] = 0.0
        weights[:, points - 1] = 0.0
        weights[3, points - 1] = 2.5
        weights[2, points - 1] = -2.0
        weights[1, points - 1] = -0.5
    else:
        strength = ALPHA_FILTER
        lower[:] = strength
        upper[:] = strength
        weights[3] = 11.0 / 16.0 + 5.0 * strength / 8.0
        weights[2] = 15.0 / 64.0 + 17.0 * strength / 32.0
        weights[4] = weights[2]
        weights[1] = -3.0 / 32.0 + 3.0 * strength / 16.0
        weights[5] = weights[1]
        weights[0] = 1.0 / 64.0 - strength / 32.0
        weights[6] = weights[0]
        for edge_row in (2, points - 3):
            weights[:, edge_row] = 0.0
            weights[3, edge_row] = 5.0 / 8.0 + 3.0 * strength / 4.0
            weights[2, edge_row] = 0.25 + strength / 2.0
            weights[4, edge_row] = 0.25 + strength / 2.0
            weights[1, edge_row] = -1.0 / 16.0 + strength / 8.0
            weights[5, edge_row] = -1.0 / 16.0 + strength / 8.0
        for edge_row in (1, points - 2):
            weights[:, edge_row] = 0.0
            weights[3, edge_row] = 0.5 + strength
            weights[2, edge_row] = 0.25 + strength / 2.0
            weights[4, edge_row] = 0.25 + strength / 2.0
        for edge_row in (0, points - 1):
            lower[edge_row] = 0.0
            upper[edge_row] = 0.0
            weights[:, edge_row] = 0.0
            weights[3, edge_row] = 1.0
    return (lower, middle, upper, weights)


def inverse_metric(points):
    places = 2.0 * np.arange(points) / (points - 1) - 1.0
    growth = np.exp(STRETCH * places)
    cosh_values = 0.5 * (growth + 1.0 / growth)
    edge_growth = np.exp(STRETCH)
    tanh_value = (edge_growth - 1.0 / edge_growth) / (edge_growth + 1.0 / edge_growth)
    return tanh_value * cosh_values**2 / (0.64 * STRETCH)


def periodic_matrix(points, spacing):
    near_weight, far_weight = slope_weights()
    wave_numbers = np.arange(1, points // 2)
    angles = 2.0 * np.pi * wave_numbers / points
    modified = (2.0 * near_weight * np.sin(angles) + 2.0 * far_weight * np.sin(2.0 * angles)) / (
        1.0 + 2.0 * ALPHA_SLOPE * np.cos(angles)
    )
    phases = np.arange(points)[:, None] * wave_numbers[None, :] % points
    circulant = -2.0 / (points * spacing) * (np.sin(2.0 * np.pi * phases / points) @ modified)
    shifts = (np.arange(points)[:, None] - np.arange(points)[None, :]) % points
    return circulant[shifts].T


@functools.lru_cache(maxsize=None)
def wall_tables(kind, points, rows, pad, extra=0):
    assert extra == 0 or kind == "slope"
    lower, middle, upper, weights = system_rows(kind, points)
    system = np.diag(middle) + np.diag(lower[1:], -1) + np.diag(upper[:-1], 1)
    inv = np.linalg.inv(system)
    stencil = np.zeros((points, points + 6))
    for row in range(points):
        for offset in range(-3, 4):
            if weights[3 + offset, row] != 0.0:
                assert abs(offset) <= pad and 0 <= row + offset < points
                stencil[row, row + offset + 3] = weights[3 + offset, row]
    scale = inverse_metric(points) if kind == "slope" else np.ones(points)
    blocks = points // rows
    outputs = rows + 2 * extra
    combine = np.zeros((blocks, outputs + 2, rows + 2 * pad))
    rise_gain = np.zeros((blocks, outputs))
    fall_gain = np.zeros((blocks, outputs))
    rise_step = np.zeros(blocks)
    fall_step = np.zeros(blocks)
    for block in range(blocks):
        lo, hi = block * rows, block * rows + rows
        own = slice(lo, hi)
        window = slice(lo - pad + 3, hi + pad + 3)
        rise_part = np.zeros(rows)
        fall_part = np.zeros(rows)
        rise_ref = hi if block < blocks - 1 else lo
        fall_ref = lo - 1 if block > 0 else hi - 1
        if block > 0:
            rise_step[block] = inv[rise_ref, lo - 1] / inv[lo, lo - 1]
            fall_part = inv[lo - 1, own]
        if block < blocks - 1:
            fall_step[block] = inv[fall_ref, hi] / inv[hi - 1, hi]
            rise_part = inv[hi, own]
        for out, row in enumerate(range(lo - extra, hi + extra)):
            if row < 0 or row >= points:
                continue
            alpha = beta = 0.0
            if block > 0 or row >= hi:
                column = lo - 1 if lo <= row < hi else min(row, rise_ref) - 1
                alpha = inv[row, column] / inv[rise_ref, column]
            if block < blocks - 1:
                column = hi if row < hi else row + 1
                beta = inv[row, column] / inv[fall_ref, column]
            coef = np.zeros(points + 6)
            coef += (inv[row, own] - alpha * rise_part - beta * fall_part) @ stencil[own]
            if row == lo - 2:
                model = inv[row, row - 1] / inv[lo - 1, row - 1] * inv[lo - 1, lo - 1]
                coef += (inv[row, lo - 1] - model) * stencil[lo - 1]
            if row == hi + 1:
                model = inv[row, row + 1] / inv[hi, row + 1] * inv[hi, hi]
                coef += (inv[row, hi] - model) * stencil[hi]
            outside = coef.copy()
            outside[window] = 0.0
            assert not outside.any()
            combine[block, out] = scale[row] * coef[window]
            rise_gain[block, out] = scale[row] * alpha
            fall_gain[block, out] = scale[row] * beta
        rows_stencil = stencil[own, window]
        combine[block, outputs] = rise_part @ rows_stencil
        combine[block, outputs + 1] = fall_part @ rows_stencil
    return combine, rise_gain, fall_gain, rise_step, fall_step


def scan_rounds(blocks):
    rounds = []
    stride = 1
    while stride < blocks:
        radix = min(2, -(-blocks // stride))
        rounds.append((stride, list(range(1, radix))))
        stride *= radix
    return rounds[::-1]


def scan_coefs(rise_step, fall_step, shift):
    blocks = rise_step.shape[0]
    rise = np.zeros(blocks)
    fall = np.zeros(blocks)
    for block in range(blocks):
        if block - shift >= 0:
            rise[block] = np.prod(rise_step[block - shift + 1 : block + 1])
        if block + shift <= blocks - 1:
            fall[block] = np.prod(fall_step[block : block + shift])
    return rise, fall


class TableBank:
    def __init__(self):
        self.parts = []
        self.width = 0

    def add(self, table):
        table = np.asarray(table, np.float64)
        handle = (self.width, table.shape[1:])
        self.parts.append(table.reshape(table.shape[0], -1))
        self.width += self.parts[-1].shape[1]
        return handle

    def lookup(self, position):
        whole = jnp.asarray(np.concatenate(self.parts, axis=1), jnp.float32)
        self.row = lax.dynamic_index_in_dim(whole, position, 0, keepdims=False)

    def get(self, handle):
        start, shape = handle
        return self.row[start : start + int(np.prod(shape))].reshape(shape)


def plan_wall(bank, kinds_sizes, points, rows, pads, extras):
    tables = [
        wall_tables(kind, points, rows, pad, extra)
        for (kind, _), pad, extra in zip(kinds_sizes, pads, extras)
    ]
    groups = [
        (
            bank.add(table[0].transpose(0, 2, 1)),
            bank.add(table[1]),
            bank.add(table[2]),
            table[1].shape[1],
        )
        for table in tables
    ]
    blocks = points // rows
    rounds = []
    for stride, multiples in scan_rounds(blocks):
        entries = []
        for multiple in multiples:
            shift = stride * multiple
            coefs = [scan_coefs(table[3], table[4], shift) for table in tables]
            rise = np.concatenate(
                [np.repeat(c[0][:, None], n, 1) for c, (_, n) in zip(coefs, kinds_sizes)], 1
            )
            fall = np.concatenate(
                [np.repeat(c[1][:, None], n, 1) for c, (_, n) in zip(coefs, kinds_sizes)], 1
            )
            entries.append((shift, bank.add(rise), bank.add(fall)))
        rounds.append(entries)
    return groups, rounds


def wall_apply(bank, plan, padded_groups, rows, pad):
    count = lax.axis_size("gy")
    groups, rounds = plan

    def taps(padded, by_tap):
        summed = None
        for tap in range(by_tap.shape[0]):
            term = by_tap[tap][:, None, None] * padded[:, None, tap]
            summed = term if summed is None else summed + term
        return summed

    partials = [
        taps(padded, bank.get(handles[0])[:, handles[3] :])
        for padded, handles in zip(padded_groups, groups)
    ]
    sizes = [padded.shape[0] for padded in padded_groups]
    rise = jnp.concatenate([part[:, 0] for part in partials], axis=0)
    fall = jnp.concatenate([part[:, 1] for part in partials], axis=0)
    for entries in rounds:
        rise_next, fall_next = rise, fall
        for shift, rise_handle, fall_handle in entries:
            up_pairs = [(i, i + shift) for i in range(count - shift)]
            down_pairs = [(i + shift, i) for i in range(count - shift)]
            from_below = lax.ppermute(rise, "gy", up_pairs)
            from_above = lax.ppermute(fall, "gy", down_pairs)
            rise_next = rise_next + bank.get(rise_handle)[:, None, None] * from_below
            fall_next = fall_next + bank.get(fall_handle)[:, None, None] * from_above
        rise, fall = rise_next, fall_next
    results = []
    first = 0
    for padded, handles, size in zip(padded_groups, groups, sizes):
        local = taps(padded, bank.get(handles[0])[:, : handles[3]])
        rise_gain = bank.get(handles[1])
        fall_gain = bank.get(handles[2])
        results.append(
            local
            + rise_gain[None, :, None, None] * rise[first : first + size, None]
            + fall_gain[None, :, None, None] * fall[first : first + size, None]
        )
        first += size
    return results


def halo(block, width):
    count = lax.axis_size("gy")
    up_pairs = [(i, i + 1) for i in range(count - 1)]
    down_pairs = [(i + 1, i) for i in range(count - 1)]
    below = lax.ppermute(block[:, block.shape[1] - width :], "gy", up_pairs)
    above = lax.ppermute(block[:, :width], "gy", down_pairs)
    return jnp.concatenate([below, block, above], axis=1)


def stream_slope(fields, stream_matrix):
    flat_rows = fields.reshape(-1, stream_matrix.shape[0])
    return jnp.dot(
        flat_rows, stream_matrix, precision=HIGHEST, preferred_element_type=jnp.float32
    ).reshape(fields.shape)


def span_slope(fields, own_block, other_block):
    other = lax.ppermute(fields, "pa", [(0, 1), (1, 0)])
    return jnp.einsum("fyzx,zw->fywx", fields, own_block, precision=HIGHEST) + jnp.einsum(
        "fyzx,zw->fywx", other, other_block, precision=HIGHEST
    )


def flux_along(direction, momentum, energy, speed, push, gradients):
    divergence = gradients[0][0] + gradients[1][1] + gradients[2][2]
    conduct = VISCOSITY * GAMMA_GAS / ((GAMMA_GAS - 1.0) * PRANDTL)
    rows_out = [momentum[direction]]
    energy_flux = (energy + push) * speed[direction]
    for component in range(3):
        stress = VISCOSITY * (gradients[direction][component] + gradients[component][direction])
        if component == direction:
            stress = stress - 2.0 / 3.0 * VISCOSITY * divergence
            rows_out.append(momentum[component] * speed[direction] + push - stress)
        else:
            rows_out.append(momentum[component] * speed[direction] - stress)
        energy_flux = energy_flux - speed[component] * stress
    energy_flux = energy_flux - conduct * gradients[direction][3]
    rows_out.append(energy_flux)
    return jnp.stack(rows_out)


def per_device(mass_per_volume, mass_flux_vector, total_heat_content):
    rows, span_own, stream_cells = mass_per_volume.shape
    count = lax.axis_size("gy")
    points = rows * count
    position = lax.axis_index("gy")
    span_total = span_own * lax.axis_size("pa")
    stream_matrix = jnp.asarray(periodic_matrix(stream_cells, STREAM_STEP), jnp.float32)
    span_full = periodic_matrix(span_total, SPAN_STEP)
    own_block = jnp.asarray(span_full[:span_own, :span_own], jnp.float32)
    other_block = jnp.asarray(span_full[span_own : 2 * span_own, :span_own], jnp.float32)

    bank = TableBank()
    first_plan = plan_wall(bank, [("slope", 4)], points, rows, (3,), (2,))
    second_plan = plan_wall(
        bank, [("slope", 5), ("smooth", 5)], points, rows, (2, 3), (0, 0)
    )
    bank.lookup(position)

    state = jnp.concatenate(
        [mass_per_volume[None], mass_flux_vector, total_heat_content[None]], axis=0
    )
    padded = halo(state, 3)
    global_rows = position * rows - 3 + jnp.arange(rows + 6)
    inside = ((global_rows >= 0) & (global_rows < points))[:, None, None]
    density = jnp.where(inside, padded[0], 1.0)
    speed_pad = padded[1:4] / density[None]
    kinetic = 0.5 * jnp.sum(speed_pad * padded[1:4], axis=0)
    push_pad = (GAMMA_GAS - 1.0) * (padded[4] - kinetic)
    warmth_pad = push_pad / density
    basic_pad = jnp.concatenate([speed_pad, warmth_pad[None]], axis=0)

    (wall_grad,) = wall_apply(bank, first_plan, [basic_pad], rows, 3)

    basic = basic_pad[:, 1 : rows + 5]
    speed = basic[:3]
    push = push_pad[1 : rows + 5]
    momentum = padded[1:4, 1 : rows + 5]
    energy = padded[4, 1 : rows + 5]
    grad_stream = stream_slope(basic, stream_matrix)
    grad_span = span_slope(basic, own_block, other_block)
    gradients = [grad_stream, wall_grad, grad_span]
    flux_wall = flux_along(1, momentum, energy, speed, push, gradients)
    wall_term, smoothed = wall_apply(bank, second_plan, [flux_wall, padded], rows, 2)
    own = slice(2, 2 + rows)
    gradients = [[part[own] for part in grad] for grad in gradients]
    speed, push = speed[:, own], push[own]
    momentum, energy = mass_flux_vector, total_heat_content
    stream_term = stream_slope(
        flux_along(0, momentum, energy, speed, push, gradients), stream_matrix
    )
    span_term = span_slope(
        flux_along(2, momentum, energy, speed, push, gradients), own_block, other_block
    )
    time_rate = -(stream_term + wall_term + span_term)
    own_rows = position * rows + jnp.arange(rows)
    at_wall = ((own_rows == 0) | (own_rows == points - 1))[None, :, None, None]
    held = jnp.where(at_wall, 0.0, time_rate[1:4])
    time_rate = jnp.concatenate([time_rate[:1], held, time_rate[4:]], axis=0)
    return (time_rate, smoothed)


def solution(mesh):
    placed = (P("gy", "pa", None), P(None, "gy", "pa", None), P("gy", "pa", None))
    return jax.shard_map(
        per_device,
        mesh=mesh,
        in_specs=placed,
        out_specs=(P(None, "gy", "pa", None), P(None, "gy", "pa", None)),
        check_vma=False,
    )
```

```python
import functools

import jax
import jax.numpy as jnp
import numpy as np
from jax import lax
from jax.sharding import PartitionSpec as P

GAMMA_GAS = 1.4
PRANDTL = 0.72
VISCOSITY = 0.25
ALPHA_FILTER = 0.499
ALPHA_SLOPE = 0.498
STRETCH = 1.2
STREAM_STEP = 1.0
SPAN_STEP = 0.5
HIGHEST = lax.Precision.HIGHEST


def slope_weights():
    near_weight = (2.0 + ALPHA_SLOPE) / 3.0
    far_weight = (4.0 * ALPHA_SLOPE - 1.0) / 12.0
    return (near_weight, far_weight)


def system_rows(system_kind, points):
    lower = np.zeros(points)
    middle = np.ones(points)
    upper = np.zeros(points)
    weights = np.zeros((7, points))
    if system_kind == "slope":
        near_weight, far_weight = slope_weights()
        lower[:] = ALPHA_SLOPE
        upper[:] = ALPHA_SLOPE
        weights[1] = -far_weight
        weights[2] = -near_weight
        weights[4] = near_weight
        weights[5] = far_weight
        for edge_row in (1, points - 2):
            lower[edge_row] = 0.25
            upper[edge_row] = 0.25
            weights[:, edge_row] = 0.0
            weights[2, edge_row] = -0.75
            weights[4, edge_row] = 0.75
        lower[0] = 0.0
        upper[0] = 2.0
        weights[:, 0] = 0.0
        weights[3, 0] = -2.5
        weights[4, 0] = 2.0
        weights[5, 0] = 0.5
        lower[points - 1] = 2.0
        upper[points - 1] = 0.0
        weights[:, points - 1] = 0.0
        weights[3, points - 1] = 2.5
        weights[2, points - 1] = -2.0
        weights[1, points - 1] = -0.5
    else:
        strength = ALPHA_FILTER
        lower[:] = strength
        upper[:] = strength
        weights[3] = 11.0 / 16.0 + 5.0 * strength / 8.0
        weights[2] = 15.0 / 64.0 + 17.0 * strength / 32.0
        weights[4] = weights[2]
        weights[1] = -3.0 / 32.0 + 3.0 * strength / 16.0
        weights[5] = weights[1]
        weights[0] = 1.0 / 64.0 - strength / 32.0
        weights[6] = weights[0]
        for edge_row in (2, points - 3):
            weights[:, edge_row] = 0.0
            weights[3, edge_row] = 5.0 / 8.0 + 3.0 * strength / 4.0
            weights[2, edge_row] = 0.25 + strength / 2.0
            weights[4, edge_row] = 0.25 + strength / 2.0
            weights[1, edge_row] = -1.0 / 16.0 + strength / 8.0
            weights[5, edge_row] = -1.0 / 16.0 + strength / 8.0
        for edge_row in (1, points - 2):
            weights[:, edge_row] = 0.0
            weights[3, edge_row] = 0.5 + strength
            weights[2, edge_row] = 0.25 + strength / 2.0
            weights[4, edge_row] = 0.25 + strength / 2.0
        for edge_row in (0, points - 1):
            lower[edge_row] = 0.0
            upper[edge_row] = 0.0
            weights[:, edge_row] = 0.0
            weights[3, edge_row] = 1.0
    return (lower, middle, upper, weights)


def inverse_metric(points):
    places = 2.0 * np.arange(points) / (points - 1) - 1.0
    growth = np.exp(STRETCH * places)
    cosh_values = 0.5 * (growth + 1.0 / growth)
    edge_growth = np.exp(STRETCH)
    tanh_value = (edge_growth - 1.0 / edge_growth) / (edge_growth + 1.0 / edge_growth)
    return tanh_value * cosh_values**2 / (0.64 * STRETCH)


def periodic_matrix(points, spacing):
    near_weight, far_weight = slope_weights()
    wave_numbers = np.arange(1, points // 2)
    angles = 2.0 * np.pi * wave_numbers / points
    modified = (2.0 * near_weight * np.sin(angles) + 2.0 * far_weight * np.sin(2.0 * angles)) / (
        1.0 + 2.0 * ALPHA_SLOPE * np.cos(angles)
    )
    phases = np.arange(points)[:, None] * wave_numbers[None, :] % points
    circulant = -2.0 / (points * spacing) * (np.sin(2.0 * np.pi * phases / points) @ modified)
    shifts = (np.arange(points)[:, None] - np.arange(points)[None, :]) % points
    return circulant[shifts].T


@functools.lru_cache(maxsize=None)
def wall_tables(kind, points, rows, pad, extra=0):
    assert extra == 0 or kind == "slope"
    lower, middle, upper, weights = system_rows(kind, points)
    system = np.diag(middle) + np.diag(lower[1:], -1) + np.diag(upper[:-1], 1)
    inv = np.linalg.inv(system)
    stencil = np.zeros((points, points + 6))
    for row in range(points):
        for offset in range(-3, 4):
            if weights[3 + offset, row] != 0.0:
                assert abs(offset) <= pad and 0 <= row + offset < points
                stencil[row, row + offset + 3] = weights[3 + offset, row]
    scale = inverse_metric(points) if kind == "slope" else np.ones(points)
    blocks = points // rows
    outputs = rows + 2 * extra
    combine = np.zeros((blocks, outputs + 2, rows + 2 * pad))
    rise_gain = np.zeros((blocks, outputs))
    fall_gain = np.zeros((blocks, outputs))
    rise_step = np.zeros(blocks)
    fall_step = np.zeros(blocks)
    for block in range(blocks):
        lo, hi = block * rows, block * rows + rows
        own = slice(lo, hi)
        window = slice(lo - pad + 3, hi + pad + 3)
        rise_part = np.zeros(rows)
        fall_part = np.zeros(rows)
        rise_ref = hi if block < blocks - 1 else lo
        fall_ref = lo - 1 if block > 0 else hi - 1
        if block > 0:
            rise_step[block] = inv[rise_ref, lo - 1] / inv[lo, lo - 1]
            fall_part = inv[lo - 1, own]
        if block < blocks - 1:
            fall_step[block] = inv[fall_ref, hi] / inv[hi - 1, hi]
            rise_part = inv[hi, own]
        for out, row in enumerate(range(lo - extra, hi + extra)):
            if row < 0 or row >= points:
                continue
            alpha = beta = 0.0
            if block > 0 or row >= hi:
                column = lo - 1 if lo <= row < hi else min(row, rise_ref) - 1
                alpha = inv[row, column] / inv[rise_ref, column]
            if block < blocks - 1:
                column = hi if row < hi else row + 1
                beta = inv[row, column] / inv[fall_ref, column]
            coef = np.zeros(points + 6)
            coef += (inv[row, own] - alpha * rise_part - beta * fall_part) @ stencil[own]
            if row == lo - 2:
                model = inv[row, row - 1] / inv[lo - 1, row - 1] * inv[lo - 1, lo - 1]
                coef += (inv[row, lo - 1] - model) * stencil[lo - 1]
            if row == hi + 1:
                model = inv[row, row + 1] / inv[hi, row + 1] * inv[hi, hi]
                coef += (inv[row, hi] - model) * stencil[hi]
            outside = coef.copy()
            outside[window] = 0.0
            assert not outside.any()
            combine[block, out] = scale[row] * coef[window]
            rise_gain[block, out] = scale[row] * alpha
            fall_gain[block, out] = scale[row] * beta
        rows_stencil = stencil[own, window]
        combine[block, outputs] = rise_part @ rows_stencil
        combine[block, outputs + 1] = fall_part @ rows_stencil
    return combine, rise_gain, fall_gain, rise_step, fall_step


def scan_rounds(blocks):
    rounds = []
    stride = 1
    while stride < blocks:
        radix = min(2, -(-blocks // stride))
        rounds.append((stride, list(range(1, radix))))
        stride *= radix
    return rounds[::-1]


def scan_coefs(rise_step, fall_step, shift):
    blocks = rise_step.shape[0]
    rise = np.zeros(blocks)
    fall = np.zeros(blocks)
    for block in range(blocks):
        if block - shift >= 0:
            rise[block] = np.prod(rise_step[block - shift + 1 : block + 1])
        if block + shift <= blocks - 1:
            fall[block] = np.prod(fall_step[block : block + shift])
    return rise, fall


class TableBank:
    def __init__(self):
        self.parts = []
        self.width = 0

    def add(self, table):
        table = np.asarray(table, np.float64)
        handle = (self.width, table.shape[1:])
        self.parts.append(table.reshape(table.shape[0], -1))
        self.width += self.parts[-1].shape[1]
        return handle

    def lookup(self, position):
        whole = jnp.asarray(np.concatenate(self.parts, axis=1), jnp.float32)
        self.row = lax.dynamic_index_in_dim(whole, position, 0, keepdims=False)

    def get(self, handle):
        start, shape = handle
        return self.row[start : start + int(np.prod(shape))].reshape(shape)


def plan_wall(bank, kinds_sizes, points, rows, pad, extras):
    tables = [
        wall_tables(kind, points, rows, pad, extra)
        for (kind, _), extra in zip(kinds_sizes, extras)
    ]
    groups = [
        (
            bank.add(table[0].transpose(0, 2, 1)),
            bank.add(table[1]),
            bank.add(table[2]),
            table[1].shape[1],
        )
        for table in tables
    ]
    blocks = points // rows
    rounds = []
    for stride, multiples in scan_rounds(blocks):
        entries = []
        for multiple in multiples:
            shift = stride * multiple
            coefs = [scan_coefs(table[3], table[4], shift) for table in tables]
            rise = np.concatenate(
                [np.repeat(c[0][:, None], n, 1) for c, (_, n) in zip(coefs, kinds_sizes)], 1
            )
            fall = np.concatenate(
                [np.repeat(c[1][:, None], n, 1) for c, (_, n) in zip(coefs, kinds_sizes)], 1
            )
            entries.append((shift, bank.add(rise), bank.add(fall)))
        rounds.append(entries)
    return groups, rounds


def wall_apply(bank, plan, padded_groups, rows, pad):
    count = lax.axis_size("gy")
    groups, rounds = plan

    def taps(padded, by_tap):
        summed = None
        for tap in range(by_tap.shape[0]):
            term = by_tap[tap][:, None, None] * padded[:, None, tap]
            summed = term if summed is None else summed + term
        return summed

    partials = [
        taps(padded, bank.get(handles[0])[:, handles[3] :])
        for padded, handles in zip(padded_groups, groups)
    ]
    sizes = [padded.shape[0] for padded in padded_groups]
    rise = jnp.concatenate([part[:, 0] for part in partials], axis=0)
    fall = jnp.concatenate([part[:, 1] for part in partials], axis=0)
    locals_ = [
        taps(padded, bank.get(handles[0])[:, : handles[3]])
        for padded, handles in zip(padded_groups, groups)
    ]
    for level, entries in enumerate(rounds):
        if level == len(rounds) // 2:
            rise, fall, locals_ = lax.optimization_barrier((rise, fall, locals_))
        rise_next, fall_next = rise, fall
        for shift, rise_handle, fall_handle in entries:
            up_pairs = [(i, i + shift) for i in range(count - shift)]
            down_pairs = [(i + shift, i) for i in range(count - shift)]
            from_below = lax.ppermute(rise, "gy", up_pairs)
            from_above = lax.ppermute(fall, "gy", down_pairs)
            rise_next = rise_next + bank.get(rise_handle)[:, None, None] * from_below
            fall_next = fall_next + bank.get(fall_handle)[:, None, None] * from_above
        rise, fall = rise_next, fall_next
    results = []
    first = 0
    for local, handles, size in zip(locals_, groups, sizes):
        rise_gain = bank.get(handles[1])
        fall_gain = bank.get(handles[2])
        results.append(
            local
            + rise_gain[None, :, None, None] * rise[first : first + size, None]
            + fall_gain[None, :, None, None] * fall[first : first + size, None]
        )
        first += size
    return results


def halo(block, width):
    count = lax.axis_size("gy")
    up_pairs = [(i, i + 1) for i in range(count - 1)]
    down_pairs = [(i + 1, i) for i in range(count - 1)]
    below = lax.ppermute(block[:, block.shape[1] - width :], "gy", up_pairs)
    above = lax.ppermute(block[:, :width], "gy", down_pairs)
    return jnp.concatenate([below, block, above], axis=1)


def stream_slope(fields, stream_matrix):
    flat_rows = fields.reshape(-1, stream_matrix.shape[0])
    return jnp.dot(
        flat_rows, stream_matrix, precision=HIGHEST, preferred_element_type=jnp.float32
    ).reshape(fields.shape)


def span_slope(fields, own_block, other_block):
    other = lax.ppermute(fields, "pa", [(0, 1), (1, 0)])
    return jnp.einsum("fyzx,zw->fywx", fields, own_block, precision=HIGHEST) + jnp.einsum(
        "fyzx,zw->fywx", other, other_block, precision=HIGHEST
    )


def flux_along(direction, momentum, energy, speed, push, gradients):
    divergence = gradients[0][0] + gradients[1][1] + gradients[2][2]
    conduct = VISCOSITY * GAMMA_GAS / ((GAMMA_GAS - 1.0) * PRANDTL)
    rows_out = [momentum[direction]]
    energy_flux = (energy + push) * speed[direction]
    for component in range(3):
        stress = VISCOSITY * (gradients[direction][component] + gradients[component][direction])
        if component == direction:
            stress = stress - 2.0 / 3.0 * VISCOSITY * divergence
            rows_out.append(momentum[component] * speed[direction] + push - stress)
        else:
            rows_out.append(momentum[component] * speed[direction] - stress)
        energy_flux = energy_flux - speed[component] * stress
    energy_flux = energy_flux - conduct * gradients[direction][3]
    rows_out.append(energy_flux)
    return jnp.stack(rows_out)


def per_device(mass_per_volume, mass_flux_vector, total_heat_content):
    rows, span_own, stream_cells = mass_per_volume.shape
    count = lax.axis_size("gy")
    points = rows * count
    position = lax.axis_index("gy")
    span_total = span_own * lax.axis_size("pa")
    stream_matrix = jnp.asarray(periodic_matrix(stream_cells, STREAM_STEP), jnp.float32)
    span_full = periodic_matrix(span_total, SPAN_STEP)
    own_block = jnp.asarray(span_full[:span_own, :span_own], jnp.float32)
    other_block = jnp.asarray(span_full[span_own : 2 * span_own, :span_own], jnp.float32)

    bank = TableBank()
    first_plan = plan_wall(bank, [("slope", 4), ("smooth", 5)], points, rows, 3, (2, 0))
    second_plan = plan_wall(bank, [("slope", 5)], points, rows, 2, (0,))
    bank.lookup(position)

    state = jnp.concatenate(
        [mass_per_volume[None], mass_flux_vector, total_heat_content[None]], axis=0
    )
    padded = halo(state, 3)
    global_rows = position * rows - 3 + jnp.arange(rows + 6)
    inside = ((global_rows >= 0) & (global_rows < points))[:, None, None]
    density = jnp.where(inside, padded[0], 1.0)
    speed_pad = padded[1:4] / density[None]
    kinetic = 0.5 * jnp.sum(speed_pad * padded[1:4], axis=0)
    push_pad = (GAMMA_GAS - 1.0) * (padded[4] - kinetic)
    warmth_pad = push_pad / density
    basic_pad = jnp.concatenate([speed_pad, warmth_pad[None]], axis=0)

    wall_grad, smoothed = wall_apply(bank, first_plan, [basic_pad, padded], rows, 3)

    basic = basic_pad[:, 1 : rows + 5]
    speed = basic[:3]
    push = push_pad[1 : rows + 5]
    momentum = padded[1:4, 1 : rows + 5]
    energy = padded[4, 1 : rows + 5]
    grad_stream = stream_slope(basic, stream_matrix)
    grad_span = span_slope(basic, own_block, other_block)
    gradients = [grad_stream, wall_grad, grad_span]
    flux_wall = flux_along(1, momentum, energy, speed, push, gradients)
    (wall_term,) = wall_apply(bank, second_plan, [flux_wall], rows, 2)
    own = slice(2, 2 + rows)
    gradients = [[part[own] for part in grad] for grad in gradients]
    speed, push = speed[:, own], push[own]
    momentum, energy = mass_flux_vector, total_heat_content
    stream_term = stream_slope(
        flux_along(0, momentum, energy, speed, push, gradients), stream_matrix
    )
    span_term = span_slope(
        flux_along(2, momentum, energy, speed, push, gradients), own_block, other_block
    )
    time_rate = -(stream_term + wall_term + span_term)
    own_rows = position * rows + jnp.arange(rows)
    at_wall = ((own_rows == 0) | (own_rows == points - 1))[None, :, None, None]
    held = jnp.where(at_wall, 0.0, time_rate[1:4])
    time_rate = jnp.concatenate([time_rate[:1], held, time_rate[4:]], axis=0)
    return (time_rate, smoothed)


def solution(mesh):
    placed = (P("gy", "pa", None), P(None, "gy", "pa", None), P("gy", "pa", None))
    return jax.shard_map(
        per_device,
        mesh=mesh,
        in_specs=placed,
        out_specs=(P(None, "gy", "pa", None), P(None, "gy", "pa", None)),
        check_vma=False,
    )
```

```python
import functools

import jax
import jax.numpy as jnp
import numpy as np
from jax import lax
from jax.sharding import PartitionSpec as P

GAMMA_GAS = 1.4
PRANDTL = 0.72
VISCOSITY = 0.25
ALPHA_FILTER = 0.499
ALPHA_SLOPE = 0.498
STRETCH = 1.2
STREAM_STEP = 1.0
SPAN_STEP = 0.5
HIGHEST = lax.Precision.HIGHEST


def slope_weights():
    near_weight = (2.0 + ALPHA_SLOPE) / 3.0
    far_weight = (4.0 * ALPHA_SLOPE - 1.0) / 12.0
    return (near_weight, far_weight)


def system_rows(system_kind, points):
    lower = np.zeros(points)
    middle = np.ones(points)
    upper = np.zeros(points)
    weights = np.zeros((7, points))
    if system_kind == "slope":
        near_weight, far_weight = slope_weights()
        lower[:] = ALPHA_SLOPE
        upper[:] = ALPHA_SLOPE
        weights[1] = -far_weight
        weights[2] = -near_weight
        weights[4] = near_weight
        weights[5] = far_weight
        for edge_row in (1, points - 2):
            lower[edge_row] = 0.25
            upper[edge_row] = 0.25
            weights[:, edge_row] = 0.0
            weights[2, edge_row] = -0.75
            weights[4, edge_row] = 0.75
        lower[0] = 0.0
        upper[0] = 2.0
        weights[:, 0] = 0.0
        weights[3, 0] = -2.5
        weights[4, 0] = 2.0
        weights[5, 0] = 0.5
        lower[points - 1] = 2.0
        upper[points - 1] = 0.0
        weights[:, points - 1] = 0.0
        weights[3, points - 1] = 2.5
        weights[2, points - 1] = -2.0
        weights[1, points - 1] = -0.5
    else:
        strength = ALPHA_FILTER
        lower[:] = strength
        upper[:] = strength
        weights[3] = 11.0 / 16.0 + 5.0 * strength / 8.0
        weights[2] = 15.0 / 64.0 + 17.0 * strength / 32.0
        weights[4] = weights[2]
        weights[1] = -3.0 / 32.0 + 3.0 * strength / 16.0
        weights[5] = weights[1]
        weights[0] = 1.0 / 64.0 - strength / 32.0
        weights[6] = weights[0]
        for edge_row in (2, points - 3):
            weights[:, edge_row] = 0.0
            weights[3, edge_row] = 5.0 / 8.0 + 3.0 * strength / 4.0
            weights[2, edge_row] = 0.25 + strength / 2.0
            weights[4, edge_row] = 0.25 + strength / 2.0
            weights[1, edge_row] = -1.0 / 16.0 + strength / 8.0
            weights[5, edge_row] = -1.0 / 16.0 + strength / 8.0
        for edge_row in (1, points - 2):
            weights[:, edge_row] = 0.0
            weights[3, edge_row] = 0.5 + strength
            weights[2, edge_row] = 0.25 + strength / 2.0
            weights[4, edge_row] = 0.25 + strength / 2.0
        for edge_row in (0, points - 1):
            lower[edge_row] = 0.0
            upper[edge_row] = 0.0
            weights[:, edge_row] = 0.0
            weights[3, edge_row] = 1.0
    return (lower, middle, upper, weights)


def inverse_metric(points):
    places = 2.0 * np.arange(points) / (points - 1) - 1.0
    growth = np.exp(STRETCH * places)
    cosh_values = 0.5 * (growth + 1.0 / growth)
    edge_growth = np.exp(STRETCH)
    tanh_value = (edge_growth - 1.0 / edge_growth) / (edge_growth + 1.0 / edge_growth)
    return tanh_value * cosh_values**2 / (0.64 * STRETCH)


def periodic_matrix(points, spacing):
    near_weight, far_weight = slope_weights()
    wave_numbers = np.arange(1, points // 2)
    angles = 2.0 * np.pi * wave_numbers / points
    modified = (2.0 * near_weight * np.sin(angles) + 2.0 * far_weight * np.sin(2.0 * angles)) / (
        1.0 + 2.0 * ALPHA_SLOPE * np.cos(angles)
    )
    phases = np.arange(points)[:, None] * wave_numbers[None, :] % points
    circulant = -2.0 / (points * spacing) * (np.sin(2.0 * np.pi * phases / points) @ modified)
    shifts = (np.arange(points)[:, None] - np.arange(points)[None, :]) % points
    return circulant[shifts].T


@functools.lru_cache(maxsize=None)
def wall_tables(kind, points, rows, pad, extra=0):
    assert extra == 0 or kind == "slope"
    lower, middle, upper, weights = system_rows(kind, points)
    system = np.diag(middle) + np.diag(lower[1:], -1) + np.diag(upper[:-1], 1)
    inv = np.linalg.inv(system)
    stencil = np.zeros((points, points + 6))
    for row in range(points):
        for offset in range(-3, 4):
            if weights[3 + offset, row] != 0.0:
                assert abs(offset) <= pad and 0 <= row + offset < points
                stencil[row, row + offset + 3] = weights[3 + offset, row]
    scale = inverse_metric(points) if kind == "slope" else np.ones(points)
    blocks = points // rows
    outputs = rows + 2 * extra
    combine = np.zeros((blocks, outputs + 2, rows + 2 * pad))
    rise_gain = np.zeros((blocks, outputs))
    fall_gain = np.zeros((blocks, outputs))
    rise_step = np.zeros(blocks)
    fall_step = np.zeros(blocks)
    for block in range(blocks):
        lo, hi = block * rows, block * rows + rows
        own = slice(lo, hi)
        window = slice(lo - pad + 3, hi + pad + 3)
        rise_part = np.zeros(rows)
        fall_part = np.zeros(rows)
        rise_ref = hi if block < blocks - 1 else lo
        fall_ref = lo - 1 if block > 0 else hi - 1
        if block > 0:
            rise_step[block] = inv[rise_ref, lo - 1] / inv[lo, lo - 1]
            fall_part = inv[lo - 1, own]
        if block < blocks - 1:
            fall_step[block] = inv[fall_ref, hi] / inv[hi - 1, hi]
            rise_part = inv[hi, own]
        for out, row in enumerate(range(lo - extra, hi + extra)):
            if row < 0 or row >= points:
                continue
            alpha = beta = 0.0
            if block > 0 or row >= hi:
                column = lo - 1 if lo <= row < hi else min(row, rise_ref) - 1
                alpha = inv[row, column] / inv[rise_ref, column]
            if block < blocks - 1:
                column = hi if row < hi else row + 1
                beta = inv[row, column] / inv[fall_ref, column]
            coef = np.zeros(points + 6)
            coef += (inv[row, own] - alpha * rise_part - beta * fall_part) @ stencil[own]
            if row == lo - 2:
                model = inv[row, row - 1] / inv[lo - 1, row - 1] * inv[lo - 1, lo - 1]
                coef += (inv[row, lo - 1] - model) * stencil[lo - 1]
            if row == hi + 1:
                model = inv[row, row + 1] / inv[hi, row + 1] * inv[hi, hi]
                coef += (inv[row, hi] - model) * stencil[hi]
            outside = coef.copy()
            outside[window] = 0.0
            assert not outside.any()
            combine[block, out] = scale[row] * coef[window]
            rise_gain[block, out] = scale[row] * alpha
            fall_gain[block, out] = scale[row] * beta
        rows_stencil = stencil[own, window]
        combine[block, outputs] = rise_part @ rows_stencil
        combine[block, outputs + 1] = fall_part @ rows_stencil
    return combine, rise_gain, fall_gain, rise_step, fall_step


def scan_rounds(blocks):
    rounds = []
    stride = 1
    while stride < blocks:
        radix = min(2, -(-blocks // stride))
        rounds.append((stride, list(range(1, radix))))
        stride *= radix
    return rounds[::-1]


def scan_coefs(rise_step, fall_step, shift):
    blocks = rise_step.shape[0]
    rise = np.zeros(blocks)
    fall = np.zeros(blocks)
    for block in range(blocks):
        if block - shift >= 0:
            rise[block] = np.prod(rise_step[block - shift + 1 : block + 1])
        if block + shift <= blocks - 1:
            fall[block] = np.prod(fall_step[block : block + shift])
    return rise, fall


class TableBank:
    def __init__(self):
        self.parts = []
        self.width = 0

    def add(self, table):
        table = np.asarray(table, np.float64)
        handle = (self.width, table.shape[1:])
        self.parts.append(table.reshape(table.shape[0], -1))
        self.width += self.parts[-1].shape[1]
        return handle

    def lookup(self, position):
        whole = jnp.asarray(np.concatenate(self.parts, axis=1), jnp.float32)
        self.row = lax.dynamic_index_in_dim(whole, position, 0, keepdims=False)

    def get(self, handle):
        start, shape = handle
        return self.row[start : start + int(np.prod(shape))].reshape(shape)


def plan_wall(bank, kinds_sizes, points, rows, pad, extras):
    tables = [
        wall_tables(kind, points, rows, pad, extra)
        for (kind, _), extra in zip(kinds_sizes, extras)
    ]
    groups = [
        (
            bank.add(table[0].transpose(0, 2, 1)),
            bank.add(table[1]),
            bank.add(table[2]),
            table[1].shape[1],
        )
        for table in tables
    ]
    blocks = points // rows
    rounds = []
    for stride, multiples in scan_rounds(blocks):
        entries = []
        for multiple in multiples:
            shift = stride * multiple
            coefs = [scan_coefs(table[3], table[4], shift) for table in tables]
            rise = np.concatenate(
                [np.repeat(c[0][:, None], n, 1) for c, (_, n) in zip(coefs, kinds_sizes)], 1
            )
            fall = np.concatenate(
                [np.repeat(c[1][:, None], n, 1) for c, (_, n) in zip(coefs, kinds_sizes)], 1
            )
            entries.append((shift, bank.add(rise), bank.add(fall)))
        rounds.append(entries)
    return groups, rounds


def wall_apply(bank, plan, padded_groups, rows, pad):
    count = lax.axis_size("gy")
    groups, rounds = plan

    def taps(padded, by_tap):
        summed = None
        for tap in range(by_tap.shape[0]):
            term = by_tap[tap][:, None, None] * padded[:, None, tap]
            summed = term if summed is None else summed + term
        return summed

    partials = [
        taps(padded, bank.get(handles[0])[:, handles[3] :])
        for padded, handles in zip(padded_groups, groups)
    ]
    sizes = [padded.shape[0] for padded in padded_groups]
    rise = jnp.concatenate([part[:, 0] for part in partials], axis=0)
    fall = jnp.concatenate([part[:, 1] for part in partials], axis=0)
    locals_ = [
        taps(padded, bank.get(handles[0])[:, : handles[3]])
        for padded, handles in zip(padded_groups, groups)
    ]
    for level, entries in enumerate(rounds):
        if level == len(rounds) - 1:
            rise, fall, locals_ = lax.optimization_barrier((rise, fall, locals_))
        rise_next, fall_next = rise, fall
        for shift, rise_handle, fall_handle in entries:
            up_pairs = [(i, i + shift) for i in range(count - shift)]
            down_pairs = [(i + shift, i) for i in range(count - shift)]
            from_below = lax.ppermute(rise, "gy", up_pairs)
            from_above = lax.ppermute(fall, "gy", down_pairs)
            rise_next = rise_next + bank.get(rise_handle)[:, None, None] * from_below
            fall_next = fall_next + bank.get(fall_handle)[:, None, None] * from_above
        rise, fall = rise_next, fall_next
    results = []
    first = 0
    for local, handles, size in zip(locals_, groups, sizes):
        rise_gain = bank.get(handles[1])
        fall_gain = bank.get(handles[2])
        results.append(
            local
            + rise_gain[None, :, None, None] * rise[first : first + size, None]
            + fall_gain[None, :, None, None] * fall[first : first + size, None]
        )
        first += size
    return results


def halo(block, width):
    count = lax.axis_size("gy")
    up_pairs = [(i, i + 1) for i in range(count - 1)]
    down_pairs = [(i + 1, i) for i in range(count - 1)]
    below = lax.ppermute(block[:, block.shape[1] - width :], "gy", up_pairs)
    above = lax.ppermute(block[:, :width], "gy", down_pairs)
    return jnp.concatenate([below, block, above], axis=1)


def stream_slope(fields, stream_matrix):
    flat_rows = fields.reshape(-1, stream_matrix.shape[0])
    return jnp.dot(
        flat_rows, stream_matrix, precision=HIGHEST, preferred_element_type=jnp.float32
    ).reshape(fields.shape)


def span_slope(fields, own_block, other_block):
    other = lax.ppermute(fields, "pa", [(0, 1), (1, 0)])
    return jnp.einsum("fyzx,zw->fywx", fields, own_block, precision=HIGHEST) + jnp.einsum(
        "fyzx,zw->fywx", other, other_block, precision=HIGHEST
    )


def flux_along(direction, momentum, energy, speed, push, gradients):
    divergence = gradients[0][0] + gradients[1][1] + gradients[2][2]
    conduct = VISCOSITY * GAMMA_GAS / ((GAMMA_GAS - 1.0) * PRANDTL)
    rows_out = [momentum[direction]]
    energy_flux = (energy + push) * speed[direction]
    for component in range(3):
        stress = VISCOSITY * (gradients[direction][component] + gradients[component][direction])
        if component == direction:
            stress = stress - 2.0 / 3.0 * VISCOSITY * divergence
            rows_out.append(momentum[component] * speed[direction] + push - stress)
        else:
            rows_out.append(momentum[component] * speed[direction] - stress)
        energy_flux = energy_flux - speed[component] * stress
    energy_flux = energy_flux - conduct * gradients[direction][3]
    rows_out.append(energy_flux)
    return jnp.stack(rows_out)


def per_device(mass_per_volume, mass_flux_vector, total_heat_content):
    rows, span_own, stream_cells = mass_per_volume.shape
    count = lax.axis_size("gy")
    points = rows * count
    position = lax.axis_index("gy")
    span_total = span_own * lax.axis_size("pa")
    stream_matrix = jnp.asarray(periodic_matrix(stream_cells, STREAM_STEP), jnp.float32)
    span_full = periodic_matrix(span_total, SPAN_STEP)
    own_block = jnp.asarray(span_full[:span_own, :span_own], jnp.float32)
    other_block = jnp.asarray(span_full[span_own : 2 * span_own, :span_own], jnp.float32)

    bank = TableBank()
    first_plan = plan_wall(bank, [("slope", 4), ("smooth", 5)], points, rows, 3, (2, 0))
    second_plan = plan_wall(bank, [("slope", 5)], points, rows, 2, (0,))
    bank.lookup(position)

    state = jnp.concatenate(
        [mass_per_volume[None], mass_flux_vector, total_heat_content[None]], axis=0
    )
    padded = halo(state, 3)
    global_rows = position * rows - 3 + jnp.arange(rows + 6)
    inside = ((global_rows >= 0) & (global_rows < points))[:, None, None]
    density = jnp.where(inside, padded[0], 1.0)
    speed_pad = padded[1:4] / density[None]
    kinetic = 0.5 * jnp.sum(speed_pad * padded[1:4], axis=0)
    push_pad = (GAMMA_GAS - 1.0) * (padded[4] - kinetic)
    warmth_pad = push_pad / density
    basic_pad = jnp.concatenate([speed_pad, warmth_pad[None]], axis=0)

    wall_grad, smoothed = wall_apply(bank, first_plan, [basic_pad, padded], rows, 3)

    basic = basic_pad[:, 1 : rows + 5]
    speed = basic[:3]
    push = push_pad[1 : rows + 5]
    momentum = padded[1:4, 1 : rows + 5]
    energy = padded[4, 1 : rows + 5]
    grad_stream = stream_slope(basic, stream_matrix)
    grad_span = span_slope(basic, own_block, other_block)
    gradients = [grad_stream, wall_grad, grad_span]
    flux_wall = flux_along(1, momentum, energy, speed, push, gradients)
    (wall_term,) = wall_apply(bank, second_plan, [flux_wall], rows, 2)
    own = slice(2, 2 + rows)
    gradients = [[part[own] for part in grad] for grad in gradients]
    speed, push = speed[:, own], push[own]
    momentum, energy = mass_flux_vector, total_heat_content
    stream_term = stream_slope(
        flux_along(0, momentum, energy, speed, push, gradients), stream_matrix
    )
    span_term = span_slope(
        flux_along(2, momentum, energy, speed, push, gradients), own_block, other_block
    )
    time_rate = -(stream_term + wall_term + span_term)
    own_rows = position * rows + jnp.arange(rows)
    at_wall = ((own_rows == 0) | (own_rows == points - 1))[None, :, None, None]
    held = jnp.where(at_wall, 0.0, time_rate[1:4])
    time_rate = jnp.concatenate([time_rate[:1], held, time_rate[4:]], axis=0)
    return (time_rate, smoothed)


def solution(mesh):
    placed = (P("gy", "pa", None), P(None, "gy", "pa", None), P("gy", "pa", None))
    return jax.shard_map(
        per_device,
        mesh=mesh,
        in_specs=placed,
        out_specs=(P(None, "gy", "pa", None), P(None, "gy", "pa", None)),
        check_vma=False,
    )
```

```python
import functools

import jax
import jax.numpy as jnp
import numpy as np
from jax import lax
from jax.sharding import PartitionSpec as P

GAMMA_GAS = 1.4
PRANDTL = 0.72
VISCOSITY = 0.25
ALPHA_FILTER = 0.499
ALPHA_SLOPE = 0.498
STRETCH = 1.2
STREAM_STEP = 1.0
SPAN_STEP = 0.5
HIGHEST = lax.Precision.HIGHEST


def slope_weights():
    near_weight = (2.0 + ALPHA_SLOPE) / 3.0
    far_weight = (4.0 * ALPHA_SLOPE - 1.0) / 12.0
    return (near_weight, far_weight)


def system_rows(system_kind, points):
    lower = np.zeros(points)
    middle = np.ones(points)
    upper = np.zeros(points)
    weights = np.zeros((7, points))
    if system_kind == "slope":
        near_weight, far_weight = slope_weights()
        lower[:] = ALPHA_SLOPE
        upper[:] = ALPHA_SLOPE
        weights[1] = -far_weight
        weights[2] = -near_weight
        weights[4] = near_weight
        weights[5] = far_weight
        for edge_row in (1, points - 2):
            lower[edge_row] = 0.25
            upper[edge_row] = 0.25
            weights[:, edge_row] = 0.0
            weights[2, edge_row] = -0.75
            weights[4, edge_row] = 0.75
        lower[0] = 0.0
        upper[0] = 2.0
        weights[:, 0] = 0.0
        weights[3, 0] = -2.5
        weights[4, 0] = 2.0
        weights[5, 0] = 0.5
        lower[points - 1] = 2.0
        upper[points - 1] = 0.0
        weights[:, points - 1] = 0.0
        weights[3, points - 1] = 2.5
        weights[2, points - 1] = -2.0
        weights[1, points - 1] = -0.5
    else:
        strength = ALPHA_FILTER
        lower[:] = strength
        upper[:] = strength
        weights[3] = 11.0 / 16.0 + 5.0 * strength / 8.0
        weights[2] = 15.0 / 64.0 + 17.0 * strength / 32.0
        weights[4] = weights[2]
        weights[1] = -3.0 / 32.0 + 3.0 * strength / 16.0
        weights[5] = weights[1]
        weights[0] = 1.0 / 64.0 - strength / 32.0
        weights[6] = weights[0]
        for edge_row in (2, points - 3):
            weights[:, edge_row] = 0.0
            weights[3, edge_row] = 5.0 / 8.0 + 3.0 * strength / 4.0
            weights[2, edge_row] = 0.25 + strength / 2.0
            weights[4, edge_row] = 0.25 + strength / 2.0
            weights[1, edge_row] = -1.0 / 16.0 + strength / 8.0
            weights[5, edge_row] = -1.0 / 16.0 + strength / 8.0
        for edge_row in (1, points - 2):
            weights[:, edge_row] = 0.0
            weights[3, edge_row] = 0.5 + strength
            weights[2, edge_row] = 0.25 + strength / 2.0
            weights[4, edge_row] = 0.25 + strength / 2.0
        for edge_row in (0, points - 1):
            lower[edge_row] = 0.0
            upper[edge_row] = 0.0
            weights[:, edge_row] = 0.0
            weights[3, edge_row] = 1.0
    return (lower, middle, upper, weights)


def inverse_metric(points):
    places = 2.0 * np.arange(points) / (points - 1) - 1.0
    growth = np.exp(STRETCH * places)
    cosh_values = 0.5 * (growth + 1.0 / growth)
    edge_growth = np.exp(STRETCH)
    tanh_value = (edge_growth - 1.0 / edge_growth) / (edge_growth + 1.0 / edge_growth)
    return tanh_value * cosh_values**2 / (0.64 * STRETCH)


def periodic_matrix(points, spacing):
    near_weight, far_weight = slope_weights()
    wave_numbers = np.arange(1, points // 2)
    angles = 2.0 * np.pi * wave_numbers / points
    modified = (2.0 * near_weight * np.sin(angles) + 2.0 * far_weight * np.sin(2.0 * angles)) / (
        1.0 + 2.0 * ALPHA_SLOPE * np.cos(angles)
    )
    phases = np.arange(points)[:, None] * wave_numbers[None, :] % points
    circulant = -2.0 / (points * spacing) * (np.sin(2.0 * np.pi * phases / points) @ modified)
    shifts = (np.arange(points)[:, None] - np.arange(points)[None, :]) % points
    return circulant[shifts].T


@functools.lru_cache(maxsize=None)
def wall_tables(kind, points, rows, pad, extra=0):
    assert extra == 0 or kind == "slope"
    lower, middle, upper, weights = system_rows(kind, points)
    system = np.diag(middle) + np.diag(lower[1:], -1) + np.diag(upper[:-1], 1)
    inv = np.linalg.inv(system)
    stencil = np.zeros((points, points + 6))
    for row in range(points):
        for offset in range(-3, 4):
            if weights[3 + offset, row] != 0.0:
                assert abs(offset) <= pad and 0 <= row + offset < points
                stencil[row, row + offset + 3] = weights[3 + offset, row]
    scale = inverse_metric(points) if kind == "slope" else np.ones(points)
    blocks = points // rows
    outputs = rows + 2 * extra
    combine = np.zeros((blocks, outputs + 2, rows + 2 * pad))
    rise_gain = np.zeros((blocks, outputs))
    fall_gain = np.zeros((blocks, outputs))
    rise_step = np.zeros(blocks)
    fall_step = np.zeros(blocks)
    for block in range(blocks):
        lo, hi = block * rows, block * rows + rows
        own = slice(lo, hi)
        window = slice(lo - pad + 3, hi + pad + 3)
        rise_part = np.zeros(rows)
        fall_part = np.zeros(rows)
        rise_ref = hi if block < blocks - 1 else lo
        fall_ref = lo - 1 if block > 0 else hi - 1
        if block > 0:
            rise_step[block] = inv[rise_ref, lo - 1] / inv[lo, lo - 1]
            fall_part = inv[lo - 1, own]
        if block < blocks - 1:
            fall_step[block] = inv[fall_ref, hi] / inv[hi - 1, hi]
            rise_part = inv[hi, own]
        for out, row in enumerate(range(lo - extra, hi + extra)):
            if row < 0 or row >= points:
                continue
            alpha = beta = 0.0
            if block > 0 or row >= hi:
                column = lo - 1 if lo <= row < hi else min(row, rise_ref) - 1
                alpha = inv[row, column] / inv[rise_ref, column]
            if block < blocks - 1:
                column = hi if row < hi else row + 1
                beta = inv[row, column] / inv[fall_ref, column]
            coef = np.zeros(points + 6)
            coef += (inv[row, own] - alpha * rise_part - beta * fall_part) @ stencil[own]
            if row == lo - 2:
                model = inv[row, row - 1] / inv[lo - 1, row - 1] * inv[lo - 1, lo - 1]
                coef += (inv[row, lo - 1] - model) * stencil[lo - 1]
            if row == hi + 1:
                model = inv[row, row + 1] / inv[hi, row + 1] * inv[hi, hi]
                coef += (inv[row, hi] - model) * stencil[hi]
            outside = coef.copy()
            outside[window] = 0.0
            assert not outside.any()
            combine[block, out] = scale[row] * coef[window]
            rise_gain[block, out] = scale[row] * alpha
            fall_gain[block, out] = scale[row] * beta
        rows_stencil = stencil[own, window]
        combine[block, outputs] = rise_part @ rows_stencil
        combine[block, outputs + 1] = fall_part @ rows_stencil
    return combine, rise_gain, fall_gain, rise_step, fall_step


def scan_rounds(blocks):
    rounds = []
    stride = 1
    while stride < blocks:
        radix = min(2, -(-blocks // stride))
        rounds.append((stride, list(range(1, radix))))
        stride *= radix
    longest_first = rounds[::-1]
    return longest_first[0::2] + longest_first[1::2]


def scan_coefs(rise_step, fall_step, shift):
    blocks = rise_step.shape[0]
    rise = np.zeros(blocks)
    fall = np.zeros(blocks)
    for block in range(blocks):
        if block - shift >= 0:
            rise[block] = np.prod(rise_step[block - shift + 1 : block + 1])
        if block + shift <= blocks - 1:
            fall[block] = np.prod(fall_step[block : block + shift])
    return rise, fall


class TableBank:
    def __init__(self):
        self.parts = []
        self.width = 0

    def add(self, table):
        table = np.asarray(table, np.float64)
        handle = (self.width, table.shape[1:])
        self.parts.append(table.reshape(table.shape[0], -1))
        self.width += self.parts[-1].shape[1]
        return handle

    def lookup(self, position):
        whole = jnp.asarray(np.concatenate(self.parts, axis=1), jnp.float32)
        self.row = lax.dynamic_index_in_dim(whole, position, 0, keepdims=False)

    def get(self, handle):
        start, shape = handle
        return self.row[start : start + int(np.prod(shape))].reshape(shape)


def plan_wall(bank, kinds_sizes, points, rows, pad, extras):
    tables = [
        wall_tables(kind, points, rows, pad, extra)
        for (kind, _), extra in zip(kinds_sizes, extras)
    ]
    groups = [
        (
            bank.add(table[0].transpose(0, 2, 1)),
            bank.add(table[1]),
            bank.add(table[2]),
            table[1].shape[1],
        )
        for table in tables
    ]
    blocks = points // rows
    rounds = []
    for stride, multiples in scan_rounds(blocks):
        entries = []
        for multiple in multiples:
            shift = stride * multiple
            coefs = [scan_coefs(table[3], table[4], shift) for table in tables]
            rise = np.concatenate(
                [np.repeat(c[0][:, None], n, 1) for c, (_, n) in zip(coefs, kinds_sizes)], 1
            )
            fall = np.concatenate(
                [np.repeat(c[1][:, None], n, 1) for c, (_, n) in zip(coefs, kinds_sizes)], 1
            )
            entries.append((shift, bank.add(rise), bank.add(fall)))
        rounds.append(entries)
    return groups, rounds


def wall_apply(bank, plan, padded_groups, rows, pad):
    count = lax.axis_size("gy")
    groups, rounds = plan

    def taps(padded, by_tap):
        summed = None
        for tap in range(by_tap.shape[0]):
            term = by_tap[tap][:, None, None] * padded[:, None, tap]
            summed = term if summed is None else summed + term
        return summed

    partials = [
        taps(padded, bank.get(handles[0])[:, handles[3] :])
        for padded, handles in zip(padded_groups, groups)
    ]
    sizes = [padded.shape[0] for padded in padded_groups]
    rise = jnp.concatenate([part[:, 0] for part in partials], axis=0)
    fall = jnp.concatenate([part[:, 1] for part in partials], axis=0)
    for entries in rounds:
        rise_next, fall_next = rise, fall
        for shift, rise_handle, fall_handle in entries:
            up_pairs = [(i, i + shift) for i in range(count - shift)]
            down_pairs = [(i + shift, i) for i in range(count - shift)]
            from_below = lax.ppermute(rise, "gy", up_pairs)
            from_above = lax.ppermute(fall, "gy", down_pairs)
            rise_next = rise_next + bank.get(rise_handle)[:, None, None] * from_below
            fall_next = fall_next + bank.get(fall_handle)[:, None, None] * from_above
        rise, fall = rise_next, fall_next
    results = []
    first = 0
    for padded, handles, size in zip(padded_groups, groups, sizes):
        local = taps(padded, bank.get(handles[0])[:, : handles[3]])
        rise_gain = bank.get(handles[1])
        fall_gain = bank.get(handles[2])
        results.append(
            local
            + rise_gain[None, :, None, None] * rise[first : first + size, None]
            + fall_gain[None, :, None, None] * fall[first : first + size, None]
        )
        first += size
    return results


def halo(block, width):
    count = lax.axis_size("gy")
    up_pairs = [(i, i + 1) for i in range(count - 1)]
    down_pairs = [(i + 1, i) for i in range(count - 1)]
    below = lax.ppermute(block[:, block.shape[1] - width :], "gy", up_pairs)
    above = lax.ppermute(block[:, :width], "gy", down_pairs)
    return jnp.concatenate([below, block, above], axis=1)


def stream_slope(fields, stream_matrix):
    flat_rows = fields.reshape(-1, stream_matrix.shape[0])
    return jnp.dot(
        flat_rows, stream_matrix, precision=HIGHEST, preferred_element_type=jnp.float32
    ).reshape(fields.shape)


def span_slope(fields, own_block, other_block):
    other = lax.ppermute(fields, "pa", [(0, 1), (1, 0)])
    return jnp.einsum("fyzx,zw->fywx", fields, own_block, precision=HIGHEST) + jnp.einsum(
        "fyzx,zw->fywx", other, other_block, precision=HIGHEST
    )


def flux_along(direction, momentum, energy, speed, push, gradients):
    divergence = gradients[0][0] + gradients[1][1] + gradients[2][2]
    conduct = VISCOSITY * GAMMA_GAS / ((GAMMA_GAS - 1.0) * PRANDTL)
    rows_out = [momentum[direction]]
    energy_flux = (energy + push) * speed[direction]
    for component in range(3):
        stress = VISCOSITY * (gradients[direction][component] + gradients[component][direction])
        if component == direction:
            stress = stress - 2.0 / 3.0 * VISCOSITY * divergence
            rows_out.append(momentum[component] * speed[direction] + push - stress)
        else:
            rows_out.append(momentum[component] * speed[direction] - stress)
        energy_flux = energy_flux - speed[component] * stress
    energy_flux = energy_flux - conduct * gradients[direction][3]
    rows_out.append(energy_flux)
    return jnp.stack(rows_out)


def per_device(mass_per_volume, mass_flux_vector, total_heat_content):
    rows, span_own, stream_cells = mass_per_volume.shape
    count = lax.axis_size("gy")
    points = rows * count
    position = lax.axis_index("gy")
    span_total = span_own * lax.axis_size("pa")
    stream_matrix = jnp.asarray(periodic_matrix(stream_cells, STREAM_STEP), jnp.float32)
    span_full = periodic_matrix(span_total, SPAN_STEP)
    own_block = jnp.asarray(span_full[:span_own, :span_own], jnp.float32)
    other_block = jnp.asarray(span_full[span_own : 2 * span_own, :span_own], jnp.float32)

    bank = TableBank()
    first_plan = plan_wall(bank, [("slope", 4), ("smooth", 5)], points, rows, 3, (2, 0))
    second_plan = plan_wall(bank, [("slope", 5)], points, rows, 2, (0,))
    bank.lookup(position)

    state = jnp.concatenate(
        [mass_per_volume[None], mass_flux_vector, total_heat_content[None]], axis=0
    )
    padded = halo(state, 3)
    global_rows = position * rows - 3 + jnp.arange(rows + 6)
    inside = ((global_rows >= 0) & (global_rows < points))[:, None, None]
    density = jnp.where(inside, padded[0], 1.0)
    speed_pad = padded[1:4] / density[None]
    kinetic = 0.5 * jnp.sum(speed_pad * padded[1:4], axis=0)
    push_pad = (GAMMA_GAS - 1.0) * (padded[4] - kinetic)
    warmth_pad = push_pad / density
    basic_pad = jnp.concatenate([speed_pad, warmth_pad[None]], axis=0)

    wall_grad, smoothed = wall_apply(bank, first_plan, [basic_pad, padded], rows, 3)

    basic = basic_pad[:, 1 : rows + 5]
    speed = basic[:3]
    push = push_pad[1 : rows + 5]
    momentum = padded[1:4, 1 : rows + 5]
    energy = padded[4, 1 : rows + 5]
    grad_stream = stream_slope(basic, stream_matrix)
    grad_span = span_slope(basic, own_block, other_block)
    gradients = [grad_stream, wall_grad, grad_span]
    flux_wall = flux_along(1, momentum, energy, speed, push, gradients)
    (wall_term,) = wall_apply(bank, second_plan, [flux_wall], rows, 2)
    own = slice(2, 2 + rows)
    gradients = [[part[own] for part in grad] for grad in gradients]
    speed, push = speed[:, own], push[own]
    momentum, energy = mass_flux_vector, total_heat_content
    stream_term = stream_slope(
        flux_along(0, momentum, energy, speed, push, gradients), stream_matrix
    )
    span_term = span_slope(
        flux_along(2, momentum, energy, speed, push, gradients), own_block, other_block
    )
    time_rate = -(stream_term + wall_term + span_term)
    own_rows = position * rows + jnp.arange(rows)
    at_wall = ((own_rows == 0) | (own_rows == points - 1))[None, :, None, None]
    held = jnp.where(at_wall, 0.0, time_rate[1:4])
    time_rate = jnp.concatenate([time_rate[:1], held, time_rate[4:]], axis=0)
    return (time_rate, smoothed)


def solution(mesh):
    placed = (P("gy", "pa", None), P(None, "gy", "pa", None), P("gy", "pa", None))
    return jax.shard_map(
        per_device,
        mesh=mesh,
        in_specs=placed,
        out_specs=(P(None, "gy", "pa", None), P(None, "gy", "pa", None)),
        check_vma=False,
    )
```

```python
import functools

import jax
import jax.numpy as jnp
import numpy as np
from jax import lax
from jax.sharding import PartitionSpec as P

GAMMA_GAS = 1.4
PRANDTL = 0.72
VISCOSITY = 0.25
ALPHA_FILTER = 0.499
ALPHA_SLOPE = 0.498
STRETCH = 1.2
STREAM_STEP = 1.0
SPAN_STEP = 0.5
HIGHEST = lax.Precision.HIGHEST


def slope_weights():
    near_weight = (2.0 + ALPHA_SLOPE) / 3.0
    far_weight = (4.0 * ALPHA_SLOPE - 1.0) / 12.0
    return (near_weight, far_weight)


def system_rows(system_kind, points):
    lower = np.zeros(points)
    middle = np.ones(points)
    upper = np.zeros(points)
    weights = np.zeros((7, points))
    if system_kind == "slope":
        near_weight, far_weight = slope_weights()
        lower[:] = ALPHA_SLOPE
        upper[:] = ALPHA_SLOPE
        weights[1] = -far_weight
        weights[2] = -near_weight
        weights[4] = near_weight
        weights[5] = far_weight
        for edge_row in (1, points - 2):
            lower[edge_row] = 0.25
            upper[edge_row] = 0.25
            weights[:, edge_row] = 0.0
            weights[2, edge_row] = -0.75
            weights[4, edge_row] = 0.75
        lower[0] = 0.0
        upper[0] = 2.0
        weights[:, 0] = 0.0
        weights[3, 0] = -2.5
        weights[4, 0] = 2.0
        weights[5, 0] = 0.5
        lower[points - 1] = 2.0
        upper[points - 1] = 0.0
        weights[:, points - 1] = 0.0
        weights[3, points - 1] = 2.5
        weights[2, points - 1] = -2.0
        weights[1, points - 1] = -0.5
    else:
        strength = ALPHA_FILTER
        lower[:] = strength
        upper[:] = strength
        weights[3] = 11.0 / 16.0 + 5.0 * strength / 8.0
        weights[2] = 15.0 / 64.0 + 17.0 * strength / 32.0
        weights[4] = weights[2]
        weights[1] = -3.0 / 32.0 + 3.0 * strength / 16.0
        weights[5] = weights[1]
        weights[0] = 1.0 / 64.0 - strength / 32.0
        weights[6] = weights[0]
        for edge_row in (2, points - 3):
            weights[:, edge_row] = 0.0
            weights[3, edge_row] = 5.0 / 8.0 + 3.0 * strength / 4.0
            weights[2, edge_row] = 0.25 + strength / 2.0
            weights[4, edge_row] = 0.25 + strength / 2.0
            weights[1, edge_row] = -1.0 / 16.0 + strength / 8.0
            weights[5, edge_row] = -1.0 / 16.0 + strength / 8.0
        for edge_row in (1, points - 2):
            weights[:, edge_row] = 0.0
            weights[3, edge_row] = 0.5 + strength
            weights[2, edge_row] = 0.25 + strength / 2.0
            weights[4, edge_row] = 0.25 + strength / 2.0
        for edge_row in (0, points - 1):
            lower[edge_row] = 0.0
            upper[edge_row] = 0.0
            weights[:, edge_row] = 0.0
            weights[3, edge_row] = 1.0
    return (lower, middle, upper, weights)


def inverse_metric(points):
    places = 2.0 * np.arange(points) / (points - 1) - 1.0
    growth = np.exp(STRETCH * places)
    cosh_values = 0.5 * (growth + 1.0 / growth)
    edge_growth = np.exp(STRETCH)
    tanh_value = (edge_growth - 1.0 / edge_growth) / (edge_growth + 1.0 / edge_growth)
    return tanh_value * cosh_values**2 / (0.64 * STRETCH)


def periodic_matrix(points, spacing):
    near_weight, far_weight = slope_weights()
    wave_numbers = np.arange(1, points // 2)
    angles = 2.0 * np.pi * wave_numbers / points
    modified = (2.0 * near_weight * np.sin(angles) + 2.0 * far_weight * np.sin(2.0 * angles)) / (
        1.0 + 2.0 * ALPHA_SLOPE * np.cos(angles)
    )
    phases = np.arange(points)[:, None] * wave_numbers[None, :] % points
    circulant = -2.0 / (points * spacing) * (np.sin(2.0 * np.pi * phases / points) @ modified)
    shifts = (np.arange(points)[:, None] - np.arange(points)[None, :]) % points
    return circulant[shifts].T


@functools.lru_cache(maxsize=None)
def wall_tables(kind, points, rows, pad, extra=0):
    assert extra == 0 or kind == "slope"
    lower, middle, upper, weights = system_rows(kind, points)
    system = np.diag(middle) + np.diag(lower[1:], -1) + np.diag(upper[:-1], 1)
    inv = np.linalg.inv(system)
    stencil = np.zeros((points, points + 6))
    for row in range(points):
        for offset in range(-3, 4):
            if weights[3 + offset, row] != 0.0:
                assert abs(offset) <= pad and 0 <= row + offset < points
                stencil[row, row + offset + 3] = weights[3 + offset, row]
    scale = inverse_metric(points) if kind == "slope" else np.ones(points)
    blocks = points // rows
    outputs = rows + 2 * extra
    combine = np.zeros((blocks, outputs + 2, rows + 2 * pad))
    rise_gain = np.zeros((blocks, outputs))
    fall_gain = np.zeros((blocks, outputs))
    rise_step = np.zeros(blocks)
    fall_step = np.zeros(blocks)
    for block in range(blocks):
        lo, hi = block * rows, block * rows + rows
        own = slice(lo, hi)
        window = slice(lo - pad + 3, hi + pad + 3)
        rise_part = np.zeros(rows)
        fall_part = np.zeros(rows)
        rise_ref = hi if block < blocks - 1 else lo
        fall_ref = lo - 1 if block > 0 else hi - 1
        if block > 0:
            rise_step[block] = inv[rise_ref, lo - 1] / inv[lo, lo - 1]
            fall_part = inv[lo - 1, own]
        if block < blocks - 1:
            fall_step[block] = inv[fall_ref, hi] / inv[hi - 1, hi]
            rise_part = inv[hi, own]
        for out, row in enumerate(range(lo - extra, hi + extra)):
            if row < 0 or row >= points:
                continue
            alpha = beta = 0.0
            if block > 0 or row >= hi:
                column = lo - 1 if lo <= row < hi else min(row, rise_ref) - 1
                alpha = inv[row, column] / inv[rise_ref, column]
            if block < blocks - 1:
                column = hi if row < hi else row + 1
                beta = inv[row, column] / inv[fall_ref, column]
            coef = np.zeros(points + 6)
            coef += (inv[row, own] - alpha * rise_part - beta * fall_part) @ stencil[own]
            if row == lo - 2:
                model = inv[row, row - 1] / inv[lo - 1, row - 1] * inv[lo - 1, lo - 1]
                coef += (inv[row, lo - 1] - model) * stencil[lo - 1]
            if row == hi + 1:
                model = inv[row, row + 1] / inv[hi, row + 1] * inv[hi, hi]
                coef += (inv[row, hi] - model) * stencil[hi]
            outside = coef.copy()
            outside[window] = 0.0
            assert not outside.any()
            combine[block, out] = scale[row] * coef[window]
            rise_gain[block, out] = scale[row] * alpha
            fall_gain[block, out] = scale[row] * beta
        rows_stencil = stencil[own, window]
        combine[block, outputs] = rise_part @ rows_stencil
        combine[block, outputs + 1] = fall_part @ rows_stencil
    return combine, rise_gain, fall_gain, rise_step, fall_step


def scan_rounds(blocks):
    rounds = []
    stride = 1
    while stride < blocks:
        radix = min(2, -(-blocks // stride))
        rounds.append((stride, list(range(1, radix))))
        stride *= radix
    longest_first = rounds[::-1]
    half = (len(longest_first) + 1) // 2
    order = []
    for index in range(half):
        order += longest_first[index : index + 1] + longest_first[half + index : half + index + 1]
    return order


def scan_coefs(rise_step, fall_step, shift):
    blocks = rise_step.shape[0]
    rise = np.zeros(blocks)
    fall = np.zeros(blocks)
    for block in range(blocks):
        if block - shift >= 0:
            rise[block] = np.prod(rise_step[block - shift + 1 : block + 1])
        if block + shift <= blocks - 1:
            fall[block] = np.prod(fall_step[block : block + shift])
    return rise, fall


class TableBank:
    def __init__(self):
        self.parts = []
        self.width = 0

    def add(self, table):
        table = np.asarray(table, np.float64)
        handle = (self.width, table.shape[1:])
        self.parts.append(table.reshape(table.shape[0], -1))
        self.width += self.parts[-1].shape[1]
        return handle

    def lookup(self, position):
        whole = jnp.asarray(np.concatenate(self.parts, axis=1), jnp.float32)
        self.row = lax.dynamic_index_in_dim(whole, position, 0, keepdims=False)

    def get(self, handle):
        start, shape = handle
        return self.row[start : start + int(np.prod(shape))].reshape(shape)


def plan_wall(bank, kinds_sizes, points, rows, pad, extras):
    tables = [
        wall_tables(kind, points, rows, pad, extra)
        for (kind, _), extra in zip(kinds_sizes, extras)
    ]
    groups = [
        (
            bank.add(table[0].transpose(0, 2, 1)),
            bank.add(table[1]),
            bank.add(table[2]),
            table[1].shape[1],
        )
        for table in tables
    ]
    blocks = points // rows
    rounds = []
    for stride, multiples in scan_rounds(blocks):
        entries = []
        for multiple in multiples:
            shift = stride * multiple
            coefs = [scan_coefs(table[3], table[4], shift) for table in tables]
            rise = np.concatenate(
                [np.repeat(c[0][:, None], n, 1) for c, (_, n) in zip(coefs, kinds_sizes)], 1
            )
            fall = np.concatenate(
                [np.repeat(c[1][:, None], n, 1) for c, (_, n) in zip(coefs, kinds_sizes)], 1
            )
            entries.append((shift, bank.add(rise), bank.add(fall)))
        rounds.append(entries)
    return groups, rounds


def wall_apply(bank, plan, padded_groups, rows, pad):
    count = lax.axis_size("gy")
    groups, rounds = plan

    def taps(padded, by_tap):
        summed = None
        for tap in range(by_tap.shape[0]):
            term = by_tap[tap][:, None, None] * padded[:, None, tap]
            summed = term if summed is None else summed + term
        return summed

    partials = [
        taps(padded, bank.get(handles[0])[:, handles[3] :])
        for padded, handles in zip(padded_groups, groups)
    ]
    sizes = [padded.shape[0] for padded in padded_groups]
    rise = jnp.concatenate([part[:, 0] for part in partials], axis=0)
    fall = jnp.concatenate([part[:, 1] for part in partials], axis=0)
    for entries in rounds:
        rise_next, fall_next = rise, fall
        for shift, rise_handle, fall_handle in entries:
            up_pairs = [(i, i + shift) for i in range(count - shift)]
            down_pairs = [(i + shift, i) for i in range(count - shift)]
            from_below = lax.ppermute(rise, "gy", up_pairs)
            from_above = lax.ppermute(fall, "gy", down_pairs)
            rise_next = rise_next + bank.get(rise_handle)[:, None, None] * from_below
            fall_next = fall_next + bank.get(fall_handle)[:, None, None] * from_above
        rise, fall = rise_next, fall_next
    results = []
    first = 0
    for padded, handles, size in zip(padded_groups, groups, sizes):
        local = taps(padded, bank.get(handles[0])[:, : handles[3]])
        rise_gain = bank.get(handles[1])
        fall_gain = bank.get(handles[2])
        results.append(
            local
            + rise_gain[None, :, None, None] * rise[first : first + size, None]
            + fall_gain[None, :, None, None] * fall[first : first + size, None]
        )
        first += size
    return results


def halo(block, width):
    count = lax.axis_size("gy")
    up_pairs = [(i, i + 1) for i in range(count - 1)]
    down_pairs = [(i + 1, i) for i in range(count - 1)]
    below = lax.ppermute(block[:, block.shape[1] - width :], "gy", up_pairs)
    above = lax.ppermute(block[:, :width], "gy", down_pairs)
    return jnp.concatenate([below, block, above], axis=1)


def stream_slope(fields, stream_matrix):
    flat_rows = fields.reshape(-1, stream_matrix.shape[0])
    return jnp.dot(
        flat_rows, stream_matrix, precision=HIGHEST, preferred_element_type=jnp.float32
    ).reshape(fields.shape)


def span_slope(fields, own_block, other_block):
    other = lax.ppermute(fields, "pa", [(0, 1), (1, 0)])
    return jnp.einsum("fyzx,zw->fywx", fields, own_block, precision=HIGHEST) + jnp.einsum(
        "fyzx,zw->fywx", other, other_block, precision=HIGHEST
    )


def flux_along(direction, momentum, energy, speed, push, gradients):
    divergence = gradients[0][0] + gradients[1][1] + gradients[2][2]
    conduct = VISCOSITY * GAMMA_GAS / ((GAMMA_GAS - 1.0) * PRANDTL)
    rows_out = [momentum[direction]]
    energy_flux = (energy + push) * speed[direction]
    for component in range(3):
        stress = VISCOSITY * (gradients[direction][component] + gradients[component][direction])
        if component == direction:
            stress = stress - 2.0 / 3.0 * VISCOSITY * divergence
            rows_out.append(momentum[component] * speed[direction] + push - stress)
        else:
            rows_out.append(momentum[component] * speed[direction] - stress)
        energy_flux = energy_flux - speed[component] * stress
    energy_flux = energy_flux - conduct * gradients[direction][3]
    rows_out.append(energy_flux)
    return jnp.stack(rows_out)


def per_device(mass_per_volume, mass_flux_vector, total_heat_content):
    rows, span_own, stream_cells = mass_per_volume.shape
    count = lax.axis_size("gy")
    points = rows * count
    position = lax.axis_index("gy")
    span_total = span_own * lax.axis_size("pa")
    stream_matrix = jnp.asarray(periodic_matrix(stream_cells, STREAM_STEP), jnp.float32)
    span_full = periodic_matrix(span_total, SPAN_STEP)
    own_block = jnp.asarray(span_full[:span_own, :span_own], jnp.float32)
    other_block = jnp.asarray(span_full[span_own : 2 * span_own, :span_own], jnp.float32)

    bank = TableBank()
    first_plan = plan_wall(bank, [("slope", 4), ("smooth", 5)], points, rows, 3, (2, 0))
    second_plan = plan_wall(bank, [("slope", 5)], points, rows, 2, (0,))
    bank.lookup(position)

    state = jnp.concatenate(
        [mass_per_volume[None], mass_flux_vector, total_heat_content[None]], axis=0
    )
    padded = halo(state, 3)
    global_rows = position * rows - 3 + jnp.arange(rows + 6)
    inside = ((global_rows >= 0) & (global_rows < points))[:, None, None]
    density = jnp.where(inside, padded[0], 1.0)
    speed_pad = padded[1:4] / density[None]
    kinetic = 0.5 * jnp.sum(speed_pad * padded[1:4], axis=0)
    push_pad = (GAMMA_GAS - 1.0) * (padded[4] - kinetic)
    warmth_pad = push_pad / density
    basic_pad = jnp.concatenate([speed_pad, warmth_pad[None]], axis=0)

    wall_grad, smoothed = wall_apply(bank, first_plan, [basic_pad, padded], rows, 3)

    basic = basic_pad[:, 1 : rows + 5]
    speed = basic[:3]
    push = push_pad[1 : rows + 5]
    momentum = padded[1:4, 1 : rows + 5]
    energy = padded[4, 1 : rows + 5]
    grad_stream = stream_slope(basic, stream_matrix)
    grad_span = span_slope(basic, own_block, other_block)
    gradients = [grad_stream, wall_grad, grad_span]
    flux_wall = flux_along(1, momentum, energy, speed, push, gradients)
    (wall_term,) = wall_apply(bank, second_plan, [flux_wall], rows, 2)
    own = slice(2, 2 + rows)
    gradients = [[part[own] for part in grad] for grad in gradients]
    speed, push = speed[:, own], push[own]
    momentum, energy = mass_flux_vector, total_heat_content
    stream_term = stream_slope(
        flux_along(0, momentum, energy, speed, push, gradients), stream_matrix
    )
    span_term = span_slope(
        flux_along(2, momentum, energy, speed, push, gradients), own_block, other_block
    )
    time_rate = -(stream_term + wall_term + span_term)
    own_rows = position * rows + jnp.arange(rows)
    at_wall = ((own_rows == 0) | (own_rows == points - 1))[None, :, None, None]
    held = jnp.where(at_wall, 0.0, time_rate[1:4])
    time_rate = jnp.concatenate([time_rate[:1], held, time_rate[4:]], axis=0)
    return (time_rate, smoothed)


def solution(mesh):
    placed = (P("gy", "pa", None), P(None, "gy", "pa", None), P("gy", "pa", None))
    return jax.shard_map(
        per_device,
        mesh=mesh,
        in_specs=placed,
        out_specs=(P(None, "gy", "pa", None), P(None, "gy", "pa", None)),
        check_vma=False,
    )
```
